128 devices in a mesh: tm: 4 (over y), tile: 32 (over z, x, core).
Axes of the slice: x: 4, y: 4, z: 4, core: 2. Of those that a mesh axis runs over, the one named last changes fastest.
Arguments:
- traces: bfloat16 [8, 20480, 1536], P('tm', 'tile'), may hold values from -6 to 6
- weights: bfloat16 [1536, 32, 640], P('tile', 'tm'), may hold values from -128 to 128
- pair_tile: int32 [1536], P('tile'), may hold values from 0 to 127, as said below
- pair_offset: int32 [1536], P('tile'), may hold values from 0 to 1408, as said below
- tile_order: int32 [128], replicated, may hold values from 0 to 127, as said below
Outputs:
- phase_stack: float32 [8, 128, 32, 128], P('tm', 'tile')
The draws below stay inside these ranges and needn't reach their ends.
Inputs may be any that keep to these rules, and one draw needn't show every extreme that they name: `pair_tile`: pair p uses channel block p // 48. The 48 pairs of one block name distinct tiles. Call position // 4 of a tile in tile_order its owner: the pairs of one block name the tiles of one owner either exactly 2 times or never. Every tile is named by some pair. A permutation of the tiles; output row r holds tile tile_order[r]. `pair_offset`: A multiple of 128.
All inputs are finite; a program needn't handle non-finite values.
Results may differ from the reference program's by a relative error of at most 0.0021.
Values may be sent and summed in bfloat16 or wider, within the bound.
No kernel may reach another device: no remote copies, remote signals or barrier semaphores. Data moves between devices by JAX's collectives and lax.ppermute only.
A program may use at most 128 MiB of HBM per device.

```python
import jax
import jax.numpy as jnp
from jax import lax

NS = 1536
CH_DEV = 640
GT = 32
LO = 128
SLOT = 2
OWN_CAP = 4
PAIR_DEV = 48
WINDOWS = 8
CHANNELS = 20480
TILES = 128
PAIRS = 1536
N_TILE = 32


def owner_plan(key):
    owner_count = TILES // OWN_CAP
    group_count = PAIR_DEV // SLOT
    tile_perm = jax.random.permutation(jax.random.fold_in(key, 11), TILES).astype(jnp.int32)
    first_owner = jax.random.permutation(jax.random.fold_in(key, 12), owner_count).astype(jnp.int32)
    second_owner = jnp.roll(first_owner, -1)
    busy_owner = jax.random.randint(jax.random.fold_in(key, 13), (), 0, owner_count)
    owner_iota = jnp.arange(owner_count, dtype=jnp.int32)[None, :]
    noise_draw = jax.random.randint(jax.random.fold_in(key, 14), (owner_count, owner_count), 0, 65536)
    scores = noise_draw * owner_count + owner_iota
    scores = scores + jnp.where(owner_iota == first_owner[:, None], 3 * 2 ** 24, 0)
    scores = scores + jnp.where(owner_iota == second_owner[:, None], 2 * 2 ** 24, 0)
    scores = scores + jnp.where(owner_iota == busy_owner, 2 ** 24, 0)
    chosen = lax.top_k(scores, group_count)[1].astype(jnp.int32)
    slot_noise = jax.random.randint(jax.random.fold_in(key, 15), (owner_count, group_count, OWN_CAP), 0, 65536)
    slot_noise = slot_noise * OWN_CAP + jnp.arange(OWN_CAP, dtype=jnp.int32)
    sub_slot = lax.top_k(slot_noise, SLOT)[1].astype(jnp.int32)
    group_iota = jnp.arange(group_count, dtype=jnp.int32)[None, :, None]
    slot_iota = jnp.arange(SLOT, dtype=jnp.int32)[None, None, :]
    sub_slot = jnp.where(group_iota == 0, slot_iota, jnp.where(group_iota == 1, SLOT + slot_iota, sub_slot))
    out_rows = (chosen[:, :, None] * OWN_CAP + sub_slot).reshape(owner_count, PAIR_DEV)
    shuffle_key = jax.random.randint(jax.random.fold_in(key, 16), (owner_count, PAIR_DEV), 0, 65536)
    shuffle_key = shuffle_key * PAIR_DEV + jnp.arange(PAIR_DEV, dtype=jnp.int32)[None, :]
    shuffle_order = jnp.argsort(shuffle_key, axis=1, stable=True)
    out_rows = jnp.take_along_axis(out_rows, shuffle_order, axis=1)
    pair_tiles = tile_perm[out_rows.reshape(PAIRS)]
    return (tile_perm, pair_tiles.astype(jnp.int32))


def draw_pair_tile(key, part):
    return owner_plan(key)[1]


def draw_tile_order(key, part):
    return owner_plan(key)[0]


def draw_pair_offset(key, part):
    block_total = NS // LO
    chosen = jax.random.randint(jax.random.fold_in(key, 31), (PAIRS,), 0, block_total).astype(jnp.int32)
    pair_iota = jnp.arange(PAIRS, dtype=jnp.int32)
    chosen = jnp.where(pair_iota == 0, block_total - 1, jnp.where(pair_iota == 1, 0, chosen))
    return (chosen * LO).astype(jnp.int32)


def draw_weights(key, part):
    shape = (PAIRS, GT, CH_DEV)
    block_count = PAIRS // PAIR_DEV
    block_index = (jnp.arange(PAIRS, dtype=jnp.int32) // PAIR_DEV).astype(jnp.float32)
    rise_factor = jnp.sqrt(1.0 + 2.0 * block_index / max(block_count - 1, 1))
    base_draw = jax.random.truncated_normal(jax.random.fold_in(key, 21), -4.0, 4.0, shape, jnp.float32)
    row_scale = jnp.exp(jax.random.uniform(jax.random.fold_in(key, 23), (PAIRS, GT, 1), jnp.float32) * jnp.log(10.0))
    col_scale = jnp.exp(jax.random.uniform(jax.random.fold_in(key, 24), (PAIRS, 1, CH_DEV), jnp.float32) * jnp.log(10.0))
    values = base_draw * row_scale * col_scale * rise_factor[:, None, None] / jnp.sqrt(float(CH_DEV))
    values = jnp.clip(values, -128.0, 128.0)
    return values.astype(jnp.bfloat16)


def block_scale(key, dims, split, smallest, top_value):
    gain, own = 1.0, jax.random.fold_in(key, 6)
    for axis_at, blocks in split:
        heights = jnp.exp(jax.random.uniform(jax.random.fold_in(own, axis_at), (blocks,), jnp.float32, smallest / len(split), top_value / len(split)))
        gain = gain * jnp.repeat(heights, dims[axis_at] // blocks).reshape([-1 if axis == axis_at else 1 for axis in range(len(dims))])
    return gain


def noise(stream_key, extent, width, reach, split=(), held_as=jnp.bfloat16):
    array = jax.random.normal(stream_key, extent, jnp.float32) * width
    if len(split) > 0:
        array = block_scale(stream_key, extent, split, -0.22, 0.18) * array
    return jnp.clip(array, min=-reach, max=reach).astype(held_as)


def setup_inputs(seed: int = 0) -> dict:
    splits = jax.random.split(jax.random.key(seed), 6)
    traces = noise(splits[0], (WINDOWS, CHANNELS, NS), 1.0, 6.0, ((0, 4), (1, 32)))
    weights = draw_weights(jax.random.fold_in(splits[5], 71), 0)
    pair_tile = draw_pair_tile(jax.random.fold_in(splits[5], 71), 0)
    pair_offset = draw_pair_offset(jax.random.fold_in(splits[5], 71), 0)
    tile_order = draw_tile_order(jax.random.fold_in(splits[5], 71), 0)
    return {"traces": traces, "weights": weights, "pair_tile": pair_tile, "pair_offset": pair_offset, "tile_order": tile_order}


AMP_FLOOR = 0.5
ENERGY_EPS = 1e-06

def hilbert_build(length):
    sample_index = jnp.arange(length, dtype=jnp.int32)
    lag_index = (sample_index[None, :] - sample_index[:, None]) % length
    odd_lag = lag_index % 2 == 1
    phase_angle = jnp.pi * lag_index.astype(jnp.float32) / length
    safe_sine = jnp.where(odd_lag, jnp.sin(phase_angle), 1.0)
    kernel = jnp.where(odd_lag, 2.0 / length * jnp.cos(phase_angle) / safe_sine, 0.0)
    return kernel.astype(jnp.bfloat16)

def analytic(block_traces, hilbert):
    length = block_traces.shape[-1]
    quadrature = jnp.dot(block_traces.reshape(-1, length), hilbert, preferred_element_type=jnp.float32)
    quadrature = quadrature.reshape(block_traces.shape)
    real_part = block_traces.astype(jnp.float32)
    amplitude = jnp.maximum(jnp.sqrt(real_part * real_part + quadrature * quadrature), AMP_FLOOR)
    cosine = (real_part / amplitude).astype(jnp.bfloat16)
    sine_part = (quadrature / amplitude).astype(jnp.bfloat16)
    return jnp.stack([block_traces, cosine, sine_part], axis=2)

def reference(traces, weights, pair_tile, pair_offset, tile_order):
    hilbert = hilbert_build(NS)
    zero_stacks = jnp.zeros((TILES, WINDOWS, GT, 3, LO), jnp.float32)
    zero_energy = jnp.zeros((TILES, GT), jnp.float32)

    def per_block(carry, block_index):
        stacks, energies = carry
        start_channel = (block_index * CH_DEV).astype(jnp.int32)
        start_pair = (block_index * PAIR_DEV).astype(jnp.int32)
        block_traces = lax.dynamic_slice_in_dim(traces, start_channel, CH_DEV, axis=1)
        features = analytic(block_traces, hilbert)
        shifts = lax.dynamic_slice_in_dim(pair_offset, start_pair, PAIR_DEV)
        block_weights = lax.dynamic_slice_in_dim(weights, start_pair, PAIR_DEV, axis=0)
        block_tiles = lax.dynamic_slice_in_dim(pair_tile, start_pair, PAIR_DEV)
        shifted = jax.vmap(lambda shift: lax.dynamic_slice_in_dim(features, shift.astype(jnp.int32), LO, axis=3))(shifts)
        partial_value = jnp.einsum('pgc,pwckt->pwgkt', block_weights.astype(jnp.float32), shifted.astype(jnp.float32))
        weight_f = block_weights.astype(jnp.float32)
        pair_energy = lax.optimization_barrier(jnp.sum(weight_f * weight_f, axis=2))
        stacks = stacks + jax.ops.segment_sum(partial_value, block_tiles, num_segments=TILES)
        energies = energies + jax.ops.segment_sum(pair_energy, block_tiles, num_segments=TILES)
        return ((stacks, energies), None)
    (stacks, energies), _ = lax.scan(per_block, (zero_stacks, zero_energy), jnp.arange(N_TILE, dtype=jnp.int32))
    row_stacks = stacks[tile_order]
    energy_rows = energies[tile_order] + ENERGY_EPS
    linear = row_stacks[:, :, :, 0, :]
    cosine_sum = row_stacks[:, :, :, 1, :]
    sine_sum = row_stacks[:, :, :, 2, :]
    energy_b = energy_rows[:, None, :, None]
    phase_stack = linear * (cosine_sum * cosine_sum + sine_sum * sine_sum) / (energy_b * jnp.sqrt(energy_b))
    return jnp.transpose(phase_stack, (1, 0, 2, 3))
```

```python
import jax
import jax.numpy as jnp
from jax import lax
from jax.experimental import pallas as pl
from jax.experimental.pallas import tpu as pltpu
from jax.sharding import PartitionSpec as P

LO = 128
SLOT = 2

AMP_FLOOR = 0.5
ENERGY_EPS = 1e-06


def hilbert_build(length):
    row = jnp.arange(LO, dtype=jnp.int32)[:, None]
    col = jnp.arange(length, dtype=jnp.int32)[None, :]
    lag_index = (col - row) % length
    odd_lag = lag_index % 2 == 1
    phase_angle = jnp.pi * lag_index.astype(jnp.float32) / length
    safe_sine = jnp.where(odd_lag, jnp.sin(phase_angle), 1.0)
    kernel = jnp.where(odd_lag, 2.0 / length * jnp.cos(phase_angle) / safe_sine, 0.0)
    first = kernel.astype(jnp.bfloat16)
    return jnp.concatenate(
        [jnp.roll(first, LO * i, axis=1) for i in range(length // LO)], axis=0
    )


def analytic(block_traces, hilbert):
    length = block_traces.shape[-1]
    quadrature = jnp.dot(
        block_traces.reshape(-1, length), hilbert, preferred_element_type=jnp.float32
    )
    quadrature = quadrature.reshape(block_traces.shape)
    real_part = block_traces.astype(jnp.float32)
    amplitude = jnp.maximum(jnp.sqrt(real_part * real_part + quadrature * quadrature), AMP_FLOOR)
    cosine = (real_part / amplitude).astype(jnp.bfloat16)
    sine_part = (quadrature / amplitude).astype(jnp.bfloat16)
    return jnp.stack([block_traces, cosine, sine_part], axis=1)


def pair_kernel(order_ref, blk_ref, dst_ref, valid_ref, w_ref, f_ref, o_ref):
    i = pl.program_id(0)
    planes = f_ref.shape[0]

    @pl.when(valid_ref[i] == 1)
    def _():
        w = w_ref[0]
        for j in range(planes):
            o_ref[0, :, j * LO:(j + 1) * LO] = jnp.dot(
                w, f_ref[j], preferred_element_type=jnp.float32
            )

    @pl.when(valid_ref[i] == 0)
    def _():
        o_ref[...] = jnp.zeros(o_ref.shape, o_ref.dtype)


def pair_stacks(order, blk, dst, valid, full_weights, planes_feat, positions):
    pair_count, grid_count, channel_count = full_weights.shape
    planes = planes_feat.shape[0]
    steps = order.shape[0]
    grid_spec = pltpu.PrefetchScalarGridSpec(
        num_scalar_prefetch=4,
        grid=(steps,),
        in_specs=[
            pl.BlockSpec((1, grid_count, channel_count), lambda i, o, b, d, v: (o[i], 0, 0)),
            pl.BlockSpec((planes, channel_count, LO), lambda i, o, b, d, v: (0, 0, b[i])),
        ],
        out_specs=pl.BlockSpec((1, grid_count, planes * LO), lambda i, o, b, d, v: (d[i], 0, 0)),
    )
    return pl.pallas_call(
        pair_kernel,
        grid_spec=grid_spec,
        out_shape=jax.ShapeDtypeStruct((positions, grid_count, planes * LO), jnp.float32),
    )(order, blk, dst, valid, full_weights, planes_feat)


def owner_of(pair_tile, tile_order, owned_count):
    tile_count = tile_order.shape[0]
    match = tile_order[None, :] == pair_tile[:, None]
    pos = jnp.sum(jnp.where(match, jnp.arange(tile_count, dtype=jnp.int32)[None, :], 0), axis=1)
    return pos // owned_count, pos % owned_count


def slot_of(owner):
    n = owner.shape[-1]
    idx = jnp.arange(n, dtype=jnp.int32)
    earlier = idx[None, :] < idx[:, None]
    same = owner[..., :, None] == owner[..., None, :]
    return jnp.sum((same & earlier).astype(jnp.int32), axis=-1)


def local(traces, weights, pair_tile, pair_offset, tile_order):
    window_count = traces.shape[0]
    sample_count = traces.shape[2]
    devices = lax.axis_size("tile")
    me = lax.axis_index("tile")
    tile_count = tile_order.shape[0]
    owned_count = tile_count // devices
    positions = devices * SLOT

    features = analytic(traces, hilbert_build(sample_count))
    planes_feat = features.reshape(window_count * 3, traces.shape[1], sample_count)

    full_weights = lax.all_gather(weights, "tm", axis=1, tiled=True)
    pair_count, grid_count, _ = full_weights.shape
    wf = full_weights.astype(jnp.float32)
    energy = jnp.sum(wf * wf, axis=2)

    pidx = jnp.arange(pair_count, dtype=jnp.int32)
    pair_block = pair_offset // LO
    key = pair_block * pair_count + pidx
    rank = jnp.sum((key[None, :] < key[:, None]).astype(jnp.int32), axis=1)
    order = jnp.sum(jnp.where(rank[None, :] == pidx[:, None], pidx[None, :], 0), axis=1)
    owner, _ = owner_of(pair_tile, tile_order, owned_count)
    dst = owner * SLOT + slot_of(owner)
    pos_idx = jnp.arange(positions, dtype=jnp.int32)
    unused = jnp.sum((dst[None, :] == pos_idx[:, None]).astype(jnp.int32), axis=1) == 0
    empty_rank = jnp.cumsum(unused.astype(jnp.int32)) - 1
    empty_count = positions - pair_count
    eidx = jnp.arange(empty_count, dtype=jnp.int32)
    empties = jnp.sum(
        jnp.where(unused[None, :] & (empty_rank[None, :] == eidx[:, None]), pos_idx[None, :], 0), axis=1
    )
    last = order[pair_count - 1]
    step_order = jnp.concatenate([order, jnp.full((empty_count,), last, jnp.int32)])
    step_blk = pair_block[step_order]
    step_dst = jnp.concatenate([dst[order], empties])
    step_valid = jnp.concatenate(
        [jnp.ones((pair_count,), jnp.int32), jnp.zeros((empty_count,), jnp.int32)]
    )

    slots = pair_stacks(step_order, step_blk, step_dst, step_valid, full_weights, planes_feat, positions)
    row_width = slots.shape[-1]
    slots = slots.reshape(devices, SLOT, grid_count, row_width)
    received = lax.all_to_all(slots, "tile", 0, 0, tiled=True)

    all_tiles = lax.all_gather(pair_tile, "tile", tiled=True)
    all_energy = lax.all_gather(energy, "tile", axis=0, tiled=True)
    src_owner, src_row = owner_of(all_tiles, tile_order, owned_count)
    src_owner = src_owner.reshape(devices, pair_count)
    src_row = src_row.reshape(devices, pair_count)
    src_slot = slot_of(src_owner)
    rows = jnp.arange(owned_count, dtype=jnp.int32)
    slot_ids = jnp.arange(SLOT, dtype=jnp.int32)
    hit = (
        (src_owner == me)[None, :, None, :]
        & (src_slot[None, :, None, :] == slot_ids[None, None, :, None])
        & (src_row[None, :, None, :] == rows[:, None, None, None])
    )
    select = jnp.sum(hit.astype(jnp.float32), axis=3)
    stacks = jnp.einsum(
        "rds,dsx->rx",
        select,
        received.reshape(devices, SLOT, grid_count * row_width),
        precision=lax.Precision.HIGHEST,
        preferred_element_type=jnp.float32,
    )
    my_tiles = lax.dynamic_slice_in_dim(tile_order, me * owned_count, owned_count)
    energy_mask = all_tiles[None, :] == my_tiles[:, None]
    tile_energy = jnp.sum(jnp.where(energy_mask[:, :, None], all_energy[None, :, :], 0.0), axis=1)

    row_stacks = stacks.reshape(owned_count, grid_count, window_count, 3, LO)
    energy_rows = tile_energy + ENERGY_EPS
    linear = row_stacks[:, :, :, 0, :]
    cosine_sum = row_stacks[:, :, :, 1, :]
    sine_sum = row_stacks[:, :, :, 2, :]
    energy_b = energy_rows[:, :, None, None]
    phase_stack = (
        linear * (cosine_sum * cosine_sum + sine_sum * sine_sum) / (energy_b * jnp.sqrt(energy_b))
    )
    return jnp.transpose(phase_stack, (2, 0, 1, 3))


def solution(mesh):
    return jax.shard_map(
        local,
        mesh=mesh,
        in_specs=(P("tm", "tile", None), P("tile", "tm", None), P("tile"), P("tile"), P()),
        out_specs=P("tm", "tile", None, None),
        check_vma=False,
    )
```

```python
import jax
import jax.numpy as jnp
from jax import lax
from jax.experimental import pallas as pl
from jax.experimental.pallas import tpu as pltpu
from jax.sharding import PartitionSpec as P

LO = 128
SLOT = 2

AMP_FLOOR = 0.5
ENERGY_EPS = 1e-06


def hilbert_build(length):
    row = jnp.arange(LO, dtype=jnp.int32)[:, None]
    col = jnp.arange(length, dtype=jnp.int32)[None, :]
    lag_index = (col - row) % length
    odd_lag = lag_index % 2 == 1
    phase_angle = jnp.pi * lag_index.astype(jnp.float32) / length
    safe_sine = jnp.where(odd_lag, jnp.sin(phase_angle), 1.0)
    kernel = jnp.where(odd_lag, 2.0 / length * jnp.cos(phase_angle) / safe_sine, 0.0)
    first = kernel.astype(jnp.bfloat16)
    return jnp.concatenate(
        [jnp.roll(first, LO * i, axis=1) for i in range(length // LO)], axis=0
    )


def analytic(block_traces, hilbert):
    length = block_traces.shape[-1]
    quadrature = jnp.dot(
        block_traces.reshape(-1, length), hilbert, preferred_element_type=jnp.float32
    )
    quadrature = quadrature.reshape(block_traces.shape)
    real_part = block_traces.astype(jnp.float32)
    amplitude = jnp.maximum(jnp.sqrt(real_part * real_part + quadrature * quadrature), AMP_FLOOR)
    cosine = (real_part / amplitude).astype(jnp.bfloat16)
    sine_part = (quadrature / amplitude).astype(jnp.bfloat16)
    return jnp.stack([block_traces, cosine, sine_part], axis=1)


CHUNK = 8
INFO_ROWS = 8


def pair_kernel(order_ref, bstart_ref, dst_ref, empty_ref, w_ref, info_ref, f_ref, o_ref, wscr):
    b = pl.program_id(0)
    planes = f_ref.shape[0]
    grid_count = w_ref.shape[1]
    pair_count = w_ref.shape[0]
    data_rows = planes * grid_count

    @pl.when(b == 0)
    def _():
        def zero_one(e, carry):
            o_ref[empty_ref[e]] = jnp.zeros(o_ref.shape[1:], o_ref.dtype)
            return carry

        lax.fori_loop(0, empty_ref.shape[0], zero_one, 0)

    lo_idx = bstart_ref[b]
    hi_idx = bstart_ref[b + 1]
    chunks = (hi_idx - lo_idx + CHUNK - 1) // CHUNK

    def one_chunk(ch, carry):
        base = lo_idx + ch * CHUNK
        for k in range(CHUNK):
            p = order_ref[jnp.minimum(base + k, pair_count - 1)]
            wscr[k * grid_count:(k + 1) * grid_count, :] = w_ref[p]
        for j in range(planes):
            res = jnp.dot(wscr[...], f_ref[j], preferred_element_type=jnp.float32)
            for k in range(CHUNK):
                @pl.when(base + k < hi_idx)
                def _():
                    d = dst_ref[base + k]
                    o_ref[d, j * grid_count:(j + 1) * grid_count, :] = res[k * grid_count:(k + 1) * grid_count]
        for k in range(CHUNK):
            @pl.when(base + k < hi_idx)
            def _():
                d = dst_ref[base + k]
                p = order_ref[base + k]
                o_ref[d, data_rows:, :] = info_ref[p]
        return carry

    lax.fori_loop(0, chunks, one_chunk, 0)


def pair_stacks(order, bstart, dst, empties, full_weights, info, planes_feat, positions):
    pair_count, grid_count, channel_count = full_weights.shape
    planes = planes_feat.shape[0]
    blocks = planes_feat.shape[2] // LO
    rows = planes * grid_count + INFO_ROWS
    grid_spec = pltpu.PrefetchScalarGridSpec(
        num_scalar_prefetch=4,
        grid=(blocks,),
        in_specs=[
            pl.BlockSpec(full_weights.shape, lambda b, *_: (0, 0, 0)),
            pl.BlockSpec(info.shape, lambda b, *_: (0, 0, 0)),
            pl.BlockSpec((planes, channel_count, LO), lambda b, *_: (0, 0, b)),
        ],
        out_specs=pl.BlockSpec((positions, rows, LO), lambda b, *_: (0, 0, 0)),
        scratch_shapes=[pltpu.VMEM((CHUNK * grid_count, channel_count), full_weights.dtype)],
    )
    return pl.pallas_call(
        pair_kernel,
        grid_spec=grid_spec,
        out_shape=jax.ShapeDtypeStruct((positions, rows, LO), jnp.float32),
        compiler_params=pltpu.CompilerParams(vmem_limit_bytes=48 * 1024 * 1024),
    )(order, bstart, dst, empties, full_weights, info, planes_feat)


def gather_kernel(x_ref, o_ref):
    owned = o_ref.shape[0]
    data_rows = o_ref.shape[1] - INFO_ROWS
    for r in range(owned):
        def add_one(p, acc):
            x = x_ref[p]
            coef = x[data_rows:data_rows + 1, 32 + r:33 + r]
            return acc + coef * x

        o_ref[r] = lax.fori_loop(0, x_ref.shape[0], add_one, jnp.zeros(x_ref.shape[1:], jnp.float32))


def gather_rows(received, owned):
    return pl.pallas_call(
        gather_kernel,
        out_shape=jax.ShapeDtypeStruct((owned,) + received.shape[1:], jnp.float32),
        compiler_params=pltpu.CompilerParams(vmem_limit_bytes=48 * 1024 * 1024),
    )(received)


def owner_of(pair_tile, tile_order, owned_count):
    tile_count = tile_order.shape[0]
    match = tile_order[None, :] == pair_tile[:, None]
    pos = jnp.sum(jnp.where(match, jnp.arange(tile_count, dtype=jnp.int32)[None, :], 0), axis=1)
    return pos // owned_count, pos % owned_count


def slot_of(owner):
    n = owner.shape[-1]
    idx = jnp.arange(n, dtype=jnp.int32)
    earlier = idx[None, :] < idx[:, None]
    same = owner[..., :, None] == owner[..., None, :]
    return jnp.sum((same & earlier).astype(jnp.int32), axis=-1)


def local(traces, weights, pair_tile, pair_offset, tile_order):
    window_count = traces.shape[0]
    sample_count = traces.shape[2]
    blocks = sample_count // LO
    devices = lax.axis_size("tile")
    tile_count = tile_order.shape[0]
    owned_count = tile_count // devices
    positions = devices * SLOT

    features = analytic(traces, hilbert_build(sample_count))
    planes_feat = features.reshape(window_count * 3, traces.shape[1], sample_count)

    full_weights = lax.all_gather(weights, "tm", axis=1, tiled=True)
    pair_count, grid_count, _ = full_weights.shape
    wf = full_weights.astype(jnp.float32)
    energy = jnp.sum(wf * wf, axis=2)

    pidx = jnp.arange(pair_count, dtype=jnp.int32)
    pair_block = pair_offset // LO
    key = pair_block * pair_count + pidx
    rank = jnp.sum((key[None, :] < key[:, None]).astype(jnp.int32), axis=1)
    order = jnp.sum(jnp.where(rank[None, :] == pidx[:, None], pidx[None, :], 0), axis=1)
    bidx = jnp.arange(blocks + 1, dtype=jnp.int32)
    bstart = jnp.sum((pair_block[None, :] < bidx[:, None]).astype(jnp.int32), axis=1)
    owner, row = owner_of(pair_tile, tile_order, owned_count)
    dst = owner * SLOT + slot_of(owner)
    pos_idx = jnp.arange(positions, dtype=jnp.int32)
    unused = jnp.sum((dst[None, :] == pos_idx[:, None]).astype(jnp.int32), axis=1) == 0
    empty_rank = jnp.cumsum(unused.astype(jnp.int32)) - 1
    empty_count = positions - pair_count
    eidx = jnp.arange(empty_count, dtype=jnp.int32)
    empties = jnp.sum(
        jnp.where(unused[None, :] & (empty_rank[None, :] == eidx[:, None]), pos_idx[None, :], 0), axis=1
    )
    dst_sorted = jnp.sum(jnp.where(order[:, None] == pidx[None, :], dst[None, :], 0), axis=1)

    lanes = jnp.arange(LO, dtype=jnp.int32)[None, :]
    energy_lanes = jnp.pad(energy, ((0, 0), (0, LO - grid_count)))
    info_row = jnp.where(lanes < grid_count, energy_lanes, jnp.where(lanes - 32 == row[:, None], 1.0, 0.0))
    info = jnp.concatenate(
        [info_row[:, None, :], jnp.zeros((pair_count, INFO_ROWS - 1, LO), jnp.float32)], axis=1
    )

    slots = pair_stacks(order, bstart, dst_sorted, empties, full_weights, info, planes_feat, positions)
    rows = slots.shape[1]
    received = lax.all_to_all(slots.reshape(devices, SLOT, rows, LO), "tile", 0, 0, tiled=True)
    stacks = gather_rows(received.reshape(positions, rows, LO), owned_count)

    data_rows = rows - INFO_ROWS
    tile_energy = stacks[:, data_rows, :grid_count]
    row_stacks = stacks[:, :data_rows].reshape(owned_count, window_count, 3, grid_count, LO)
    energy_rows = tile_energy + ENERGY_EPS
    linear = row_stacks[:, :, 0]
    cosine_sum = row_stacks[:, :, 1]
    sine_sum = row_stacks[:, :, 2]
    energy_b = energy_rows[:, None, :, None]
    phase_stack = (
        linear * (cosine_sum * cosine_sum + sine_sum * sine_sum) / (energy_b * jnp.sqrt(energy_b))
    )
    return jnp.transpose(phase_stack, (1, 0, 2, 3))


def solution(mesh):
    return jax.shard_map(
        local,
        mesh=mesh,
        in_specs=(P("tm", "tile", None), P("tile", "tm", None), P("tile"), P("tile"), P()),
        out_specs=P("tm", "tile", None, None),
        check_vma=False,
    )
```

```python
import jax
import jax.numpy as jnp
from jax import lax
from jax.experimental import pallas as pl
from jax.experimental.pallas import tpu as pltpu
from jax.sharding import PartitionSpec as P

LO = 128
SLOT = 2

AMP_FLOOR = 0.5
ENERGY_EPS = 1e-06


def hilbert_build(length):
    row = jnp.arange(LO, dtype=jnp.int32)[:, None]
    col = jnp.arange(length, dtype=jnp.int32)[None, :]
    lag_index = (col - row) % length
    odd_lag = lag_index % 2 == 1
    phase_angle = jnp.pi * lag_index.astype(jnp.float32) / length
    safe_sine = jnp.where(odd_lag, jnp.sin(phase_angle), 1.0)
    kernel = jnp.where(odd_lag, 2.0 / length * jnp.cos(phase_angle) / safe_sine, 0.0)
    first = kernel.astype(jnp.bfloat16)
    return jnp.concatenate(
        [jnp.roll(first, LO * i, axis=1) for i in range(length // LO)], axis=0
    )


def analytic(block_traces, hilbert):
    length = block_traces.shape[-1]
    quadrature = jnp.dot(
        block_traces.reshape(-1, length), hilbert, preferred_element_type=jnp.float32
    )
    quadrature = quadrature.reshape(block_traces.shape)
    real_part = block_traces.astype(jnp.float32)
    amplitude = jnp.maximum(jnp.sqrt(real_part * real_part + quadrature * quadrature), AMP_FLOOR)
    cosine = (real_part / amplitude).astype(jnp.bfloat16)
    sine_part = (quadrature / amplitude).astype(jnp.bfloat16)
    planes = []
    for w in range(block_traces.shape[0]):
        planes += [block_traces[w], cosine[w], sine_part[w]]
    return jnp.stack(planes, axis=0)


CHUNK = 8
INFO_ROWS = 8


def pair_kernel(order_ref, bstart_ref, dst_ref, empty_ref, w_ref, info_ref, f_ref, o_ref, wscr):
    b = pl.program_id(0)
    planes = f_ref.shape[0]
    grid_count = w_ref.shape[1]
    pair_count = w_ref.shape[0]
    data_rows = planes * grid_count

    @pl.when(b == 0)
    def _():
        def zero_one(e, carry):
            o_ref[empty_ref[e]] = jnp.zeros(o_ref.shape[1:], o_ref.dtype)
            return carry

        lax.fori_loop(0, empty_ref.shape[0], zero_one, 0)

    lo_idx = bstart_ref[b]
    hi_idx = bstart_ref[b + 1]
    chunks = (hi_idx - lo_idx + CHUNK - 1) // CHUNK

    def one_chunk(ch, carry):
        base = lo_idx + ch * CHUNK
        for k in range(CHUNK):
            p = order_ref[jnp.minimum(base + k, pair_count - 1)]
            wscr[k * grid_count:(k + 1) * grid_count, :] = w_ref[p]
        for j in range(planes):
            res = jnp.dot(wscr[...], f_ref[j], preferred_element_type=jnp.float32)
            for k in range(CHUNK):
                @pl.when(base + k < hi_idx)
                def _():
                    d = dst_ref[base + k]
                    o_ref[d, j * grid_count:(j + 1) * grid_count, :] = res[k * grid_count:(k + 1) * grid_count]
        for k in range(CHUNK):
            @pl.when(base + k < hi_idx)
            def _():
                d = dst_ref[base + k]
                p = order_ref[base + k]
                o_ref[d, data_rows:, :] = info_ref[p]
        return carry

    lax.fori_loop(0, chunks, one_chunk, 0)


def pair_stacks(order, bstart, dst, empties, full_weights, info, planes_feat, positions):
    pair_count, grid_count, channel_count = full_weights.shape
    planes = planes_feat.shape[0]
    blocks = planes_feat.shape[2] // LO
    rows = planes * grid_count + INFO_ROWS
    grid_spec = pltpu.PrefetchScalarGridSpec(
        num_scalar_prefetch=4,
        grid=(blocks,),
        in_specs=[
            pl.BlockSpec(full_weights.shape, lambda b, *_: (0, 0, 0)),
            pl.BlockSpec(info.shape, lambda b, *_: (0, 0, 0)),
            pl.BlockSpec((planes, channel_count, LO), lambda b, *_: (0, 0, b)),
        ],
        out_specs=pl.BlockSpec((positions, rows, LO), lambda b, *_: (0, 0, 0)),
        scratch_shapes=[pltpu.VMEM((CHUNK * grid_count, channel_count), full_weights.dtype)],
    )
    return pl.pallas_call(
        pair_kernel,
        grid_spec=grid_spec,
        out_shape=jax.ShapeDtypeStruct((positions, rows, LO), jnp.float32),
        compiler_params=pltpu.CompilerParams(vmem_limit_bytes=48 * 1024 * 1024),
    )(order, bstart, dst, empties, full_weights, info, planes_feat)


def gather_kernel(row_ref, x_ref, o_ref):
    c = pl.program_id(0)
    per = x_ref.shape[0]

    @pl.when(c == 0)
    def _():
        o_ref[...] = jnp.zeros(o_ref.shape, o_ref.dtype)

    for q in range(per):
        r = row_ref[c * per + q]

        @pl.when(r >= 0)
        def _():
            o_ref[r] += x_ref[q]


def gather_rows(received, owned):
    positions, rows, lanes = received.shape
    data_rows = rows - INFO_ROWS
    onehot = received[:, data_rows, 32:32 + owned]
    row = jnp.where(
        jnp.sum(onehot, axis=1) > 0.5,
        jnp.sum(onehot * jnp.arange(owned, dtype=jnp.float32)[None, :], axis=1),
        -1.0,
    ).astype(jnp.int32)
    per = 8
    grid_spec = pltpu.PrefetchScalarGridSpec(
        num_scalar_prefetch=1,
        grid=(positions // per,),
        in_specs=[pl.BlockSpec((per, rows, lanes), lambda c, r: (c, 0, 0))],
        out_specs=pl.BlockSpec((owned, rows, lanes), lambda c, r: (0, 0, 0)),
    )
    return pl.pallas_call(
        gather_kernel,
        grid_spec=grid_spec,
        out_shape=jax.ShapeDtypeStruct((owned, rows, lanes), jnp.float32),
    )(row, received)


def owner_of(pair_tile, tile_order, owned_count):
    tile_count = tile_order.shape[0]
    match = tile_order[None, :] == pair_tile[:, None]
    pos = jnp.sum(jnp.where(match, jnp.arange(tile_count, dtype=jnp.int32)[None, :], 0), axis=1)
    return pos // owned_count, pos % owned_count


def slot_of(owner):
    n = owner.shape[-1]
    idx = jnp.arange(n, dtype=jnp.int32)
    earlier = idx[None, :] < idx[:, None]
    same = owner[..., :, None] == owner[..., None, :]
    return jnp.sum((same & earlier).astype(jnp.int32), axis=-1)


def local(traces, weights, pair_tile, pair_offset, tile_order):
    window_count = traces.shape[0]
    sample_count = traces.shape[2]
    blocks = sample_count // LO
    devices = lax.axis_size("tile")
    tile_count = tile_order.shape[0]
    owned_count = tile_count // devices
    positions = devices * SLOT

    features = analytic(traces, hilbert_build(sample_count))
    planes_feat = features

    full_weights = lax.all_gather(weights, "tm", axis=1, tiled=True)
    pair_count, grid_count, _ = full_weights.shape
    wf = full_weights.astype(jnp.float32)
    energy = jnp.sum(wf * wf, axis=2)

    pidx = jnp.arange(pair_count, dtype=jnp.int32)
    pair_block = pair_offset // LO
    key = pair_block * pair_count + pidx
    rank = jnp.sum((key[None, :] < key[:, None]).astype(jnp.int32), axis=1)
    order = jnp.sum(jnp.where(rank[None, :] == pidx[:, None], pidx[None, :], 0), axis=1)
    bidx = jnp.arange(blocks + 1, dtype=jnp.int32)
    bstart = jnp.sum((pair_block[None, :] < bidx[:, None]).astype(jnp.int32), axis=1)
    owner, row = owner_of(pair_tile, tile_order, owned_count)
    dst = owner * SLOT + slot_of(owner)
    pos_idx = jnp.arange(positions, dtype=jnp.int32)
    unused = jnp.sum((dst[None, :] == pos_idx[:, None]).astype(jnp.int32), axis=1) == 0
    empty_rank = jnp.cumsum(unused.astype(jnp.int32)) - 1
    empty_count = positions - pair_count
    eidx = jnp.arange(empty_count, dtype=jnp.int32)
    empties = jnp.sum(
        jnp.where(unused[None, :] & (empty_rank[None, :] == eidx[:, None]), pos_idx[None, :], 0), axis=1
    )
    dst_sorted = jnp.sum(jnp.where(order[:, None] == pidx[None, :], dst[None, :], 0), axis=1)

    lanes = jnp.arange(LO, dtype=jnp.int32)[None, :]
    energy_lanes = jnp.pad(energy, ((0, 0), (0, LO - grid_count)))
    info_row = jnp.where(lanes < grid_count, energy_lanes, jnp.where(lanes - 32 == row[:, None], 1.0, 0.0))
    info = jnp.concatenate(
        [info_row[:, None, :], jnp.zeros((pair_count, INFO_ROWS - 1, LO), jnp.float32)], axis=1
    )

    slots = pair_stacks(order, bstart, dst_sorted, empties, full_weights, info, planes_feat, positions)
    rows = slots.shape[1]
    received = lax.all_to_all(slots.reshape(devices, SLOT, rows, LO), "tile", 0, 0, tiled=True)
    stacks = gather_rows(received.reshape(positions, rows, LO), owned_count)

    data_rows = rows - INFO_ROWS
    tile_energy = stacks[:, data_rows, :grid_count]
    row_stacks = stacks[:, :data_rows].reshape(owned_count, window_count, 3, grid_count, LO)
    energy_rows = tile_energy + ENERGY_EPS
    linear = row_stacks[:, :, 0]
    cosine_sum = row_stacks[:, :, 1]
    sine_sum = row_stacks[:, :, 2]
    energy_b = energy_rows[:, None, :, None]
    phase_stack = (
        linear * (cosine_sum * cosine_sum + sine_sum * sine_sum) / (energy_b * jnp.sqrt(energy_b))
    )
    return jnp.transpose(phase_stack, (1, 0, 2, 3))


def solution(mesh):
    return jax.shard_map(
        local,
        mesh=mesh,
        in_specs=(P("tm", "tile", None), P("tile", "tm", None), P("tile"), P("tile"), P()),
        out_specs=P("tm", "tile", None, None),
        check_vma=False,
    )
```

```python
import jax
import jax.numpy as jnp
from jax import lax
from jax.experimental import pallas as pl
from jax.experimental.pallas import tpu as pltpu
from jax.sharding import PartitionSpec as P

LO = 128
SLOT = 2

AMP_FLOOR = 0.5
ENERGY_EPS = 1e-06


def hilbert_build(length):
    row = jnp.arange(LO, dtype=jnp.int32)[:, None]
    col = jnp.arange(length, dtype=jnp.int32)[None, :]
    lag_index = (col - row) % length
    odd_lag = lag_index % 2 == 1
    phase_angle = jnp.pi * lag_index.astype(jnp.float32) / length
    safe_sine = jnp.where(odd_lag, jnp.sin(phase_angle), 1.0)
    kernel = jnp.where(odd_lag, 2.0 / length * jnp.cos(phase_angle) / safe_sine, 0.0)
    first = kernel.astype(jnp.bfloat16)
    return jnp.concatenate(
        [jnp.roll(first, LO * i, axis=1) for i in range(length // LO)], axis=0
    )


def analytic(window_traces, hilbert):
    quadrature = jnp.dot(window_traces, hilbert, preferred_element_type=jnp.float32)
    real_part = window_traces.astype(jnp.float32)
    amplitude = jnp.maximum(jnp.sqrt(real_part * real_part + quadrature * quadrature), AMP_FLOOR)
    cosine = (real_part / amplitude).astype(jnp.bfloat16)
    sine_part = (quadrature / amplitude).astype(jnp.bfloat16)
    return jnp.stack([window_traces, cosine, sine_part], axis=0)


CHUNK = 8
INFO_ROWS = 8


def pair_kernel(order_ref, bstart_ref, dst_ref, empty_ref, w_ref, info_ref, f_ref, o_ref, wscr):
    b = pl.program_id(0)
    with_info = o_ref.shape[1] > f_ref.shape[0] * w_ref.shape[1]
    planes = f_ref.shape[0]
    grid_count = w_ref.shape[1]
    pair_count = w_ref.shape[0]
    data_rows = planes * grid_count

    @pl.when(b == 0)
    def _():
        def zero_one(e, carry):
            o_ref[empty_ref[e]] = jnp.zeros(o_ref.shape[1:], o_ref.dtype)
            return carry

        lax.fori_loop(0, empty_ref.shape[0], zero_one, 0)

    lo_idx = bstart_ref[b]
    hi_idx = bstart_ref[b + 1]
    chunks = (hi_idx - lo_idx + CHUNK - 1) // CHUNK

    def one_chunk(ch, carry):
        base = lo_idx + ch * CHUNK
        for k in range(CHUNK):
            p = order_ref[jnp.minimum(base + k, pair_count - 1)]
            wscr[k * grid_count:(k + 1) * grid_count, :] = w_ref[p]
        for j in range(planes):
            res = jnp.dot(wscr[...], f_ref[j], preferred_element_type=jnp.float32)
            for k in range(CHUNK):
                @pl.when(base + k < hi_idx)
                def _():
                    d = dst_ref[base + k]
                    o_ref[d, j * grid_count:(j + 1) * grid_count, :] = res[k * grid_count:(k + 1) * grid_count]
        for k in range(CHUNK if with_info else 0):
            @pl.when(base + k < hi_idx)
            def _():
                d = dst_ref[base + k]
                p = order_ref[base + k]
                o_ref[d, data_rows:, :] = info_ref[p]
        return carry

    lax.fori_loop(0, chunks, one_chunk, 0)


def pair_stacks(order, bstart, dst, empties, full_weights, info, planes_feat, positions, with_info):
    pair_count, grid_count, channel_count = full_weights.shape
    planes = planes_feat.shape[0]
    blocks = planes_feat.shape[2] // LO
    rows = planes * grid_count + (INFO_ROWS if with_info else 0)
    grid_spec = pltpu.PrefetchScalarGridSpec(
        num_scalar_prefetch=4,
        grid=(blocks,),
        in_specs=[
            pl.BlockSpec(full_weights.shape, lambda b, *_: (0, 0, 0)),
            pl.BlockSpec(info.shape, lambda b, *_: (0, 0, 0)),
            pl.BlockSpec((planes, channel_count, LO), lambda b, *_: (0, 0, b)),
        ],
        out_specs=pl.BlockSpec((positions, rows, LO), lambda b, *_: (0, 0, 0)),
        scratch_shapes=[pltpu.VMEM((CHUNK * grid_count, channel_count), full_weights.dtype)],
    )
    return pl.pallas_call(
        pair_kernel,
        grid_spec=grid_spec,
        out_shape=jax.ShapeDtypeStruct((positions, rows, LO), jnp.float32),
        compiler_params=pltpu.CompilerParams(vmem_limit_bytes=48 * 1024 * 1024),
    )(order, bstart, dst, empties, full_weights, info, planes_feat)


def gather_kernel(row_ref, x_ref, o_ref):
    c = pl.program_id(0)
    per = x_ref.shape[0]

    @pl.when(c == 0)
    def _():
        o_ref[...] = jnp.zeros(o_ref.shape, o_ref.dtype)

    for q in range(per):
        r = row_ref[c * per + q]

        @pl.when(r >= 0)
        def _():
            o_ref[r] += x_ref[q]


def slot_rows(received, owned, data_rows):
    onehot = received[:, data_rows, 32:32 + owned]
    return jnp.where(
        jnp.sum(onehot, axis=1) > 0.5,
        jnp.sum(onehot * jnp.arange(owned, dtype=jnp.float32)[None, :], axis=1),
        -1.0,
    ).astype(jnp.int32)


def gather_rows(received, row, owned):
    positions, rows, lanes = received.shape
    per = 8
    grid_spec = pltpu.PrefetchScalarGridSpec(
        num_scalar_prefetch=1,
        grid=(positions // per,),
        in_specs=[pl.BlockSpec((per, rows, lanes), lambda c, r: (c, 0, 0))],
        out_specs=pl.BlockSpec((owned, rows, lanes), lambda c, r: (0, 0, 0)),
    )
    return pl.pallas_call(
        gather_kernel,
        grid_spec=grid_spec,
        out_shape=jax.ShapeDtypeStruct((owned, rows, lanes), jnp.float32),
    )(row, received)


def owner_of(pair_tile, tile_order, owned_count):
    tile_count = tile_order.shape[0]
    match = tile_order[None, :] == pair_tile[:, None]
    pos = jnp.sum(jnp.where(match, jnp.arange(tile_count, dtype=jnp.int32)[None, :], 0), axis=1)
    return pos // owned_count, pos % owned_count


def slot_of(owner):
    n = owner.shape[-1]
    idx = jnp.arange(n, dtype=jnp.int32)
    earlier = idx[None, :] < idx[:, None]
    same = owner[..., :, None] == owner[..., None, :]
    return jnp.sum((same & earlier).astype(jnp.int32), axis=-1)


def local(traces, weights, pair_tile, pair_offset, tile_order):
    window_count = traces.shape[0]
    sample_count = traces.shape[2]
    blocks = sample_count // LO
    devices = lax.axis_size("tile")
    tile_count = tile_order.shape[0]
    owned_count = tile_count // devices
    positions = devices * SLOT

    hilbert = hilbert_build(sample_count)

    full_weights = lax.all_gather(weights, "tm", axis=1, tiled=True)
    pair_count, grid_count, _ = full_weights.shape
    wf = full_weights.astype(jnp.float32)
    energy = jnp.sum(wf * wf, axis=2)

    pidx = jnp.arange(pair_count, dtype=jnp.int32)
    pair_block = pair_offset // LO
    key = pair_block * pair_count + pidx
    rank = jnp.sum((key[None, :] < key[:, None]).astype(jnp.int32), axis=1)
    order = jnp.sum(jnp.where(rank[None, :] == pidx[:, None], pidx[None, :], 0), axis=1)
    bidx = jnp.arange(blocks + 1, dtype=jnp.int32)
    bstart = jnp.sum((pair_block[None, :] < bidx[:, None]).astype(jnp.int32), axis=1)
    owner, row = owner_of(pair_tile, tile_order, owned_count)
    dst = owner * SLOT + slot_of(owner)
    pos_idx = jnp.arange(positions, dtype=jnp.int32)
    unused = jnp.sum((dst[None, :] == pos_idx[:, None]).astype(jnp.int32), axis=1) == 0
    empty_rank = jnp.cumsum(unused.astype(jnp.int32)) - 1
    empty_count = positions - pair_count
    eidx = jnp.arange(empty_count, dtype=jnp.int32)
    empties = jnp.sum(
        jnp.where(unused[None, :] & (empty_rank[None, :] == eidx[:, None]), pos_idx[None, :], 0), axis=1
    )
    dst_sorted = jnp.sum(jnp.where(order[:, None] == pidx[None, :], dst[None, :], 0), axis=1)

    lanes = jnp.arange(LO, dtype=jnp.int32)[None, :]
    energy_lanes = jnp.pad(energy, ((0, 0), (0, LO - grid_count)))
    info_row = jnp.where(lanes < grid_count, energy_lanes, jnp.where(lanes - 32 == row[:, None], 1.0, 0.0))
    info = jnp.concatenate(
        [info_row[:, None, :], jnp.zeros((pair_count, INFO_ROWS - 1, LO), jnp.float32)], axis=1
    )

    stacks = []
    row_of_slot = None
    for w in range(window_count):
        planes_feat = analytic(traces[w], hilbert)
        with_info = w == 0
        slots = pair_stacks(
            order, bstart, dst_sorted, empties, full_weights, info, planes_feat, positions, with_info
        )
        rows = slots.shape[1]
        received = lax.all_to_all(slots.reshape(devices, SLOT, rows, LO), "tile", 0, 0, tiled=True)
        received = received.reshape(positions, rows, LO)
        if with_info:
            row_of_slot = slot_rows(received, owned_count, rows - INFO_ROWS)
        stacks.append(gather_rows(received, row_of_slot, owned_count))

    data_rows = 3 * grid_count
    tile_energy = stacks[0][:, data_rows, :grid_count]
    energy_rows = tile_energy + ENERGY_EPS
    energy_b = energy_rows[:, :, None]
    out = []
    for w in range(window_count):
        row_stacks = stacks[w][:, :data_rows].reshape(owned_count, 3, grid_count, LO)
        linear = row_stacks[:, 0]
        cosine_sum = row_stacks[:, 1]
        sine_sum = row_stacks[:, 2]
        out.append(
            linear * (cosine_sum * cosine_sum + sine_sum * sine_sum) / (energy_b * jnp.sqrt(energy_b))
        )
    return jnp.stack(out, axis=0)


def solution(mesh):
    return jax.shard_map(
        local,
        mesh=mesh,
        in_specs=(P("tm", "tile", None), P("tile", "tm", None), P("tile"), P("tile"), P()),
        out_specs=P("tm", "tile", None, None),
        check_vma=False,
    )
```

```python
import jax
import jax.numpy as jnp
from jax import lax
from jax.experimental import pallas as pl
from jax.experimental.pallas import tpu as pltpu
from jax.sharding import PartitionSpec as P

LO = 128
SLOT = 2

AMP_FLOOR = 0.5
ENERGY_EPS = 1e-06


def hilbert_build(length):
    row = jnp.arange(LO, dtype=jnp.int32)[:, None]
    col = jnp.arange(length, dtype=jnp.int32)[None, :]
    lag_index = (col - row) % length
    odd_lag = lag_index % 2 == 1
    phase_angle = jnp.pi * lag_index.astype(jnp.float32) / length
    safe_sine = jnp.where(odd_lag, jnp.sin(phase_angle), 1.0)
    kernel = jnp.where(odd_lag, 2.0 / length * jnp.cos(phase_angle) / safe_sine, 0.0)
    first = kernel.astype(jnp.bfloat16)
    return jnp.concatenate(
        [jnp.roll(first, LO * i, axis=1) for i in range(length // LO)], axis=0
    )


def analytic(window_traces, hilbert):
    quadrature = jnp.dot(window_traces, hilbert, preferred_element_type=jnp.float32)
    real_part = window_traces.astype(jnp.float32)
    amplitude = jnp.maximum(jnp.sqrt(real_part * real_part + quadrature * quadrature), AMP_FLOOR)
    cosine = (real_part / amplitude).astype(jnp.bfloat16)
    sine_part = (quadrature / amplitude).astype(jnp.bfloat16)
    return jnp.stack([window_traces, cosine, sine_part], axis=0)


CHUNK = 8
INFO_ROWS = 8


def pair_kernel(order_ref, bstart_ref, dst_ref, empty_ref, w_ref, f_ref, o_ref, wscr):
    b = pl.program_id(0)
    planes = f_ref.shape[0]
    grid_count = w_ref.shape[1]
    pair_count = w_ref.shape[0]
    data_rows = planes * grid_count

    @pl.when(b == 0)
    def _():
        def zero_one(e, carry):
            o_ref[empty_ref[e]] = jnp.zeros(o_ref.shape[1:], o_ref.dtype)
            return carry

        lax.fori_loop(0, empty_ref.shape[0], zero_one, 0)

    lo_idx = bstart_ref[b]
    hi_idx = bstart_ref[b + 1]
    chunks = (hi_idx - lo_idx + CHUNK - 1) // CHUNK

    def one_chunk(ch, carry):
        base = lo_idx + ch * CHUNK
        for k in range(CHUNK):
            p = order_ref[jnp.minimum(base + k, pair_count - 1)]
            wscr[k * grid_count:(k + 1) * grid_count, :] = w_ref[p]
        for j in range(planes):
            res = jnp.dot(wscr[...], f_ref[j], preferred_element_type=jnp.float32)
            for k in range(CHUNK):
                @pl.when(base + k < hi_idx)
                def _():
                    d = dst_ref[base + k]
                    o_ref[d, j * grid_count:(j + 1) * grid_count, :] = res[k * grid_count:(k + 1) * grid_count]
        return carry

    lax.fori_loop(0, chunks, one_chunk, 0)


def pair_stacks(order, bstart, dst, empties, full_weights, info, planes_feat, positions, with_info):
    pair_count, grid_count, channel_count = full_weights.shape
    planes = planes_feat.shape[0]
    blocks = planes_feat.shape[2] // LO
    rows = planes * grid_count + (INFO_ROWS if with_info else 0)
    grid_spec = pltpu.PrefetchScalarGridSpec(
        num_scalar_prefetch=4,
        grid=(blocks,),
        in_specs=[
            pl.BlockSpec(full_weights.shape, lambda b, *_: (0, 0, 0)),
            pl.BlockSpec((planes, channel_count, LO), lambda b, *_: (0, 0, b)),
        ],
        out_specs=pl.BlockSpec((positions, rows, LO), lambda b, *_: (0, 0, 0)),
        scratch_shapes=[pltpu.VMEM((CHUNK * grid_count, channel_count), full_weights.dtype)],
    )
    return pl.pallas_call(
        pair_kernel,
        grid_spec=grid_spec,
        out_shape=jax.ShapeDtypeStruct((positions, rows, LO), jnp.float32),
        compiler_params=pltpu.CompilerParams(vmem_limit_bytes=48 * 1024 * 1024),
    )(order, bstart, dst, empties, full_weights, planes_feat)


def gather_kernel(row_ref, x_ref, o_ref):
    c = pl.program_id(0)
    per = x_ref.shape[0]

    @pl.when(c == 0)
    def _():
        o_ref[...] = jnp.zeros(o_ref.shape, o_ref.dtype)

    for q in range(per):
        r = row_ref[c * per + q]

        @pl.when(r >= 0)
        def _():
            o_ref[r] += x_ref[q]


def slot_rows(received, owned, data_rows):
    onehot = received[:, data_rows, 32:32 + owned]
    return jnp.where(
        jnp.sum(onehot, axis=1) > 0.5,
        jnp.sum(onehot * jnp.arange(owned, dtype=jnp.float32)[None, :], axis=1),
        -1.0,
    ).astype(jnp.int32)


def gather_rows(received, row, owned):
    positions, rows, lanes = received.shape
    per = 8
    grid_spec = pltpu.PrefetchScalarGridSpec(
        num_scalar_prefetch=1,
        grid=(positions // per,),
        in_specs=[pl.BlockSpec((per, rows, lanes), lambda c, r: (c, 0, 0))],
        out_specs=pl.BlockSpec((owned, rows, lanes), lambda c, r: (0, 0, 0)),
    )
    return pl.pallas_call(
        gather_kernel,
        grid_spec=grid_spec,
        out_shape=jax.ShapeDtypeStruct((owned, rows, lanes), jnp.float32),
    )(row, received)


def owner_of(pair_tile, tile_order, owned_count):
    tile_count = tile_order.shape[0]
    match = tile_order[None, :] == pair_tile[:, None]
    pos = jnp.sum(jnp.where(match, jnp.arange(tile_count, dtype=jnp.int32)[None, :], 0), axis=1)
    return pos // owned_count, pos % owned_count


def slot_of(owner):
    n = owner.shape[-1]
    idx = jnp.arange(n, dtype=jnp.int32)
    earlier = idx[None, :] < idx[:, None]
    same = owner[..., :, None] == owner[..., None, :]
    return jnp.sum((same & earlier).astype(jnp.int32), axis=-1)


def local(traces, weights, pair_tile, pair_offset, tile_order):
    window_count = traces.shape[0]
    sample_count = traces.shape[2]
    blocks = sample_count // LO
    devices = lax.axis_size("tile")
    tile_count = tile_order.shape[0]
    owned_count = tile_count // devices
    positions = devices * SLOT

    hilbert = hilbert_build(sample_count)

    full_weights = lax.all_gather(weights, "tm", axis=1, tiled=True)
    pair_count, grid_count, _ = full_weights.shape
    wf = full_weights.astype(jnp.float32)
    energy = jnp.sum(wf * wf, axis=2)

    pidx = jnp.arange(pair_count, dtype=jnp.int32)
    pair_block = pair_offset // LO
    key = pair_block * pair_count + pidx
    rank = jnp.sum((key[None, :] < key[:, None]).astype(jnp.int32), axis=1)
    order = jnp.sum(jnp.where(rank[None, :] == pidx[:, None], pidx[None, :], 0), axis=1)
    bidx = jnp.arange(blocks + 1, dtype=jnp.int32)
    bstart = jnp.sum((pair_block[None, :] < bidx[:, None]).astype(jnp.int32), axis=1)
    owner, row = owner_of(pair_tile, tile_order, owned_count)
    dst = owner * SLOT + slot_of(owner)
    pos_idx = jnp.arange(positions, dtype=jnp.int32)
    unused = jnp.sum((dst[None, :] == pos_idx[:, None]).astype(jnp.int32), axis=1) == 0
    empty_rank = jnp.cumsum(unused.astype(jnp.int32)) - 1
    empty_count = positions - pair_count
    eidx = jnp.arange(empty_count, dtype=jnp.int32)
    empties = jnp.sum(
        jnp.where(unused[None, :] & (empty_rank[None, :] == eidx[:, None]), pos_idx[None, :], 0), axis=1
    )
    dst_sorted = jnp.sum(jnp.where(order[:, None] == pidx[None, :], dst[None, :], 0), axis=1)

    feature_max = jnp.maximum(jnp.max(jnp.abs(traces.astype(jnp.float32))), 1.0)
    bound = jnp.max(jnp.sum(jnp.abs(wf), axis=2), axis=1) * feature_max
    exponent = jnp.where(bound > 0, jnp.ceil(jnp.log2(jnp.maximum(bound, 1e-30))) - 14.0, 0.0)

    lanes = jnp.arange(LO, dtype=jnp.int32)[None, :]
    energy_lanes = jnp.pad(energy, ((0, 0), (0, LO - grid_count)))
    info_row = jnp.where(
        lanes < grid_count,
        energy_lanes,
        jnp.where(lanes - 32 == row[:, None], 1.0, jnp.where(lanes == 40, exponent[:, None], 0.0)),
    )
    pos_pair = jnp.sum(jnp.where(dst[None, :] == pos_idx[:, None], pidx[None, :] + 1, 0), axis=1) - 1
    info_pos = jnp.where((pos_pair >= 0)[:, None], info_row[jnp.maximum(pos_pair, 0)], 0.0)
    info_pos = jnp.concatenate(
        [info_pos[:, None, :], jnp.zeros((positions, INFO_ROWS - 1, LO), jnp.float32)], axis=1
    )
    info_recv = lax.all_to_all(info_pos.reshape(devices, SLOT, INFO_ROWS, LO), "tile", 0, 0, tiled=True)
    info_recv = info_recv.reshape(positions, INFO_ROWS, LO)
    row_of_slot = slot_rows(info_recv, owned_count, 0)
    recv_scale = jnp.exp2(info_recv[:, 0, 40])
    send_exp = jnp.where(pos_pair >= 0, exponent[jnp.maximum(pos_pair, 0)], 0.0)
    send_inv = jnp.exp2(-send_exp)

    stacks = []
    for w in range(window_count):
        planes_feat = analytic(traces[w], hilbert)
        slots = pair_stacks(
            order, bstart, dst_sorted, empties, full_weights, None, planes_feat, positions, False
        )
        rows = slots.shape[1]
        wire = (slots * send_inv[:, None, None]).astype(jnp.float16)
        received = lax.all_to_all(wire.reshape(devices, SLOT, rows, LO), "tile", 0, 0, tiled=True)
        received = received.reshape(positions, rows, LO).astype(jnp.float32) * recv_scale[:, None, None]
        stacks.append(gather_rows(received, row_of_slot, owned_count))

    data_rows = 3 * grid_count
    tile_energy = jnp.sum(
        jnp.where((row_of_slot[None, :] == jnp.arange(owned_count)[:, None])[:, :, None],
                  info_recv[None, :, 0, :grid_count], 0.0),
        axis=1,
    )
    energy_rows = tile_energy + ENERGY_EPS
    energy_b = energy_rows[:, :, None]
    out = []
    for w in range(window_count):
        row_stacks = stacks[w].reshape(owned_count, 3, grid_count, LO)
        linear = row_stacks[:, 0]
        cosine_sum = row_stacks[:, 1]
        sine_sum = row_stacks[:, 2]
        out.append(
            linear * (cosine_sum * cosine_sum + sine_sum * sine_sum) / (energy_b * jnp.sqrt(energy_b))
        )
    return jnp.stack(out, axis=0)


def solution(mesh):
    return jax.shard_map(
        local,
        mesh=mesh,
        in_specs=(P("tm", "tile", None), P("tile", "tm", None), P("tile"), P("tile"), P()),
        out_specs=P("tm", "tile", None, None),
        check_vma=False,
    )
```

```python
import jax
import jax.numpy as jnp
from jax import lax
from jax.experimental import pallas as pl
from jax.experimental.pallas import tpu as pltpu
from jax.sharding import PartitionSpec as P

LO = 128
SLOT = 2

AMP_FLOOR = 0.5
ENERGY_EPS = 1e-06


def hilbert_build(length):
    row = jnp.arange(LO, dtype=jnp.int32)[:, None]
    col = jnp.arange(length, dtype=jnp.int32)[None, :]
    lag_index = (col - row) % length
    odd_lag = lag_index % 2 == 1
    phase_angle = jnp.pi * lag_index.astype(jnp.float32) / length
    safe_sine = jnp.where(odd_lag, jnp.sin(phase_angle), 1.0)
    kernel = jnp.where(odd_lag, 2.0 / length * jnp.cos(phase_angle) / safe_sine, 0.0)
    first = kernel.astype(jnp.bfloat16)
    return jnp.concatenate(
        [jnp.roll(first, LO * i, axis=1) for i in range(length // LO)], axis=0
    )


def analytic(window_traces, hilbert):
    quadrature = jnp.dot(window_traces, hilbert, preferred_element_type=jnp.float32)
    real_part = window_traces.astype(jnp.float32)
    amplitude = jnp.maximum(jnp.sqrt(real_part * real_part + quadrature * quadrature), AMP_FLOOR)
    cosine = (real_part / amplitude).astype(jnp.bfloat16)
    sine_part = (quadrature / amplitude).astype(jnp.bfloat16)
    return jnp.stack([window_traces, cosine, sine_part], axis=0)


CHUNK = 8
INFO_ROWS = 8


def pair_kernel(order_ref, bstart_ref, dst_ref, empty_ref, w_ref, f_ref, o_ref, wscr):
    b = pl.program_id(0)
    planes = f_ref.shape[0]
    grid_count = w_ref.shape[1]
    pair_count = w_ref.shape[0]
    data_rows = planes * grid_count

    @pl.when(b == 0)
    def _():
        def zero_one(e, carry):
            o_ref[empty_ref[e]] = jnp.zeros(o_ref.shape[1:], o_ref.dtype)
            return carry

        lax.fori_loop(0, empty_ref.shape[0], zero_one, 0)

    lo_idx = bstart_ref[b]
    hi_idx = bstart_ref[b + 1]
    chunks = (hi_idx - lo_idx + CHUNK - 1) // CHUNK

    def one_chunk(ch, carry):
        base = lo_idx + ch * CHUNK
        for k in range(CHUNK):
            p = order_ref[jnp.minimum(base + k, pair_count - 1)]
            wscr[k * grid_count:(k + 1) * grid_count, :] = w_ref[p]
        for j in range(planes):
            res = jnp.dot(wscr[...], f_ref[j], preferred_element_type=jnp.float32)
            for k in range(CHUNK):
                @pl.when(base + k < hi_idx)
                def _():
                    d = dst_ref[base + k]
                    o_ref[d, j * grid_count:(j + 1) * grid_count, :] = res[k * grid_count:(k + 1) * grid_count]
        return carry

    lax.fori_loop(0, chunks, one_chunk, 0)


def pair_stacks(order, bstart, dst, empties, full_weights, info, planes_feat, positions, with_info):
    pair_count, grid_count, channel_count = full_weights.shape
    planes = planes_feat.shape[0]
    blocks = planes_feat.shape[2] // LO
    rows = planes * grid_count + (INFO_ROWS if with_info else 0)
    grid_spec = pltpu.PrefetchScalarGridSpec(
        num_scalar_prefetch=4,
        grid=(blocks,),
        in_specs=[
            pl.BlockSpec(full_weights.shape, lambda b, *_: (0, 0, 0)),
            pl.BlockSpec((planes, channel_count, LO), lambda b, *_: (0, 0, b)),
        ],
        out_specs=pl.BlockSpec((positions, rows, LO), lambda b, *_: (0, 0, 0)),
        scratch_shapes=[pltpu.VMEM((CHUNK * grid_count, channel_count), full_weights.dtype)],
    )
    return pl.pallas_call(
        pair_kernel,
        grid_spec=grid_spec,
        out_shape=jax.ShapeDtypeStruct((positions, rows, LO), jnp.float32),
        compiler_params=pltpu.CompilerParams(vmem_limit_bytes=48 * 1024 * 1024),
    )(order, bstart, dst, empties, full_weights, planes_feat)


def gather_kernel(row_ref, x_ref, o_ref):
    c = pl.program_id(0)
    per = x_ref.shape[0]

    @pl.when(c == 0)
    def _():
        o_ref[...] = jnp.zeros(o_ref.shape, o_ref.dtype)

    for q in range(per):
        r = row_ref[c * per + q]

        @pl.when(r >= 0)
        def _():
            o_ref[r] += x_ref[q]


def slot_rows(received, owned, data_rows):
    onehot = received[:, data_rows, 32:32 + owned]
    return jnp.where(
        jnp.sum(onehot, axis=1) > 0.5,
        jnp.sum(onehot * jnp.arange(owned, dtype=jnp.float32)[None, :], axis=1),
        -1.0,
    ).astype(jnp.int32)


def gather_rows(received, row, owned):
    positions, rows, lanes = received.shape
    per = 8
    grid_spec = pltpu.PrefetchScalarGridSpec(
        num_scalar_prefetch=1,
        grid=(positions // per,),
        in_specs=[pl.BlockSpec((per, rows, lanes), lambda c, r: (c, 0, 0))],
        out_specs=pl.BlockSpec((owned, rows, lanes), lambda c, r: (0, 0, 0)),
    )
    return pl.pallas_call(
        gather_kernel,
        grid_spec=grid_spec,
        out_shape=jax.ShapeDtypeStruct((owned, rows, lanes), jnp.float32),
    )(row, received)


def owner_of(pair_tile, tile_order, owned_count):
    tile_count = tile_order.shape[0]
    match = tile_order[None, :] == pair_tile[:, None]
    pos = jnp.sum(jnp.where(match, jnp.arange(tile_count, dtype=jnp.int32)[None, :], 0), axis=1)
    return pos // owned_count, pos % owned_count


def slot_of(owner):
    n = owner.shape[-1]
    idx = jnp.arange(n, dtype=jnp.int32)
    earlier = idx[None, :] < idx[:, None]
    same = owner[..., :, None] == owner[..., None, :]
    return jnp.sum((same & earlier).astype(jnp.int32), axis=-1)


def local(traces, weights, pair_tile, pair_offset, tile_order):
    window_count = traces.shape[0]
    sample_count = traces.shape[2]
    blocks = sample_count // LO
    devices = lax.axis_size("tile")
    tile_count = tile_order.shape[0]
    owned_count = tile_count // devices
    positions = devices * SLOT

    hilbert = hilbert_build(sample_count)

    full_weights = lax.all_gather(weights, "tm", axis=1, tiled=True)
    pair_count, grid_count, _ = full_weights.shape
    wf = full_weights.astype(jnp.float32)
    energy = jnp.sum(wf * wf, axis=2)

    pidx = jnp.arange(pair_count, dtype=jnp.int32)
    pair_block = pair_offset // LO
    key = pair_block * pair_count + pidx
    rank = jnp.sum((key[None, :] < key[:, None]).astype(jnp.int32), axis=1)
    order = jnp.sum(jnp.where(rank[None, :] == pidx[:, None], pidx[None, :], 0), axis=1)
    bidx = jnp.arange(blocks + 1, dtype=jnp.int32)
    bstart = jnp.sum((pair_block[None, :] < bidx[:, None]).astype(jnp.int32), axis=1)
    owner, row = owner_of(pair_tile, tile_order, owned_count)
    dst = owner * SLOT + slot_of(owner)
    pos_idx = jnp.arange(positions, dtype=jnp.int32)
    unused = jnp.sum((dst[None, :] == pos_idx[:, None]).astype(jnp.int32), axis=1) == 0
    empty_rank = jnp.cumsum(unused.astype(jnp.int32)) - 1
    empty_count = positions - pair_count
    eidx = jnp.arange(empty_count, dtype=jnp.int32)
    empties = jnp.sum(
        jnp.where(unused[None, :] & (empty_rank[None, :] == eidx[:, None]), pos_idx[None, :], 0), axis=1
    )
    dst_sorted = jnp.sum(jnp.where(order[:, None] == pidx[None, :], dst[None, :], 0), axis=1)

    feature_max = jnp.maximum(jnp.max(jnp.abs(traces.astype(jnp.float32))), 1.0)
    bound = jnp.max(jnp.sum(jnp.abs(wf), axis=2), axis=1) * feature_max
    exponent = jnp.where(bound > 0, jnp.ceil(jnp.log2(jnp.maximum(bound, 1e-30))) - 14.0, 0.0)

    lanes = jnp.arange(LO, dtype=jnp.int32)[None, :]
    energy_lanes = jnp.pad(energy, ((0, 0), (0, LO - grid_count)))
    info_row = jnp.where(
        lanes < grid_count,
        energy_lanes,
        jnp.where(lanes - 32 == row[:, None], 1.0, jnp.where(lanes == 40, exponent[:, None], 0.0)),
    )
    pos_pair = jnp.sum(jnp.where(dst[None, :] == pos_idx[:, None], pidx[None, :] + 1, 0), axis=1) - 1
    info_pos = jnp.where((pos_pair >= 0)[:, None], info_row[jnp.maximum(pos_pair, 0)], 0.0)
    info_pos = jnp.concatenate(
        [info_pos[:, None, :], jnp.zeros((positions, INFO_ROWS - 1, LO), jnp.float32)], axis=1
    )
    info_recv = lax.all_to_all(info_pos.reshape(devices, SLOT, INFO_ROWS, LO), "tile", 0, 0, tiled=True)
    info_recv = info_recv.reshape(positions, INFO_ROWS, LO)
    row_of_slot = slot_rows(info_recv, owned_count, 0)
    recv_scale = jnp.exp2(info_recv[:, 0, 40])
    send_exp = jnp.where(pos_pair >= 0, exponent[jnp.maximum(pos_pair, 0)], 0.0)
    send_inv = jnp.exp2(-send_exp)

    planes_feat = jnp.concatenate([analytic(traces[w], hilbert) for w in range(window_count)], axis=0)
    slots = pair_stacks(
        order, bstart, dst_sorted, empties, full_weights, None, planes_feat, positions, False
    )
    rows = slots.shape[1]
    wire = (slots * send_inv[:, None, None]).astype(jnp.float16)
    received = lax.all_to_all(wire.reshape(devices, SLOT, rows, LO), "tile", 0, 0, tiled=True)
    received = received.reshape(positions, rows, LO).astype(jnp.float32) * recv_scale[:, None, None]
    stacked = gather_rows(received, row_of_slot, owned_count)

    data_rows = 3 * grid_count
    tile_energy = jnp.sum(
        jnp.where((row_of_slot[None, :] == jnp.arange(owned_count)[:, None])[:, :, None],
                  info_recv[None, :, 0, :grid_count], 0.0),
        axis=1,
    )
    energy_rows = tile_energy + ENERGY_EPS
    energy_b = energy_rows[:, :, None]
    out = []
    for w in range(window_count):
        row_stacks = stacked[:, w * data_rows:(w + 1) * data_rows].reshape(owned_count, 3, grid_count, LO)
        linear = row_stacks[:, 0]
        cosine_sum = row_stacks[:, 1]
        sine_sum = row_stacks[:, 2]
        out.append(
            linear * (cosine_sum * cosine_sum + sine_sum * sine_sum) / (energy_b * jnp.sqrt(energy_b))
        )
    return jnp.stack(out, axis=0)


def solution(mesh):
    return jax.shard_map(
        local,
        mesh=mesh,
        in_specs=(P("tm", "tile", None), P("tile", "tm", None), P("tile"), P("tile"), P()),
        out_specs=P("tm", "tile", None, None),
        check_vma=False,
    )
```

```python
import jax
import jax.numpy as jnp
from jax import lax
from jax.experimental import pallas as pl
from jax.experimental.pallas import tpu as pltpu
from jax.sharding import PartitionSpec as P

LO = 128
SLOT = 2

AMP_FLOOR = 0.5
ENERGY_EPS = 1e-06


def hilbert_build(length):
    row = jnp.arange(LO, dtype=jnp.int32)[:, None]
    col = jnp.arange(length, dtype=jnp.int32)[None, :]
    lag_index = (col - row) % length
    odd_lag = lag_index % 2 == 1
    phase_angle = jnp.pi * lag_index.astype(jnp.float32) / length
    safe_sine = jnp.where(odd_lag, jnp.sin(phase_angle), 1.0)
    kernel = jnp.where(odd_lag, 2.0 / length * jnp.cos(phase_angle) / safe_sine, 0.0)
    first = kernel.astype(jnp.bfloat16)
    return jnp.concatenate(
        [jnp.roll(first, LO * i, axis=1) for i in range(length // LO)], axis=0
    )


def analytic(window_traces, hilbert):
    quadrature = jnp.dot(window_traces, hilbert, preferred_element_type=jnp.float32)
    real_part = window_traces.astype(jnp.float32)
    amplitude = jnp.maximum(jnp.sqrt(real_part * real_part + quadrature * quadrature), AMP_FLOOR)
    cosine = (real_part / amplitude).astype(jnp.bfloat16)
    sine_part = (quadrature / amplitude).astype(jnp.bfloat16)
    return jnp.stack([window_traces, cosine, sine_part], axis=0)


CHUNK = 8
INFO_ROWS = 8


def pair_kernel(order_ref, bstart_ref, dst_ref, empty_ref, w_ref, *refs):
    f_refs, o_ref, wscr = refs[:-2], refs[-2], refs[-1]
    b = pl.program_id(0)
    per_window = f_refs[0].shape[0]
    planes = per_window * len(f_refs)
    grid_count = w_ref.shape[1]
    pair_count = w_ref.shape[0]
    data_rows = planes * grid_count

    @pl.when(b == 0)
    def _():
        def zero_one(e, carry):
            o_ref[empty_ref[e]] = jnp.zeros(o_ref.shape[1:], o_ref.dtype)
            return carry

        lax.fori_loop(0, empty_ref.shape[0], zero_one, 0)

    lo_idx = bstart_ref[b]
    hi_idx = bstart_ref[b + 1]
    chunks = (hi_idx - lo_idx + CHUNK - 1) // CHUNK

    def one_chunk(ch, carry):
        base = lo_idx + ch * CHUNK
        for k in range(CHUNK):
            p = order_ref[jnp.minimum(base + k, pair_count - 1)]
            wscr[k * grid_count:(k + 1) * grid_count, :] = w_ref[p]
        for j in range(planes):
            f_ref = f_refs[j // per_window]
            res = jnp.dot(wscr[...], f_ref[j % per_window], preferred_element_type=jnp.float32)
            for k in range(CHUNK):
                @pl.when(base + k < hi_idx)
                def _():
                    d = dst_ref[base + k]
                    o_ref[d, j * grid_count:(j + 1) * grid_count, :] = res[k * grid_count:(k + 1) * grid_count]
        return carry

    lax.fori_loop(0, chunks, one_chunk, 0)


def pair_stacks(order, bstart, dst, empties, full_weights, info, window_feats, positions, with_info):
    pair_count, grid_count, channel_count = full_weights.shape
    per_window = window_feats[0].shape[0]
    planes = per_window * len(window_feats)
    blocks = window_feats[0].shape[2] // LO
    rows = planes * grid_count + (INFO_ROWS if with_info else 0)
    grid_spec = pltpu.PrefetchScalarGridSpec(
        num_scalar_prefetch=4,
        grid=(blocks,),
        in_specs=[
            pl.BlockSpec(full_weights.shape, lambda b, *_: (0, 0, 0)),
        ] + [
            pl.BlockSpec((per_window, channel_count, LO), lambda b, *_: (0, 0, b)) for _ in window_feats
        ],
        out_specs=pl.BlockSpec((positions, rows, LO), lambda b, *_: (0, 0, 0)),
        scratch_shapes=[pltpu.VMEM((CHUNK * grid_count, channel_count), full_weights.dtype)],
    )
    return pl.pallas_call(
        pair_kernel,
        grid_spec=grid_spec,
        out_shape=jax.ShapeDtypeStruct((positions, rows, LO), jnp.float32),
        compiler_params=pltpu.CompilerParams(vmem_limit_bytes=48 * 1024 * 1024),
    )(order, bstart, dst, empties, full_weights, *window_feats)


def gather_kernel(row_ref, x_ref, o_ref):
    c = pl.program_id(0)
    per = x_ref.shape[0]

    @pl.when(c == 0)
    def _():
        o_ref[...] = jnp.zeros(o_ref.shape, o_ref.dtype)

    for q in range(per):
        r = row_ref[c * per + q]

        @pl.when(r >= 0)
        def _():
            o_ref[r] += x_ref[q]


def slot_rows(received, owned, data_rows):
    onehot = received[:, data_rows, 32:32 + owned]
    return jnp.where(
        jnp.sum(onehot, axis=1) > 0.5,
        jnp.sum(onehot * jnp.arange(owned, dtype=jnp.float32)[None, :], axis=1),
        -1.0,
    ).astype(jnp.int32)


def gather_rows(received, row, owned):
    positions, rows, lanes = received.shape
    per = 8
    grid_spec = pltpu.PrefetchScalarGridSpec(
        num_scalar_prefetch=1,
        grid=(positions // per,),
        in_specs=[pl.BlockSpec((per, rows, lanes), lambda c, r: (c, 0, 0))],
        out_specs=pl.BlockSpec((owned, rows, lanes), lambda c, r: (0, 0, 0)),
    )
    return pl.pallas_call(
        gather_kernel,
        grid_spec=grid_spec,
        out_shape=jax.ShapeDtypeStruct((owned, rows, lanes), jnp.float32),
    )(row, received)


def owner_of(pair_tile, tile_order, owned_count):
    tile_count = tile_order.shape[0]
    match = tile_order[None, :] == pair_tile[:, None]
    pos = jnp.sum(jnp.where(match, jnp.arange(tile_count, dtype=jnp.int32)[None, :], 0), axis=1)
    return pos // owned_count, pos % owned_count


def slot_of(owner):
    n = owner.shape[-1]
    idx = jnp.arange(n, dtype=jnp.int32)
    earlier = idx[None, :] < idx[:, None]
    same = owner[..., :, None] == owner[..., None, :]
    return jnp.sum((same & earlier).astype(jnp.int32), axis=-1)


def local(traces, weights, pair_tile, pair_offset, tile_order):
    window_count = traces.shape[0]
    sample_count = traces.shape[2]
    blocks = sample_count // LO
    devices = lax.axis_size("tile")
    tile_count = tile_order.shape[0]
    owned_count = tile_count // devices
    positions = devices * SLOT

    hilbert = hilbert_build(sample_count)

    full_weights = lax.all_gather(weights, "tm", axis=1, tiled=True)
    pair_count, grid_count, _ = full_weights.shape
    wf = full_weights.astype(jnp.float32)
    energy = jnp.sum(wf * wf, axis=2)

    pidx = jnp.arange(pair_count, dtype=jnp.int32)
    pair_block = pair_offset // LO
    key = pair_block * pair_count + pidx
    rank = jnp.sum((key[None, :] < key[:, None]).astype(jnp.int32), axis=1)
    order = jnp.sum(jnp.where(rank[None, :] == pidx[:, None], pidx[None, :], 0), axis=1)
    bidx = jnp.arange(blocks + 1, dtype=jnp.int32)
    bstart = jnp.sum((pair_block[None, :] < bidx[:, None]).astype(jnp.int32), axis=1)
    owner, row = owner_of(pair_tile, tile_order, owned_count)
    dst = owner * SLOT + slot_of(owner)
    pos_idx = jnp.arange(positions, dtype=jnp.int32)
    unused = jnp.sum((dst[None, :] == pos_idx[:, None]).astype(jnp.int32), axis=1) == 0
    empty_rank = jnp.cumsum(unused.astype(jnp.int32)) - 1
    empty_count = positions - pair_count
    eidx = jnp.arange(empty_count, dtype=jnp.int32)
    empties = jnp.sum(
        jnp.where(unused[None, :] & (empty_rank[None, :] == eidx[:, None]), pos_idx[None, :], 0), axis=1
    )
    dst_sorted = jnp.sum(jnp.where(order[:, None] == pidx[None, :], dst[None, :], 0), axis=1)

    feature_max = jnp.maximum(jnp.max(jnp.abs(traces.astype(jnp.float32))), 1.0)
    bound = jnp.max(jnp.sum(jnp.abs(wf), axis=2), axis=1) * feature_max
    exponent = jnp.where(bound > 0, jnp.ceil(jnp.log2(jnp.maximum(bound, 1e-30))) - 14.0, 0.0)

    lanes = jnp.arange(LO, dtype=jnp.int32)[None, :]
    energy_lanes = jnp.pad(energy, ((0, 0), (0, LO - grid_count)))
    info_row = jnp.where(
        lanes < grid_count,
        energy_lanes,
        jnp.where(lanes - 32 == row[:, None], 1.0, jnp.where(lanes == 40, exponent[:, None], 0.0)),
    )
    pos_pair = jnp.sum(jnp.where(dst[None, :] == pos_idx[:, None], pidx[None, :] + 1, 0), axis=1) - 1
    info_pos = jnp.where((pos_pair >= 0)[:, None], info_row[jnp.maximum(pos_pair, 0)], 0.0)
    info_pos = jnp.concatenate(
        [info_pos[:, None, :], jnp.zeros((positions, INFO_ROWS - 1, LO), jnp.float32)], axis=1
    )
    info_recv = lax.all_to_all(info_pos.reshape(devices, SLOT, INFO_ROWS, LO), "tile", 0, 0, tiled=True)
    info_recv = info_recv.reshape(positions, INFO_ROWS, LO)
    row_of_slot = slot_rows(info_recv, owned_count, 0)
    recv_scale = jnp.exp2(info_recv[:, 0, 40])
    send_exp = jnp.where(pos_pair >= 0, exponent[jnp.maximum(pos_pair, 0)], 0.0)
    send_inv = jnp.exp2(-send_exp)

    window_feats = [analytic(traces[w], hilbert) for w in range(window_count)]
    slots = pair_stacks(
        order, bstart, dst_sorted, empties, full_weights, None, window_feats, positions, False
    )
    rows = slots.shape[1]
    wire = (slots * send_inv[:, None, None]).astype(jnp.float16)
    received = lax.all_to_all(wire.reshape(devices, SLOT, rows, LO), "tile", 0, 0, tiled=True)
    received = received.reshape(positions, rows, LO).astype(jnp.float32) * recv_scale[:, None, None]
    stacked = gather_rows(received, row_of_slot, owned_count)

    data_rows = 3 * grid_count
    tile_energy = jnp.sum(
        jnp.where((row_of_slot[None, :] == jnp.arange(owned_count)[:, None])[:, :, None],
                  info_recv[None, :, 0, :grid_count], 0.0),
        axis=1,
    )
    energy_rows = tile_energy + ENERGY_EPS
    energy_b = energy_rows[:, :, None]
    out = []
    for w in range(window_count):
        row_stacks = stacked[:, w * data_rows:(w + 1) * data_rows].reshape(owned_count, 3, grid_count, LO)
        linear = row_stacks[:, 0]
        cosine_sum = row_stacks[:, 1]
        sine_sum = row_stacks[:, 2]
        out.append(
            linear * (cosine_sum * cosine_sum + sine_sum * sine_sum) / (energy_b * jnp.sqrt(energy_b))
        )
    return jnp.stack(out, axis=0)


def solution(mesh):
    return jax.shard_map(
        local,
        mesh=mesh,
        in_specs=(P("tm", "tile", None), P("tile", "tm", None), P("tile"), P("tile"), P()),
        out_specs=P("tm", "tile", None, None),
        check_vma=False,
    )
```

```python
import jax
import jax.numpy as jnp
from jax import lax
from jax.experimental import pallas as pl
from jax.experimental.pallas import tpu as pltpu
from jax.sharding import PartitionSpec as P

LO = 128
SLOT = 2

AMP_FLOOR = 0.5
ENERGY_EPS = 1e-06


def hilbert_build(length):
    row = jnp.arange(LO, dtype=jnp.int32)[:, None]
    col = jnp.arange(length, dtype=jnp.int32)[None, :]
    lag_index = (col - row) % length
    odd_lag = lag_index % 2 == 1
    phase_angle = jnp.pi * lag_index.astype(jnp.float32) / length
    safe_sine = jnp.where(odd_lag, jnp.sin(phase_angle), 1.0)
    kernel = jnp.where(odd_lag, 2.0 / length * jnp.cos(phase_angle) / safe_sine, 0.0)
    first = kernel.astype(jnp.bfloat16)
    return jnp.concatenate(
        [jnp.roll(first, LO * i, axis=1) for i in range(length // LO)], axis=0
    )


def analytic(window_traces, hilbert):
    quadrature = jnp.dot(window_traces, hilbert, preferred_element_type=jnp.float32)
    real_part = window_traces.astype(jnp.float32)
    amplitude = jnp.maximum(jnp.sqrt(real_part * real_part + quadrature * quadrature), AMP_FLOOR)
    cosine = (real_part / amplitude).astype(jnp.bfloat16)
    sine_part = (quadrature / amplitude).astype(jnp.bfloat16)
    return jnp.stack([window_traces, cosine, sine_part], axis=0)


CHUNK = 4
INFO_ROWS = 8


def pair_kernel(order_ref, bstart_ref, dst_ref, empty_ref, w_ref, *refs):
    f_refs, o_ref, wscr = refs[:-2], refs[-2], refs[-1]
    b = pl.program_id(0)
    per_window = f_refs[0].shape[0]
    planes = per_window * len(f_refs)
    grid_count = w_ref.shape[1]
    pair_count = w_ref.shape[0]
    data_rows = planes * grid_count

    @pl.when(b == 0)
    def _():
        def zero_one(e, carry):
            o_ref[empty_ref[e]] = jnp.zeros(o_ref.shape[1:], o_ref.dtype)
            return carry

        lax.fori_loop(0, empty_ref.shape[0], zero_one, 0)

    lo_idx = bstart_ref[b]
    hi_idx = bstart_ref[b + 1]
    chunks = (hi_idx - lo_idx + CHUNK - 1) // CHUNK

    def one_chunk(ch, carry):
        base = lo_idx + ch * CHUNK
        for k in range(CHUNK):
            p = order_ref[jnp.minimum(base + k, pair_count - 1)]
            wscr[k * grid_count:(k + 1) * grid_count, :] = w_ref[p]
        for j in range(planes):
            f_ref = f_refs[j // per_window]
            res = jnp.dot(wscr[...], f_ref[j % per_window], preferred_element_type=jnp.float32)
            for k in range(CHUNK):
                @pl.when(base + k < hi_idx)
                def _():
                    d = dst_ref[base + k]
                    o_ref[d, j * grid_count:(j + 1) * grid_count, :] = res[k * grid_count:(k + 1) * grid_count]
        return carry

    lax.fori_loop(0, chunks, one_chunk, 0)


def pair_stacks(order, bstart, dst, empties, full_weights, info, window_feats, positions, with_info):
    pair_count, grid_count, channel_count = full_weights.shape
    per_window = window_feats[0].shape[0]
    planes = per_window * len(window_feats)
    blocks = window_feats[0].shape[2] // LO
    rows = planes * grid_count + (INFO_ROWS if with_info else 0)
    grid_spec = pltpu.PrefetchScalarGridSpec(
        num_scalar_prefetch=4,
        grid=(blocks,),
        in_specs=[
            pl.BlockSpec(full_weights.shape, lambda b, *_: (0, 0, 0)),
        ] + [
            pl.BlockSpec((per_window, channel_count, LO), lambda b, *_: (0, 0, b)) for _ in window_feats
        ],
        out_specs=pl.BlockSpec((positions, rows, LO), lambda b, *_: (0, 0, 0)),
        scratch_shapes=[pltpu.VMEM((CHUNK * grid_count, channel_count), full_weights.dtype)],
    )
    return pl.pallas_call(
        pair_kernel,
        grid_spec=grid_spec,
        out_shape=jax.ShapeDtypeStruct((positions, rows, LO), jnp.float32),
        compiler_params=pltpu.CompilerParams(vmem_limit_bytes=48 * 1024 * 1024),
    )(order, bstart, dst, empties, full_weights, *window_feats)


def gather_kernel(row_ref, x_ref, o_ref):
    c = pl.program_id(0)
    per = x_ref.shape[0]

    @pl.when(c == 0)
    def _():
        o_ref[...] = jnp.zeros(o_ref.shape, o_ref.dtype)

    for q in range(per):
        r = row_ref[c * per + q]

        @pl.when(r >= 0)
        def _():
            o_ref[r] += x_ref[q]


def slot_rows(received, owned, data_rows):
    onehot = received[:, data_rows, 32:32 + owned]
    return jnp.where(
        jnp.sum(onehot, axis=1) > 0.5,
        jnp.sum(onehot * jnp.arange(owned, dtype=jnp.float32)[None, :], axis=1),
        -1.0,
    ).astype(jnp.int32)


def gather_rows(received, row, owned):
    positions, rows, lanes = received.shape
    per = 8
    grid_spec = pltpu.PrefetchScalarGridSpec(
        num_scalar_prefetch=1,
        grid=(positions // per,),
        in_specs=[pl.BlockSpec((per, rows, lanes), lambda c, r: (c, 0, 0))],
        out_specs=pl.BlockSpec((owned, rows, lanes), lambda c, r: (0, 0, 0)),
    )
    return pl.pallas_call(
        gather_kernel,
        grid_spec=grid_spec,
        out_shape=jax.ShapeDtypeStruct((owned, rows, lanes), jnp.float32),
    )(row, received)


def owner_of(pair_tile, tile_order, owned_count):
    tile_count = tile_order.shape[0]
    match = tile_order[None, :] == pair_tile[:, None]
    pos = jnp.sum(jnp.where(match, jnp.arange(tile_count, dtype=jnp.int32)[None, :], 0), axis=1)
    return pos // owned_count, pos % owned_count


def slot_of(owner):
    n = owner.shape[-1]
    idx = jnp.arange(n, dtype=jnp.int32)
    earlier = idx[None, :] < idx[:, None]
    same = owner[..., :, None] == owner[..., None, :]
    return jnp.sum((same & earlier).astype(jnp.int32), axis=-1)


def local(traces, weights, pair_tile, pair_offset, tile_order):
    window_count = traces.shape[0]
    sample_count = traces.shape[2]
    blocks = sample_count // LO
    devices = lax.axis_size("tile")
    tile_count = tile_order.shape[0]
    owned_count = tile_count // devices
    positions = devices * SLOT

    hilbert = hilbert_build(sample_count)

    full_weights = lax.all_gather(weights, "tm", axis=1, tiled=True)
    pair_count, grid_count, _ = full_weights.shape
    wf = full_weights.astype(jnp.float32)
    energy = jnp.sum(wf * wf, axis=2)

    pidx = jnp.arange(pair_count, dtype=jnp.int32)
    pair_block = pair_offset // LO
    key = pair_block * pair_count + pidx
    rank = jnp.sum((key[None, :] < key[:, None]).astype(jnp.int32), axis=1)
    order = jnp.sum(jnp.where(rank[None, :] == pidx[:, None], pidx[None, :], 0), axis=1)
    bidx = jnp.arange(blocks + 1, dtype=jnp.int32)
    bstart = jnp.sum((pair_block[None, :] < bidx[:, None]).astype(jnp.int32), axis=1)
    owner, row = owner_of(pair_tile, tile_order, owned_count)
    dst = owner * SLOT + slot_of(owner)
    pos_idx = jnp.arange(positions, dtype=jnp.int32)
    unused = jnp.sum((dst[None, :] == pos_idx[:, None]).astype(jnp.int32), axis=1) == 0
    empty_rank = jnp.cumsum(unused.astype(jnp.int32)) - 1
    empty_count = positions - pair_count
    eidx = jnp.arange(empty_count, dtype=jnp.int32)
    empties = jnp.sum(
        jnp.where(unused[None, :] & (empty_rank[None, :] == eidx[:, None]), pos_idx[None, :], 0), axis=1
    )
    dst_sorted = jnp.sum(jnp.where(order[:, None] == pidx[None, :], dst[None, :], 0), axis=1)

    feature_max = jnp.maximum(jnp.max(jnp.abs(traces.astype(jnp.float32))), 1.0)
    bound = jnp.max(jnp.sum(jnp.abs(wf), axis=2), axis=1) * feature_max
    exponent = jnp.where(bound > 0, jnp.ceil(jnp.log2(jnp.maximum(bound, 1e-30))) - 14.0, 0.0)

    lanes = jnp.arange(LO, dtype=jnp.int32)[None, :]
    energy_lanes = jnp.pad(energy, ((0, 0), (0, LO - grid_count)))
    info_row = jnp.where(
        lanes < grid_count,
        energy_lanes,
        jnp.where(lanes - 32 == row[:, None], 1.0, jnp.where(lanes == 40, exponent[:, None], 0.0)),
    )
    pos_pair = jnp.sum(jnp.where(dst[None, :] == pos_idx[:, None], pidx[None, :] + 1, 0), axis=1) - 1
    info_pos = jnp.where((pos_pair >= 0)[:, None], info_row[jnp.maximum(pos_pair, 0)], 0.0)
    info_pos = jnp.concatenate(
        [info_pos[:, None, :], jnp.zeros((positions, INFO_ROWS - 1, LO), jnp.float32)], axis=1
    )
    info_recv = lax.all_to_all(info_pos.reshape(devices, SLOT, INFO_ROWS, LO), "tile", 0, 0, tiled=True)
    info_recv = info_recv.reshape(positions, INFO_ROWS, LO)
    row_of_slot = slot_rows(info_recv, owned_count, 0)
    recv_scale = jnp.exp2(info_recv[:, 0, 40])
    send_exp = jnp.where(pos_pair >= 0, exponent[jnp.maximum(pos_pair, 0)], 0.0)
    send_inv = jnp.exp2(-send_exp)

    window_feats = [analytic(traces[w], hilbert) for w in range(window_count)]
    slots = pair_stacks(
        order, bstart, dst_sorted, empties, full_weights, None, window_feats, positions, False
    )
    rows = slots.shape[1]
    wire = (slots * send_inv[:, None, None]).astype(jnp.float16)
    received = lax.all_to_all(wire.reshape(devices, SLOT, rows, LO), "tile", 0, 0, tiled=True)
    received = received.reshape(positions, rows, LO).astype(jnp.float32) * recv_scale[:, None, None]
    stacked = gather_rows(received, row_of_slot, owned_count)

    data_rows = 3 * grid_count
    tile_energy = jnp.sum(
        jnp.where((row_of_slot[None, :] == jnp.arange(owned_count)[:, None])[:, :, None],
                  info_recv[None, :, 0, :grid_count], 0.0),
        axis=1,
    )
    energy_rows = tile_energy + ENERGY_EPS
    energy_b = energy_rows[:, :, None]
    out = []
    for w in range(window_count):
        row_stacks = stacked[:, w * data_rows:(w + 1) * data_rows].reshape(owned_count, 3, grid_count, LO)
        linear = row_stacks[:, 0]
        cosine_sum = row_stacks[:, 1]
        sine_sum = row_stacks[:, 2]
        out.append(
            linear * (cosine_sum * cosine_sum + sine_sum * sine_sum) / (energy_b * jnp.sqrt(energy_b))
        )
    return jnp.stack(out, axis=0)


def solution(mesh):
    return jax.shard_map(
        local,
        mesh=mesh,
        in_specs=(P("tm", "tile", None), P("tile", "tm", None), P("tile"), P("tile"), P()),
        out_specs=P("tm", "tile", None, None),
        check_vma=False,
    )
```

```python
import jax
import jax.numpy as jnp
from jax import lax
from jax.experimental import pallas as pl
from jax.experimental.pallas import tpu as pltpu
from jax.sharding import PartitionSpec as P

LO = 128
SLOT = 2

AMP_FLOOR = 0.5
ENERGY_EPS = 1e-06


def hilbert_build(length):
    row = jnp.arange(LO, dtype=jnp.int32)[:, None]
    col = jnp.arange(length, dtype=jnp.int32)[None, :]
    lag_index = (col - row) % length
    odd_lag = lag_index % 2 == 1
    phase_angle = jnp.pi * lag_index.astype(jnp.float32) / length
    safe_sine = jnp.where(odd_lag, jnp.sin(phase_angle), 1.0)
    kernel = jnp.where(odd_lag, 2.0 / length * jnp.cos(phase_angle) / safe_sine, 0.0)
    first = kernel.astype(jnp.bfloat16)
    return jnp.concatenate(
        [jnp.roll(first, LO * i, axis=1) for i in range(length // LO)], axis=0
    )


def analytic(window_traces, hilbert):
    channels, length = window_traces.shape
    blocks = length // LO
    quadrature = jnp.einsum(
        "cn,nbt->bct", window_traces, hilbert.reshape(length, blocks, LO),
        preferred_element_type=jnp.float32,
    )
    block_traces = jnp.transpose(window_traces.reshape(channels, blocks, LO), (1, 0, 2))
    real_part = block_traces.astype(jnp.float32)
    amplitude = jnp.maximum(jnp.sqrt(real_part * real_part + quadrature * quadrature), AMP_FLOOR)
    cosine = (real_part / amplitude).astype(jnp.bfloat16)
    sine_part = (quadrature / amplitude).astype(jnp.bfloat16)
    return jnp.stack([block_traces, cosine, sine_part], axis=1)


CHUNK = 8
INFO_ROWS = 8


def pair_kernel(order_ref, bstart_ref, dst_ref, empty_ref, w_ref, *refs):
    f_refs, o_ref, wscr = refs[:-2], refs[-2], refs[-1]
    b = pl.program_id(0)
    per_window = f_refs[0].shape[1]
    planes = per_window * len(f_refs)
    grid_count = w_ref.shape[1]
    pair_count = w_ref.shape[0]
    data_rows = planes * grid_count

    @pl.when(b == 0)
    def _():
        def zero_one(e, carry):
            o_ref[empty_ref[e]] = jnp.zeros(o_ref.shape[1:], o_ref.dtype)
            return carry

        lax.fori_loop(0, empty_ref.shape[0], zero_one, 0)

    lo_idx = bstart_ref[b]
    hi_idx = bstart_ref[b + 1]
    chunks = (hi_idx - lo_idx + CHUNK - 1) // CHUNK

    def one_chunk(ch, carry):
        base = lo_idx + ch * CHUNK
        for k in range(CHUNK):
            p = order_ref[jnp.minimum(base + k, pair_count - 1)]
            wscr[k * grid_count:(k + 1) * grid_count, :] = w_ref[p]
        for j in range(planes):
            f_ref = f_refs[j // per_window]
            res = jnp.dot(wscr[...], f_ref[0, j % per_window], preferred_element_type=jnp.float32)
            for k in range(CHUNK):
                @pl.when(base + k < hi_idx)
                def _():
                    d = dst_ref[base + k]
                    o_ref[d, j * grid_count:(j + 1) * grid_count, :] = res[k * grid_count:(k + 1) * grid_count]
        return carry

    lax.fori_loop(0, chunks, one_chunk, 0)


def pair_stacks(order, bstart, dst, empties, full_weights, info, window_feats, positions, with_info):
    pair_count, grid_count, channel_count = full_weights.shape
    blocks, per_window = window_feats[0].shape[:2]
    planes = per_window * len(window_feats)
    rows = planes * grid_count + (INFO_ROWS if with_info else 0)
    grid_spec = pltpu.PrefetchScalarGridSpec(
        num_scalar_prefetch=4,
        grid=(blocks,),
        in_specs=[
            pl.BlockSpec(full_weights.shape, lambda b, *_: (0, 0, 0)),
        ] + [
            pl.BlockSpec((1, per_window, channel_count, LO), lambda b, *_: (b, 0, 0, 0)) for _ in window_feats
        ],
        out_specs=pl.BlockSpec((positions, rows, LO), lambda b, *_: (0, 0, 0)),
        scratch_shapes=[pltpu.VMEM((CHUNK * grid_count, channel_count), full_weights.dtype)],
    )
    return pl.pallas_call(
        pair_kernel,
        grid_spec=grid_spec,
        out_shape=jax.ShapeDtypeStruct((positions, rows, LO), jnp.float32),
        compiler_params=pltpu.CompilerParams(vmem_limit_bytes=48 * 1024 * 1024),
    )(order, bstart, dst, empties, full_weights, *window_feats)


def gather_kernel(row_ref, x_ref, o_ref):
    c = pl.program_id(0)
    per = x_ref.shape[0]

    @pl.when(c == 0)
    def _():
        o_ref[...] = jnp.zeros(o_ref.shape, o_ref.dtype)

    for q in range(per):
        r = row_ref[c * per + q]

        @pl.when(r >= 0)
        def _():
            o_ref[r] += x_ref[q]


def slot_rows(received, owned, data_rows):
    onehot = received[:, data_rows, 32:32 + owned]
    return jnp.where(
        jnp.sum(onehot, axis=1) > 0.5,
        jnp.sum(onehot * jnp.arange(owned, dtype=jnp.float32)[None, :], axis=1),
        -1.0,
    ).astype(jnp.int32)


def gather_rows(received, row, owned):
    positions, rows, lanes = received.shape
    per = 8
    grid_spec = pltpu.PrefetchScalarGridSpec(
        num_scalar_prefetch=1,
        grid=(positions // per,),
        in_specs=[pl.BlockSpec((per, rows, lanes), lambda c, r: (c, 0, 0))],
        out_specs=pl.BlockSpec((owned, rows, lanes), lambda c, r: (0, 0, 0)),
    )
    return pl.pallas_call(
        gather_kernel,
        grid_spec=grid_spec,
        out_shape=jax.ShapeDtypeStruct((owned, rows, lanes), jnp.float32),
    )(row, received)


def owner_of(pair_tile, tile_order, owned_count):
    tile_count = tile_order.shape[0]
    match = tile_order[None, :] == pair_tile[:, None]
    pos = jnp.sum(jnp.where(match, jnp.arange(tile_count, dtype=jnp.int32)[None, :], 0), axis=1)
    return pos // owned_count, pos % owned_count


def slot_of(owner):
    n = owner.shape[-1]
    idx = jnp.arange(n, dtype=jnp.int32)
    earlier = idx[None, :] < idx[:, None]
    same = owner[..., :, None] == owner[..., None, :]
    return jnp.sum((same & earlier).astype(jnp.int32), axis=-1)


def local(traces, weights, pair_tile, pair_offset, tile_order):
    window_count = traces.shape[0]
    sample_count = traces.shape[2]
    blocks = sample_count // LO
    devices = lax.axis_size("tile")
    tile_count = tile_order.shape[0]
    owned_count = tile_count // devices
    positions = devices * SLOT

    hilbert = hilbert_build(sample_count)

    full_weights = lax.all_gather(weights, "tm", axis=1, tiled=True)
    pair_count, grid_count, _ = full_weights.shape
    wf = full_weights.astype(jnp.float32)
    energy = jnp.sum(wf * wf, axis=2)

    pidx = jnp.arange(pair_count, dtype=jnp.int32)
    pair_block = pair_offset // LO
    key = pair_block * pair_count + pidx
    rank = jnp.sum((key[None, :] < key[:, None]).astype(jnp.int32), axis=1)
    order = jnp.sum(jnp.where(rank[None, :] == pidx[:, None], pidx[None, :], 0), axis=1)
    bidx = jnp.arange(blocks + 1, dtype=jnp.int32)
    bstart = jnp.sum((pair_block[None, :] < bidx[:, None]).astype(jnp.int32), axis=1)
    owner, row = owner_of(pair_tile, tile_order, owned_count)
    dst = owner * SLOT + slot_of(owner)
    pos_idx = jnp.arange(positions, dtype=jnp.int32)
    unused = jnp.sum((dst[None, :] == pos_idx[:, None]).astype(jnp.int32), axis=1) == 0
    empty_rank = jnp.cumsum(unused.astype(jnp.int32)) - 1
    empty_count = positions - pair_count
    eidx = jnp.arange(empty_count, dtype=jnp.int32)
    empties = jnp.sum(
        jnp.where(unused[None, :] & (empty_rank[None, :] == eidx[:, None]), pos_idx[None, :], 0), axis=1
    )
    dst_sorted = jnp.sum(jnp.where(order[:, None] == pidx[None, :], dst[None, :], 0), axis=1)

    feature_max = jnp.maximum(jnp.max(jnp.abs(traces.astype(jnp.float32))), 1.0)
    bound = jnp.max(jnp.sum(jnp.abs(wf), axis=2), axis=1) * feature_max
    exponent = jnp.where(bound > 0, jnp.ceil(jnp.log2(jnp.maximum(bound, 1e-30))) - 14.0, 0.0)

    lanes = jnp.arange(LO, dtype=jnp.int32)[None, :]
    energy_lanes = jnp.pad(energy, ((0, 0), (0, LO - grid_count)))
    info_row = jnp.where(
        lanes < grid_count,
        energy_lanes,
        jnp.where(lanes - 32 == row[:, None], 1.0, jnp.where(lanes == 40, exponent[:, None], 0.0)),
    )
    pos_pair = jnp.sum(jnp.where(dst[None, :] == pos_idx[:, None], pidx[None, :] + 1, 0), axis=1) - 1
    info_pos = jnp.where((pos_pair >= 0)[:, None], info_row[jnp.maximum(pos_pair, 0)], 0.0)
    info_pos = jnp.concatenate(
        [info_pos[:, None, :], jnp.zeros((positions, INFO_ROWS - 1, LO), jnp.float32)], axis=1
    )
    info_recv = lax.all_to_all(info_pos.reshape(devices, SLOT, INFO_ROWS, LO), "tile", 0, 0, tiled=True)
    info_recv = info_recv.reshape(positions, INFO_ROWS, LO)
    row_of_slot = slot_rows(info_recv, owned_count, 0)
    recv_scale = jnp.exp2(info_recv[:, 0, 40])
    send_exp = jnp.where(pos_pair >= 0, exponent[jnp.maximum(pos_pair, 0)], 0.0)
    send_inv = jnp.exp2(-send_exp)

    window_feats = [analytic(traces[w], hilbert) for w in range(window_count)]
    slots = pair_stacks(
        order, bstart, dst_sorted, empties, full_weights, None, window_feats, positions, False
    )
    rows = slots.shape[1]
    wire = (slots * send_inv[:, None, None]).astype(jnp.float16)
    received = lax.all_to_all(wire.reshape(devices, SLOT, rows, LO), "tile", 0, 0, tiled=True)
    received = received.reshape(positions, rows, LO).astype(jnp.float32) * recv_scale[:, None, None]
    stacked = gather_rows(received, row_of_slot, owned_count)

    data_rows = 3 * grid_count
    tile_energy = jnp.sum(
        jnp.where((row_of_slot[None, :] == jnp.arange(owned_count)[:, None])[:, :, None],
                  info_recv[None, :, 0, :grid_count], 0.0),
        axis=1,
    )
    energy_rows = tile_energy + ENERGY_EPS
    energy_b = energy_rows[:, :, None]
    out = []
    for w in range(window_count):
        row_stacks = stacked[:, w * data_rows:(w + 1) * data_rows].reshape(owned_count, 3, grid_count, LO)
        linear = row_stacks[:, 0]
        cosine_sum = row_stacks[:, 1]
        sine_sum = row_stacks[:, 2]
        out.append(
            linear * (cosine_sum * cosine_sum + sine_sum * sine_sum) / (energy_b * jnp.sqrt(energy_b))
        )
    return jnp.stack(out, axis=0)


def solution(mesh):
    return jax.shard_map(
        local,
        mesh=mesh,
        in_specs=(P("tm", "tile", None), P("tile", "tm", None), P("tile"), P("tile"), P()),
        out_specs=P("tm", "tile", None, None),
        check_vma=False,
    )
```

```python
import jax
import jax.numpy as jnp
from jax import lax
from jax.experimental import pallas as pl
from jax.experimental.pallas import tpu as pltpu
from jax.sharding import PartitionSpec as P

LO = 128
SLOT = 2

AMP_FLOOR = 0.5
ENERGY_EPS = 1e-06


def hilbert_build(length):
    row = jnp.arange(LO, dtype=jnp.int32)[:, None]
    col = jnp.arange(length, dtype=jnp.int32)[None, :]
    lag_index = (col - row) % length
    odd_lag = lag_index % 2 == 1
    phase_angle = jnp.pi * lag_index.astype(jnp.float32) / length
    safe_sine = jnp.where(odd_lag, jnp.sin(phase_angle), 1.0)
    kernel = jnp.where(odd_lag, 2.0 / length * jnp.cos(phase_angle) / safe_sine, 0.0)
    first = kernel.astype(jnp.bfloat16)
    return jnp.concatenate(
        [jnp.roll(first, LO * i, axis=1) for i in range(length // LO)], axis=0
    )


def analytic(window_traces, hilbert):
    quadrature = jnp.dot(window_traces, hilbert, preferred_element_type=jnp.float32)
    real_part = window_traces.astype(jnp.float32)
    amplitude = jnp.maximum(jnp.sqrt(real_part * real_part + quadrature * quadrature), AMP_FLOOR)
    cosine = (real_part / amplitude).astype(jnp.bfloat16)
    sine_part = (quadrature / amplitude).astype(jnp.bfloat16)
    return jnp.stack([window_traces, cosine, sine_part], axis=0)


CHUNK = 8
INFO_ROWS = 8


def pair_kernel(order_ref, bstart_ref, dst_ref, empty_ref, w_ref, *refs):
    f_refs, o_ref, wscr = refs[:-2], refs[-2], refs[-1]
    b = pl.program_id(0)
    per_window = f_refs[0].shape[0]
    planes = per_window * len(f_refs)
    grid_count = w_ref.shape[1]
    pair_count = w_ref.shape[0]
    data_rows = planes * grid_count

    @pl.when(b == 0)
    def _():
        def zero_one(e, carry):
            o_ref[empty_ref[e]] = jnp.zeros(o_ref.shape[1:], o_ref.dtype)
            return carry

        lax.fori_loop(0, empty_ref.shape[0], zero_one, 0)

    lo_idx = bstart_ref[b]
    hi_idx = bstart_ref[b + 1]
    chunks = (hi_idx - lo_idx + CHUNK - 1) // CHUNK

    def one_chunk(ch, carry):
        base = lo_idx + ch * CHUNK
        for k in range(CHUNK):
            p = order_ref[jnp.minimum(base + k, pair_count - 1)]
            wscr[k * grid_count:(k + 1) * grid_count, :] = w_ref[p]
        for jj in range(planes // 2):
            rhs = jnp.concatenate(
                [f_refs[j // per_window][j % per_window] for j in (2 * jj, 2 * jj + 1)], axis=1
            )
            res = jnp.dot(wscr[...], rhs, preferred_element_type=jnp.float32)
            for k in range(CHUNK):
                @pl.when(base + k < hi_idx)
                def _():
                    d = dst_ref[base + k]
                    for h in range(2):
                        j = 2 * jj + h
                        o_ref[d, j * grid_count:(j + 1) * grid_count, :] = (
                            res[k * grid_count:(k + 1) * grid_count, h * LO:(h + 1) * LO]
                        )
        return carry

    lax.fori_loop(0, chunks, one_chunk, 0)


def pair_stacks(order, bstart, dst, empties, full_weights, info, window_feats, positions, with_info):
    pair_count, grid_count, channel_count = full_weights.shape
    per_window = window_feats[0].shape[0]
    planes = per_window * len(window_feats)
    blocks = window_feats[0].shape[2] // LO
    rows = planes * grid_count + (INFO_ROWS if with_info else 0)
    grid_spec = pltpu.PrefetchScalarGridSpec(
        num_scalar_prefetch=4,
        grid=(blocks,),
        in_specs=[
            pl.BlockSpec(full_weights.shape, lambda b, *_: (0, 0, 0)),
        ] + [
            pl.BlockSpec((per_window, channel_count, LO), lambda b, *_: (0, 0, b)) for _ in window_feats
        ],
        out_specs=pl.BlockSpec((positions, rows, LO), lambda b, *_: (0, 0, 0)),
        scratch_shapes=[pltpu.VMEM((CHUNK * grid_count, channel_count), full_weights.dtype)],
    )
    return pl.pallas_call(
        pair_kernel,
        grid_spec=grid_spec,
        out_shape=jax.ShapeDtypeStruct((positions, rows, LO), jnp.float32),
        compiler_params=pltpu.CompilerParams(vmem_limit_bytes=48 * 1024 * 1024),
    )(order, bstart, dst, empties, full_weights, *window_feats)


def gather_kernel(row_ref, x_ref, o_ref):
    c = pl.program_id(0)
    per = x_ref.shape[0]

    @pl.when(c == 0)
    def _():
        o_ref[...] = jnp.zeros(o_ref.shape, o_ref.dtype)

    for q in range(per):
        r = row_ref[c * per + q]

        @pl.when(r >= 0)
        def _():
            o_ref[r] += x_ref[q]


def slot_rows(received, owned, data_rows):
    onehot = received[:, data_rows, 32:32 + owned]
    return jnp.where(
        jnp.sum(onehot, axis=1) > 0.5,
        jnp.sum(onehot * jnp.arange(owned, dtype=jnp.float32)[None, :], axis=1),
        -1.0,
    ).astype(jnp.int32)


def gather_rows(received, row, owned):
    positions, rows, lanes = received.shape
    per = 8
    grid_spec = pltpu.PrefetchScalarGridSpec(
        num_scalar_prefetch=1,
        grid=(positions // per,),
        in_specs=[pl.BlockSpec((per, rows, lanes), lambda c, r: (c, 0, 0))],
        out_specs=pl.BlockSpec((owned, rows, lanes), lambda c, r: (0, 0, 0)),
    )
    return pl.pallas_call(
        gather_kernel,
        grid_spec=grid_spec,
        out_shape=jax.ShapeDtypeStruct((owned, rows, lanes), jnp.float32),
    )(row, received)


def owner_of(pair_tile, tile_order, owned_count):
    tile_count = tile_order.shape[0]
    match = tile_order[None, :] == pair_tile[:, None]
    pos = jnp.sum(jnp.where(match, jnp.arange(tile_count, dtype=jnp.int32)[None, :], 0), axis=1)
    return pos // owned_count, pos % owned_count


def slot_of(owner):
    n = owner.shape[-1]
    idx = jnp.arange(n, dtype=jnp.int32)
    earlier = idx[None, :] < idx[:, None]
    same = owner[..., :, None] == owner[..., None, :]
    return jnp.sum((same & earlier).astype(jnp.int32), axis=-1)


def local(traces, weights, pair_tile, pair_offset, tile_order):
    window_count = traces.shape[0]
    sample_count = traces.shape[2]
    blocks = sample_count // LO
    devices = lax.axis_size("tile")
    tile_count = tile_order.shape[0]
    owned_count = tile_count // devices
    positions = devices * SLOT

    hilbert = hilbert_build(sample_count)

    full_weights = lax.all_gather(weights, "tm", axis=1, tiled=True)
    pair_count, grid_count, _ = full_weights.shape
    wf = full_weights.astype(jnp.float32)
    energy = jnp.sum(wf * wf, axis=2)

    pidx = jnp.arange(pair_count, dtype=jnp.int32)
    pair_block = pair_offset // LO
    key = pair_block * pair_count + pidx
    rank = jnp.sum((key[None, :] < key[:, None]).astype(jnp.int32), axis=1)
    order = jnp.sum(jnp.where(rank[None, :] == pidx[:, None], pidx[None, :], 0), axis=1)
    bidx = jnp.arange(blocks + 1, dtype=jnp.int32)
    bstart = jnp.sum((pair_block[None, :] < bidx[:, None]).astype(jnp.int32), axis=1)
    owner, row = owner_of(pair_tile, tile_order, owned_count)
    dst = owner * SLOT + slot_of(owner)
    pos_idx = jnp.arange(positions, dtype=jnp.int32)
    unused = jnp.sum((dst[None, :] == pos_idx[:, None]).astype(jnp.int32), axis=1) == 0
    empty_rank = jnp.cumsum(unused.astype(jnp.int32)) - 1
    empty_count = positions - pair_count
    eidx = jnp.arange(empty_count, dtype=jnp.int32)
    empties = jnp.sum(
        jnp.where(unused[None, :] & (empty_rank[None, :] == eidx[:, None]), pos_idx[None, :], 0), axis=1
    )
    dst_sorted = jnp.sum(jnp.where(order[:, None] == pidx[None, :], dst[None, :], 0), axis=1)

    feature_max = jnp.maximum(jnp.max(jnp.abs(traces.astype(jnp.float32))), 1.0)
    bound = jnp.max(jnp.sum(jnp.abs(wf), axis=2), axis=1) * feature_max
    exponent = jnp.where(bound > 0, jnp.ceil(jnp.log2(jnp.maximum(bound, 1e-30))) - 14.0, 0.0)

    lanes = jnp.arange(LO, dtype=jnp.int32)[None, :]
    energy_lanes = jnp.pad(energy, ((0, 0), (0, LO - grid_count)))
    info_row = jnp.where(
        lanes < grid_count,
        energy_lanes,
        jnp.where(lanes - 32 == row[:, None], 1.0, jnp.where(lanes == 40, exponent[:, None], 0.0)),
    )
    pos_pair = jnp.sum(jnp.where(dst[None, :] == pos_idx[:, None], pidx[None, :] + 1, 0), axis=1) - 1
    info_pos = jnp.where((pos_pair >= 0)[:, None], info_row[jnp.maximum(pos_pair, 0)], 0.0)
    info_pos = jnp.concatenate(
        [info_pos[:, None, :], jnp.zeros((positions, INFO_ROWS - 1, LO), jnp.float32)], axis=1
    )
    info_recv = lax.all_to_all(info_pos.reshape(devices, SLOT, INFO_ROWS, LO), "tile", 0, 0, tiled=True)
    info_recv = info_recv.reshape(positions, INFO_ROWS, LO)
    row_of_slot = slot_rows(info_recv, owned_count, 0)
    recv_scale = jnp.exp2(info_recv[:, 0, 40])
    send_exp = jnp.where(pos_pair >= 0, exponent[jnp.maximum(pos_pair, 0)], 0.0)
    send_inv = jnp.exp2(-send_exp)

    window_feats = [analytic(traces[w], hilbert) for w in range(window_count)]
    slots = pair_stacks(
        order, bstart, dst_sorted, empties, full_weights, None, window_feats, positions, False
    )
    rows = slots.shape[1]
    wire = (slots * send_inv[:, None, None]).astype(jnp.float16)
    received = lax.all_to_all(wire.reshape(devices, SLOT, rows, LO), "tile", 0, 0, tiled=True)
    received = received.reshape(positions, rows, LO).astype(jnp.float32) * recv_scale[:, None, None]
    stacked = gather_rows(received, row_of_slot, owned_count)

    data_rows = 3 * grid_count
    tile_energy = jnp.sum(
        jnp.where((row_of_slot[None, :] == jnp.arange(owned_count)[:, None])[:, :, None],
                  info_recv[None, :, 0, :grid_count], 0.0),
        axis=1,
    )
    energy_rows = tile_energy + ENERGY_EPS
    energy_b = energy_rows[:, :, None]
    out = []
    for w in range(window_count):
        row_stacks = stacked[:, w * data_rows:(w + 1) * data_rows].reshape(owned_count, 3, grid_count, LO)
        linear = row_stacks[:, 0]
        cosine_sum = row_stacks[:, 1]
        sine_sum = row_stacks[:, 2]
        out.append(
            linear * (cosine_sum * cosine_sum + sine_sum * sine_sum) / (energy_b * jnp.sqrt(energy_b))
        )
    return jnp.stack(out, axis=0)


def solution(mesh):
    return jax.shard_map(
        local,
        mesh=mesh,
        in_specs=(P("tm", "tile", None), P("tile", "tm", None), P("tile"), P("tile"), P()),
        out_specs=P("tm", "tile", None, None),
        check_vma=False,
    )
```

```python
import jax
import jax.numpy as jnp
from jax import lax
from jax.experimental import pallas as pl
from jax.experimental.pallas import tpu as pltpu
from jax.sharding import PartitionSpec as P

LO = 128
SLOT = 2

AMP_FLOOR = 0.5
ENERGY_EPS = 1e-06


def hilbert_build(length):
    row = jnp.arange(LO, dtype=jnp.int32)[:, None]
    col = jnp.arange(length, dtype=jnp.int32)[None, :]
    lag_index = (col - row) % length
    odd_lag = lag_index % 2 == 1
    phase_angle = jnp.pi * lag_index.astype(jnp.float32) / length
    safe_sine = jnp.where(odd_lag, jnp.sin(phase_angle), 1.0)
    kernel = jnp.where(odd_lag, 2.0 / length * jnp.cos(phase_angle) / safe_sine, 0.0)
    first = kernel.astype(jnp.bfloat16)
    return jnp.concatenate(
        [jnp.roll(first, LO * i, axis=1) for i in range(length // LO)], axis=0
    )


def analytic(window_traces, hilbert):
    quadrature = jnp.dot(window_traces, hilbert, preferred_element_type=jnp.float32)
    real_part = window_traces.astype(jnp.float32)
    amplitude = jnp.maximum(jnp.sqrt(real_part * real_part + quadrature * quadrature), AMP_FLOOR)
    cosine = (real_part / amplitude).astype(jnp.bfloat16)
    sine_part = (quadrature / amplitude).astype(jnp.bfloat16)
    return jnp.stack([window_traces, cosine, sine_part], axis=0)


CHUNK = 8
INFO_ROWS = 8


def pair_kernel(order_ref, bstart_ref, dst_ref, empty_ref, w_ref, *refs):
    f_refs, o_ref, wscr = refs[:-2], refs[-2], refs[-1]
    b = pl.program_id(0)
    per_window = f_refs[0].shape[0]
    planes = per_window * len(f_refs)
    grid_count = w_ref.shape[1]
    pair_count = w_ref.shape[0]
    data_rows = planes * grid_count

    @pl.when(b == 0)
    def _():
        def zero_one(e, carry):
            o_ref[empty_ref[e]] = jnp.zeros(o_ref.shape[1:], o_ref.dtype)
            return carry

        lax.fori_loop(0, empty_ref.shape[0], zero_one, 0)

    lo_idx = bstart_ref[b]
    hi_idx = bstart_ref[b + 1]
    chunks = (hi_idx - lo_idx + CHUNK - 1) // CHUNK

    def one_chunk(ch, carry):
        base = lo_idx + ch * CHUNK
        for k in range(CHUNK):
            p = order_ref[jnp.minimum(base + k, pair_count - 1)]
            wscr[k * grid_count:(k + 1) * grid_count, :] = w_ref[p]
        rhs = jnp.concatenate(
            [f_refs[j // per_window][j % per_window] for j in range(planes)], axis=1
        )
        res = jnp.dot(wscr[...], rhs, preferred_element_type=jnp.float32)
        for k in range(CHUNK):
            @pl.when(base + k < hi_idx)
            def _():
                d = dst_ref[base + k]
                for j in range(planes):
                    o_ref[d, j * grid_count:(j + 1) * grid_count, :] = (
                        res[k * grid_count:(k + 1) * grid_count, j * LO:(j + 1) * LO]
                    )
        return carry

    lax.fori_loop(0, chunks, one_chunk, 0)


def pair_stacks(order, bstart, dst, empties, full_weights, info, window_feats, positions, with_info):
    pair_count, grid_count, channel_count = full_weights.shape
    per_window = window_feats[0].shape[0]
    planes = per_window * len(window_feats)
    blocks = window_feats[0].shape[2] // LO
    rows = planes * grid_count + (INFO_ROWS if with_info else 0)
    grid_spec = pltpu.PrefetchScalarGridSpec(
        num_scalar_prefetch=4,
        grid=(blocks,),
        in_specs=[
            pl.BlockSpec(full_weights.shape, lambda b, *_: (0, 0, 0)),
        ] + [
            pl.BlockSpec((per_window, channel_count, LO), lambda b, *_: (0, 0, b)) for _ in window_feats
        ],
        out_specs=pl.BlockSpec((positions, rows, LO), lambda b, *_: (0, 0, 0)),
        scratch_shapes=[pltpu.VMEM((CHUNK * grid_count, channel_count), full_weights.dtype)],
    )
    return pl.pallas_call(
        pair_kernel,
        grid_spec=grid_spec,
        out_shape=jax.ShapeDtypeStruct((positions, rows, LO), jnp.float32),
        compiler_params=pltpu.CompilerParams(vmem_limit_bytes=48 * 1024 * 1024),
    )(order, bstart, dst, empties, full_weights, *window_feats)


def gather_kernel(row_ref, x_ref, o_ref):
    c = pl.program_id(0)
    per = x_ref.shape[0]

    @pl.when(c == 0)
    def _():
        o_ref[...] = jnp.zeros(o_ref.shape, o_ref.dtype)

    for q in range(per):
        r = row_ref[c * per + q]

        @pl.when(r >= 0)
        def _():
            o_ref[r] += x_ref[q]


def slot_rows(received, owned, data_rows):
    onehot = received[:, data_rows, 32:32 + owned]
    return jnp.where(
        jnp.sum(onehot, axis=1) > 0.5,
        jnp.sum(onehot * jnp.arange(owned, dtype=jnp.float32)[None, :], axis=1),
        -1.0,
    ).astype(jnp.int32)


def gather_rows(received, row, owned):
    positions, rows, lanes = received.shape
    per = 8
    grid_spec = pltpu.PrefetchScalarGridSpec(
        num_scalar_prefetch=1,
        grid=(positions // per,),
        in_specs=[pl.BlockSpec((per, rows, lanes), lambda c, r: (c, 0, 0))],
        out_specs=pl.BlockSpec((owned, rows, lanes), lambda c, r: (0, 0, 0)),
    )
    return pl.pallas_call(
        gather_kernel,
        grid_spec=grid_spec,
        out_shape=jax.ShapeDtypeStruct((owned, rows, lanes), jnp.float32),
    )(row, received)


def owner_of(pair_tile, tile_order, owned_count):
    tile_count = tile_order.shape[0]
    match = tile_order[None, :] == pair_tile[:, None]
    pos = jnp.sum(jnp.where(match, jnp.arange(tile_count, dtype=jnp.int32)[None, :], 0), axis=1)
    return pos // owned_count, pos % owned_count


def slot_of(owner):
    n = owner.shape[-1]
    idx = jnp.arange(n, dtype=jnp.int32)
    earlier = idx[None, :] < idx[:, None]
    same = owner[..., :, None] == owner[..., None, :]
    return jnp.sum((same & earlier).astype(jnp.int32), axis=-1)


def local(traces, weights, pair_tile, pair_offset, tile_order):
    window_count = traces.shape[0]
    sample_count = traces.shape[2]
    blocks = sample_count // LO
    devices = lax.axis_size("tile")
    tile_count = tile_order.shape[0]
    owned_count = tile_count // devices
    positions = devices * SLOT

    hilbert = hilbert_build(sample_count)

    full_weights = lax.all_gather(weights, "tm", axis=1, tiled=True)
    pair_count, grid_count, _ = full_weights.shape
    wf = full_weights.astype(jnp.float32)
    energy = jnp.sum(wf * wf, axis=2)

    pidx = jnp.arange(pair_count, dtype=jnp.int32)
    pair_block = pair_offset // LO
    key = pair_block * pair_count + pidx
    rank = jnp.sum((key[None, :] < key[:, None]).astype(jnp.int32), axis=1)
    order = jnp.sum(jnp.where(rank[None, :] == pidx[:, None], pidx[None, :], 0), axis=1)
    bidx = jnp.arange(blocks + 1, dtype=jnp.int32)
    bstart = jnp.sum((pair_block[None, :] < bidx[:, None]).astype(jnp.int32), axis=1)
    owner, row = owner_of(pair_tile, tile_order, owned_count)
    dst = owner * SLOT + slot_of(owner)
    pos_idx = jnp.arange(positions, dtype=jnp.int32)
    unused = jnp.sum((dst[None, :] == pos_idx[:, None]).astype(jnp.int32), axis=1) == 0
    empty_rank = jnp.cumsum(unused.astype(jnp.int32)) - 1
    empty_count = positions - pair_count
    eidx = jnp.arange(empty_count, dtype=jnp.int32)
    empties = jnp.sum(
        jnp.where(unused[None, :] & (empty_rank[None, :] == eidx[:, None]), pos_idx[None, :], 0), axis=1
    )
    dst_sorted = jnp.sum(jnp.where(order[:, None] == pidx[None, :], dst[None, :], 0), axis=1)

    feature_max = jnp.maximum(jnp.max(jnp.abs(traces.astype(jnp.float32))), 1.0)
    bound = jnp.max(jnp.sum(jnp.abs(wf), axis=2), axis=1) * feature_max
    exponent = jnp.where(bound > 0, jnp.ceil(jnp.log2(jnp.maximum(bound, 1e-30))) - 14.0, 0.0)

    lanes = jnp.arange(LO, dtype=jnp.int32)[None, :]
    energy_lanes = jnp.pad(energy, ((0, 0), (0, LO - grid_count)))
    info_row = jnp.where(
        lanes < grid_count,
        energy_lanes,
        jnp.where(lanes - 32 == row[:, None], 1.0, jnp.where(lanes == 40, exponent[:, None], 0.0)),
    )
    pos_pair = jnp.sum(jnp.where(dst[None, :] == pos_idx[:, None], pidx[None, :] + 1, 0), axis=1) - 1
    info_pos = jnp.where((pos_pair >= 0)[:, None], info_row[jnp.maximum(pos_pair, 0)], 0.0)
    info_pos = jnp.concatenate(
        [info_pos[:, None, :], jnp.zeros((positions, INFO_ROWS - 1, LO), jnp.float32)], axis=1
    )
    info_recv = lax.all_to_all(info_pos.reshape(devices, SLOT, INFO_ROWS, LO), "tile", 0, 0, tiled=True)
    info_recv = info_recv.reshape(positions, INFO_ROWS, LO)
    row_of_slot = slot_rows(info_recv, owned_count, 0)
    recv_scale = jnp.exp2(info_recv[:, 0, 40])
    send_exp = jnp.where(pos_pair >= 0, exponent[jnp.maximum(pos_pair, 0)], 0.0)
    send_inv = jnp.exp2(-send_exp)

    window_feats = [analytic(traces[w], hilbert) for w in range(window_count)]
    slots = pair_stacks(
        order, bstart, dst_sorted, empties, full_weights, None, window_feats, positions, False
    )
    rows = slots.shape[1]
    wire = (slots * send_inv[:, None, None]).astype(jnp.float16)
    received = lax.all_to_all(wire.reshape(devices, SLOT, rows, LO), "tile", 0, 0, tiled=True)
    received = received.reshape(positions, rows, LO).astype(jnp.float32) * recv_scale[:, None, None]
    stacked = gather_rows(received, row_of_slot, owned_count)

    data_rows = 3 * grid_count
    tile_energy = jnp.sum(
        jnp.where((row_of_slot[None, :] == jnp.arange(owned_count)[:, None])[:, :, None],
                  info_recv[None, :, 0, :grid_count], 0.0),
        axis=1,
    )
    energy_rows = tile_energy + ENERGY_EPS
    energy_b = energy_rows[:, :, None]
    out = []
    for w in range(window_count):
        row_stacks = stacked[:, w * data_rows:(w + 1) * data_rows].reshape(owned_count, 3, grid_count, LO)
        linear = row_stacks[:, 0]
        cosine_sum = row_stacks[:, 1]
        sine_sum = row_stacks[:, 2]
        out.append(
            linear * (cosine_sum * cosine_sum + sine_sum * sine_sum) / (energy_b * jnp.sqrt(energy_b))
        )
    return jnp.stack(out, axis=0)


def solution(mesh):
    return jax.shard_map(
        local,
        mesh=mesh,
        in_specs=(P("tm", "tile", None), P("tile", "tm", None), P("tile"), P("tile"), P()),
        out_specs=P("tm", "tile", None, None),
        check_vma=False,
    )
```

```python
import jax
import jax.numpy as jnp
from jax import lax
from jax.experimental import pallas as pl
from jax.experimental.pallas import tpu as pltpu
from jax.sharding import PartitionSpec as P

LO = 128
SLOT = 2

AMP_FLOOR = 0.5
ENERGY_EPS = 1e-06


def hilbert_build(length):
    row = jnp.arange(LO, dtype=jnp.int32)[:, None]
    col = jnp.arange(length, dtype=jnp.int32)[None, :]
    lag_index = (col - row) % length
    odd_lag = lag_index % 2 == 1
    phase_angle = jnp.pi * lag_index.astype(jnp.float32) / length
    safe_sine = jnp.where(odd_lag, jnp.sin(phase_angle), 1.0)
    kernel = jnp.where(odd_lag, 2.0 / length * jnp.cos(phase_angle) / safe_sine, 0.0)
    first = kernel.astype(jnp.bfloat16)
    return jnp.concatenate(
        [jnp.roll(first, LO * i, axis=1) for i in range(length // LO)], axis=0
    )


def analytic(window_traces, hilbert):
    quadrature = jnp.dot(window_traces, hilbert, preferred_element_type=jnp.float32)
    real_part = window_traces.astype(jnp.float32)
    amplitude = jnp.maximum(jnp.sqrt(real_part * real_part + quadrature * quadrature), AMP_FLOOR)
    cosine = (real_part / amplitude).astype(jnp.bfloat16)
    sine_part = (quadrature / amplitude).astype(jnp.bfloat16)
    return jnp.stack([window_traces, cosine, sine_part], axis=0)


def exact_pow2(k):
    mag = jnp.abs(k).astype(jnp.int32)
    up = jnp.ones_like(k)
    down = jnp.ones_like(k)
    for bit in range(7):
        on = (mag >> bit) % 2 == 1
        up = up * jnp.where(on, 2.0 ** (2 ** bit), 1.0)
        down = down * jnp.where(on, 2.0 ** -(2 ** bit), 1.0)
    return jnp.where(k >= 0, up, down)


CHUNK = 8
INFO_ROWS = 8
WIRE_INFO_ROWS = 16


def pair_kernel(order_ref, bstart_ref, dst_ref, empty_ref, w_ref, *refs):
    f_refs, o_ref, wscr = refs[:-2], refs[-2], refs[-1]
    b = pl.program_id(0)
    per_window = f_refs[0].shape[0]
    planes = per_window * len(f_refs)
    grid_count = w_ref.shape[1]
    pair_count = w_ref.shape[0]
    data_rows = planes * grid_count

    @pl.when(b == 0)
    def _():
        def zero_one(e, carry):
            o_ref[empty_ref[e]] = jnp.zeros(o_ref.shape[1:], o_ref.dtype)
            return carry

        lax.fori_loop(0, empty_ref.shape[0], zero_one, 0)

    lo_idx = bstart_ref[b]
    hi_idx = bstart_ref[b + 1]
    chunks = (hi_idx - lo_idx + CHUNK - 1) // CHUNK

    def one_chunk(ch, carry):
        base = lo_idx + ch * CHUNK
        for k in range(CHUNK):
            p = order_ref[jnp.minimum(base + k, pair_count - 1)]
            wscr[k * grid_count:(k + 1) * grid_count, :] = w_ref[p]
        rhs = jnp.concatenate(
            [f_refs[j // per_window][j % per_window] for j in range(planes)], axis=1
        )
        res = jnp.dot(wscr[...], rhs, preferred_element_type=jnp.float32)
        for k in range(CHUNK):
            @pl.when(base + k < hi_idx)
            def _():
                d = dst_ref[base + k]
                for j in range(planes):
                    o_ref[d, j * grid_count:(j + 1) * grid_count, :] = (
                        res[k * grid_count:(k + 1) * grid_count, j * LO:(j + 1) * LO]
                    )
        return carry

    lax.fori_loop(0, chunks, one_chunk, 0)


def pair_stacks(order, bstart, dst, empties, full_weights, info, window_feats, positions, with_info):
    pair_count, grid_count, channel_count = full_weights.shape
    per_window = window_feats[0].shape[0]
    planes = per_window * len(window_feats)
    blocks = window_feats[0].shape[2] // LO
    rows = planes * grid_count + (INFO_ROWS if with_info else 0)
    grid_spec = pltpu.PrefetchScalarGridSpec(
        num_scalar_prefetch=4,
        grid=(blocks,),
        in_specs=[
            pl.BlockSpec(full_weights.shape, lambda b, *_: (0, 0, 0)),
        ] + [
            pl.BlockSpec((per_window, channel_count, LO), lambda b, *_: (0, 0, b)) for _ in window_feats
        ],
        out_specs=pl.BlockSpec((positions, rows, LO), lambda b, *_: (0, 0, 0)),
        scratch_shapes=[pltpu.VMEM((CHUNK * grid_count, channel_count), full_weights.dtype)],
    )
    return pl.pallas_call(
        pair_kernel,
        grid_spec=grid_spec,
        out_shape=jax.ShapeDtypeStruct((positions, rows, LO), jnp.float32),
        compiler_params=pltpu.CompilerParams(vmem_limit_bytes=48 * 1024 * 1024),
    )(order, bstart, dst, empties, full_weights, *window_feats)


def gather_kernel(row_ref, x_ref, o_ref):
    c = pl.program_id(0)
    per = x_ref.shape[0]

    @pl.when(c == 0)
    def _():
        o_ref[...] = jnp.zeros(o_ref.shape, o_ref.dtype)

    for q in range(per):
        r = row_ref[c * per + q]

        @pl.when(r >= 0)
        def _():
            o_ref[r] += x_ref[q]


def slot_rows(received, owned, data_rows):
    onehot = received[:, data_rows, 32:32 + owned]
    return jnp.where(
        jnp.sum(onehot, axis=1) > 0.5,
        jnp.sum(onehot * jnp.arange(owned, dtype=jnp.float32)[None, :], axis=1),
        -1.0,
    ).astype(jnp.int32)


def gather_rows(received, row, owned):
    positions, rows, lanes = received.shape
    per = 8
    grid_spec = pltpu.PrefetchScalarGridSpec(
        num_scalar_prefetch=1,
        grid=(positions // per,),
        in_specs=[pl.BlockSpec((per, rows, lanes), lambda c, r: (c, 0, 0))],
        out_specs=pl.BlockSpec((owned, rows, lanes), lambda c, r: (0, 0, 0)),
    )
    return pl.pallas_call(
        gather_kernel,
        grid_spec=grid_spec,
        out_shape=jax.ShapeDtypeStruct((owned, rows, lanes), jnp.float32),
    )(row, received)


def owner_of(pair_tile, tile_order, owned_count):
    tile_count = tile_order.shape[0]
    match = tile_order[None, :] == pair_tile[:, None]
    pos = jnp.sum(jnp.where(match, jnp.arange(tile_count, dtype=jnp.int32)[None, :], 0), axis=1)
    return pos // owned_count, pos % owned_count


def slot_of(owner):
    n = owner.shape[-1]
    idx = jnp.arange(n, dtype=jnp.int32)
    earlier = idx[None, :] < idx[:, None]
    same = owner[..., :, None] == owner[..., None, :]
    return jnp.sum((same & earlier).astype(jnp.int32), axis=-1)


def local(traces, weights, pair_tile, pair_offset, tile_order):
    window_count = traces.shape[0]
    sample_count = traces.shape[2]
    blocks = sample_count // LO
    devices = lax.axis_size("tile")
    tile_count = tile_order.shape[0]
    owned_count = tile_count // devices
    positions = devices * SLOT

    hilbert = hilbert_build(sample_count)

    full_weights = lax.all_gather(weights, "tm", axis=1, tiled=True)
    pair_count, grid_count, _ = full_weights.shape
    wf = full_weights.astype(jnp.float32)
    energy = jnp.sum(wf * wf, axis=2)

    pidx = jnp.arange(pair_count, dtype=jnp.int32)
    pair_block = pair_offset // LO
    key = pair_block * pair_count + pidx
    rank = jnp.sum((key[None, :] < key[:, None]).astype(jnp.int32), axis=1)
    order = jnp.sum(jnp.where(rank[None, :] == pidx[:, None], pidx[None, :], 0), axis=1)
    bidx = jnp.arange(blocks + 1, dtype=jnp.int32)
    bstart = jnp.sum((pair_block[None, :] < bidx[:, None]).astype(jnp.int32), axis=1)
    owner, row = owner_of(pair_tile, tile_order, owned_count)
    dst = owner * SLOT + slot_of(owner)
    pos_idx = jnp.arange(positions, dtype=jnp.int32)
    unused = jnp.sum((dst[None, :] == pos_idx[:, None]).astype(jnp.int32), axis=1) == 0
    empty_rank = jnp.cumsum(unused.astype(jnp.int32)) - 1
    empty_count = positions - pair_count
    eidx = jnp.arange(empty_count, dtype=jnp.int32)
    empties = jnp.sum(
        jnp.where(unused[None, :] & (empty_rank[None, :] == eidx[:, None]), pos_idx[None, :], 0), axis=1
    )
    dst_sorted = jnp.sum(jnp.where(order[:, None] == pidx[None, :], dst[None, :], 0), axis=1)

    feature_max = jnp.maximum(jnp.max(jnp.abs(traces.astype(jnp.float32))), 1.0)
    bound = jnp.max(jnp.sum(jnp.abs(wf), axis=2), axis=1) * feature_max
    exponent = jnp.where(bound > 0, jnp.ceil(jnp.log2(jnp.maximum(bound, 1e-30))) - 14.0, 0.0)

    exponent = jnp.clip(exponent, -100.0, 100.0)
    energy_max = jnp.max(energy, axis=1)
    energy_exp = jnp.where(
        energy_max > 0, jnp.ceil(jnp.log2(jnp.maximum(energy_max, 1e-30))) - 13.0, 0.0
    )
    energy_exp = jnp.clip(energy_exp, -100.0, 100.0)
    energy_scaled = energy * exact_pow2(-energy_exp)[:, None]
    energy_hi = energy_scaled.astype(jnp.float16).astype(jnp.float32)
    energy_mid = energy_scaled - energy_hi

    lanes = jnp.arange(LO, dtype=jnp.int32)[None, :]
    pad = ((0, 0), (0, LO - grid_count))
    info0 = jnp.where(
        lanes < grid_count,
        jnp.pad(energy_hi, pad),
        jnp.where(
            lanes - 32 == row[:, None],
            1.0,
            jnp.where(lanes == 40, exponent[:, None], jnp.where(lanes == 41, energy_exp[:, None], 0.0)),
        ),
    )
    info1 = jnp.pad(energy_mid, pad)
    pos_pair = jnp.sum(jnp.where(dst[None, :] == pos_idx[:, None], pidx[None, :] + 1, 0), axis=1) - 1
    filled = (pos_pair >= 0)[:, None]
    safe_pair = jnp.maximum(pos_pair, 0)
    info_pos = jnp.stack(
        [jnp.where(filled, info0[safe_pair], 0.0), jnp.where(filled, info1[safe_pair], 0.0)], axis=1
    )
    info_pos = jnp.concatenate(
        [info_pos, jnp.zeros((positions, WIRE_INFO_ROWS - 2, LO), jnp.float32)], axis=1
    ).astype(jnp.float16)
    send_exp = jnp.where(pos_pair >= 0, exponent[safe_pair], 0.0)
    send_inv = exact_pow2(-send_exp)

    window_feats = [analytic(traces[w], hilbert) for w in range(window_count)]
    slots = pair_stacks(
        order, bstart, dst_sorted, empties, full_weights, None, window_feats, positions, False
    )
    rows = slots.shape[1]
    wire = jnp.concatenate([(slots * send_inv[:, None, None]).astype(jnp.float16), info_pos], axis=1)
    wire_rows = wire.shape[1]
    received = lax.all_to_all(wire.reshape(devices, SLOT, wire_rows, LO), "tile", 0, 0, tiled=True)
    received = received.reshape(positions, wire_rows, LO)
    info_recv = received[:, rows:rows + 2].astype(jnp.float32)
    row_of_slot = slot_rows(info_recv, owned_count, 0)
    recv_scale = exact_pow2(info_recv[:, 0, 40])
    recv_energy = (info_recv[:, 0, :grid_count] + info_recv[:, 1, :grid_count]) * exact_pow2(
        info_recv[:, 0, 41]
    )[:, None]
    decoded = received[:, :rows].astype(jnp.float32) * recv_scale[:, None, None]
    stacked = gather_rows(decoded, row_of_slot, owned_count)

    data_rows = 3 * grid_count
    tile_energy = jnp.sum(
        jnp.where((row_of_slot[None, :] == jnp.arange(owned_count)[:, None])[:, :, None],
                  recv_energy[None, :, :], 0.0),
        axis=1,
    )
    energy_rows = tile_energy + ENERGY_EPS
    energy_b = energy_rows[:, :, None]
    out = []
    for w in range(window_count):
        row_stacks = stacked[:, w * data_rows:(w + 1) * data_rows].reshape(owned_count, 3, grid_count, LO)
        linear = row_stacks[:, 0]
        cosine_sum = row_stacks[:, 1]
        sine_sum = row_stacks[:, 2]
        out.append(
            linear * (cosine_sum * cosine_sum + sine_sum * sine_sum) / (energy_b * jnp.sqrt(energy_b))
        )
    return jnp.stack(out, axis=0)


def solution(mesh):
    return jax.shard_map(
        local,
        mesh=mesh,
        in_specs=(P("tm", "tile", None), P("tile", "tm", None), P("tile"), P("tile"), P()),
        out_specs=P("tm", "tile", None, None),
        check_vma=False,
    )
```

```python
import jax
import jax.numpy as jnp
from jax import lax
from jax.experimental import pallas as pl
from jax.experimental.pallas import tpu as pltpu
from jax.sharding import PartitionSpec as P

LO = 128
SLOT = 2

AMP_FLOOR = 0.5
ENERGY_EPS = 1e-06


def hilbert_build(length):
    row = jnp.arange(LO, dtype=jnp.int32)[:, None]
    col = jnp.arange(length, dtype=jnp.int32)[None, :]
    lag_index = (col - row) % length
    odd_lag = lag_index % 2 == 1
    phase_angle = jnp.pi * lag_index.astype(jnp.float32) / length
    safe_sine = jnp.where(odd_lag, jnp.sin(phase_angle), 1.0)
    kernel = jnp.where(odd_lag, 2.0 / length * jnp.cos(phase_angle) / safe_sine, 0.0)
    first = kernel.astype(jnp.bfloat16)
    return jnp.concatenate(
        [jnp.roll(first, LO * i, axis=1) for i in range(length // LO)], axis=0
    )


def analytic(window_traces, hilbert):
    quadrature = jnp.dot(window_traces, hilbert, preferred_element_type=jnp.float32)
    real_part = window_traces.astype(jnp.float32)
    amplitude = jnp.maximum(jnp.sqrt(real_part * real_part + quadrature * quadrature), AMP_FLOOR)
    cosine = (real_part / amplitude).astype(jnp.bfloat16)
    sine_part = (quadrature / amplitude).astype(jnp.bfloat16)
    return jnp.stack([window_traces, cosine, sine_part], axis=0)


CHUNK = 4
INFO_ROWS = 8


def pair_kernel(order_ref, bstart_ref, dst_ref, empty_ref, w_ref, *refs):
    f_refs, o_ref, wscr = refs[:-2], refs[-2], refs[-1]
    b = pl.program_id(0)
    per_window = f_refs[0].shape[0]
    planes = per_window * len(f_refs)
    grid_count = w_ref.shape[1]
    pair_count = w_ref.shape[0]
    data_rows = planes * grid_count

    @pl.when(b == 0)
    def _():
        def zero_one(e, carry):
            o_ref[empty_ref[e]] = jnp.zeros(o_ref.shape[1:], o_ref.dtype)
            return carry

        lax.fori_loop(0, empty_ref.shape[0], zero_one, 0)

    lo_idx = bstart_ref[b]
    hi_idx = bstart_ref[b + 1]
    chunks = (hi_idx - lo_idx + CHUNK - 1) // CHUNK

    def one_chunk(ch, carry):
        base = lo_idx + ch * CHUNK
        for k in range(CHUNK):
            p = order_ref[jnp.minimum(base + k, pair_count - 1)]
            wscr[k * grid_count:(k + 1) * grid_count, :] = w_ref[p]
        rhs = jnp.concatenate(
            [f_refs[j // per_window][j % per_window] for j in range(planes)], axis=1
        )
        res = jnp.dot(wscr[...], rhs, preferred_element_type=jnp.float32)
        for k in range(CHUNK):
            @pl.when(base + k < hi_idx)
            def _():
                d = dst_ref[base + k]
                for j in range(planes):
                    o_ref[d, j * grid_count:(j + 1) * grid_count, :] = (
                        res[k * grid_count:(k + 1) * grid_count, j * LO:(j + 1) * LO]
                    )
        return carry

    lax.fori_loop(0, chunks, one_chunk, 0)


def pair_stacks(order, bstart, dst, empties, full_weights, info, window_feats, positions, with_info):
    pair_count, grid_count, channel_count = full_weights.shape
    per_window = window_feats[0].shape[0]
    planes = per_window * len(window_feats)
    blocks = window_feats[0].shape[2] // LO
    rows = planes * grid_count + (INFO_ROWS if with_info else 0)
    grid_spec = pltpu.PrefetchScalarGridSpec(
        num_scalar_prefetch=4,
        grid=(blocks,),
        in_specs=[
            pl.BlockSpec(full_weights.shape, lambda b, *_: (0, 0, 0)),
        ] + [
            pl.BlockSpec((per_window, channel_count, LO), lambda b, *_: (0, 0, b)) for _ in window_feats
        ],
        out_specs=pl.BlockSpec((positions, rows, LO), lambda b, *_: (0, 0, 0)),
        scratch_shapes=[pltpu.VMEM((CHUNK * grid_count, channel_count), full_weights.dtype)],
    )
    return pl.pallas_call(
        pair_kernel,
        grid_spec=grid_spec,
        out_shape=jax.ShapeDtypeStruct((positions, rows, LO), jnp.float32),
        compiler_params=pltpu.CompilerParams(vmem_limit_bytes=48 * 1024 * 1024),
    )(order, bstart, dst, empties, full_weights, *window_feats)


def gather_kernel(row_ref, x_ref, o_ref):
    c = pl.program_id(0)
    per = x_ref.shape[0]

    @pl.when(c == 0)
    def _():
        o_ref[...] = jnp.zeros(o_ref.shape, o_ref.dtype)

    for q in range(per):
        r = row_ref[c * per + q]

        @pl.when(r >= 0)
        def _():
            o_ref[r] += x_ref[q]


def slot_rows(received, owned, data_rows):
    onehot = received[:, data_rows, 32:32 + owned]
    return jnp.where(
        jnp.sum(onehot, axis=1) > 0.5,
        jnp.sum(onehot * jnp.arange(owned, dtype=jnp.float32)[None, :], axis=1),
        -1.0,
    ).astype(jnp.int32)


def gather_rows(received, row, owned):
    positions, rows, lanes = received.shape
    per = 8
    grid_spec = pltpu.PrefetchScalarGridSpec(
        num_scalar_prefetch=1,
        grid=(positions // per,),
        in_specs=[pl.BlockSpec((per, rows, lanes), lambda c, r: (c, 0, 0))],
        out_specs=pl.BlockSpec((owned, rows, lanes), lambda c, r: (0, 0, 0)),
    )
    return pl.pallas_call(
        gather_kernel,
        grid_spec=grid_spec,
        out_shape=jax.ShapeDtypeStruct((owned, rows, lanes), jnp.float32),
    )(row, received)


def owner_of(pair_tile, tile_order, owned_count):
    tile_count = tile_order.shape[0]
    match = tile_order[None, :] == pair_tile[:, None]
    pos = jnp.sum(jnp.where(match, jnp.arange(tile_count, dtype=jnp.int32)[None, :], 0), axis=1)
    return pos // owned_count, pos % owned_count


def slot_of(owner):
    n = owner.shape[-1]
    idx = jnp.arange(n, dtype=jnp.int32)
    earlier = idx[None, :] < idx[:, None]
    same = owner[..., :, None] == owner[..., None, :]
    return jnp.sum((same & earlier).astype(jnp.int32), axis=-1)


def local(traces, weights, pair_tile, pair_offset, tile_order):
    window_count = traces.shape[0]
    sample_count = traces.shape[2]
    blocks = sample_count // LO
    devices = lax.axis_size("tile")
    tile_count = tile_order.shape[0]
    owned_count = tile_count // devices
    positions = devices * SLOT

    hilbert = hilbert_build(sample_count)

    full_weights = lax.all_gather(weights, "tm", axis=1, tiled=True)
    pair_count, grid_count, _ = full_weights.shape
    wf = full_weights.astype(jnp.float32)
    energy = jnp.sum(wf * wf, axis=2)

    pidx = jnp.arange(pair_count, dtype=jnp.int32)
    pair_block = pair_offset // LO
    key = pair_block * pair_count + pidx
    rank = jnp.sum((key[None, :] < key[:, None]).astype(jnp.int32), axis=1)
    order = jnp.sum(jnp.where(rank[None, :] == pidx[:, None], pidx[None, :], 0), axis=1)
    bidx = jnp.arange(blocks + 1, dtype=jnp.int32)
    bstart = jnp.sum((pair_block[None, :] < bidx[:, None]).astype(jnp.int32), axis=1)
    owner, row = owner_of(pair_tile, tile_order, owned_count)
    dst = owner * SLOT + slot_of(owner)
    pos_idx = jnp.arange(positions, dtype=jnp.int32)
    unused = jnp.sum((dst[None, :] == pos_idx[:, None]).astype(jnp.int32), axis=1) == 0
    empty_rank = jnp.cumsum(unused.astype(jnp.int32)) - 1
    empty_count = positions - pair_count
    eidx = jnp.arange(empty_count, dtype=jnp.int32)
    empties = jnp.sum(
        jnp.where(unused[None, :] & (empty_rank[None, :] == eidx[:, None]), pos_idx[None, :], 0), axis=1
    )
    dst_sorted = jnp.sum(jnp.where(order[:, None] == pidx[None, :], dst[None, :], 0), axis=1)

    feature_max = jnp.maximum(jnp.max(jnp.abs(traces.astype(jnp.float32))), 1.0)
    bound = jnp.max(jnp.sum(jnp.abs(wf), axis=2), axis=1) * feature_max
    exponent = jnp.where(bound > 0, jnp.ceil(jnp.log2(jnp.maximum(bound, 1e-30))) - 14.0, 0.0)

    lanes = jnp.arange(LO, dtype=jnp.int32)[None, :]
    energy_lanes = jnp.pad(energy, ((0, 0), (0, LO - grid_count)))
    info_row = jnp.where(
        lanes < grid_count,
        energy_lanes,
        jnp.where(lanes - 32 == row[:, None], 1.0, jnp.where(lanes == 40, exponent[:, None], 0.0)),
    )
    pos_pair = jnp.sum(jnp.where(dst[None, :] == pos_idx[:, None], pidx[None, :] + 1, 0), axis=1) - 1
    info_pos = jnp.where((pos_pair >= 0)[:, None], info_row[jnp.maximum(pos_pair, 0)], 0.0)
    info_pos = jnp.concatenate(
        [info_pos[:, None, :], jnp.zeros((positions, INFO_ROWS - 1, LO), jnp.float32)], axis=1
    )
    info_recv = lax.all_to_all(info_pos.reshape(devices, SLOT, INFO_ROWS, LO), "tile", 0, 0, tiled=True)
    info_recv = info_recv.reshape(positions, INFO_ROWS, LO)
    row_of_slot = slot_rows(info_recv, owned_count, 0)
    recv_scale = jnp.exp2(info_recv[:, 0, 40])
    send_exp = jnp.where(pos_pair >= 0, exponent[jnp.maximum(pos_pair, 0)], 0.0)
    send_inv = jnp.exp2(-send_exp)

    window_feats = [analytic(traces[w], hilbert) for w in range(window_count)]
    slots = pair_stacks(
        order, bstart, dst_sorted, empties, full_weights, None, window_feats, positions, False
    )
    rows = slots.shape[1]
    wire = (slots * send_inv[:, None, None]).astype(jnp.float16)
    received = lax.all_to_all(wire.reshape(devices, SLOT, rows, LO), "tile", 0, 0, tiled=True)
    received = received.reshape(positions, rows, LO).astype(jnp.float32) * recv_scale[:, None, None]
    stacked = gather_rows(received, row_of_slot, owned_count)

    data_rows = 3 * grid_count
    tile_energy = jnp.sum(
        jnp.where((row_of_slot[None, :] == jnp.arange(owned_count)[:, None])[:, :, None],
                  info_recv[None, :, 0, :grid_count], 0.0),
        axis=1,
    )
    energy_rows = tile_energy + ENERGY_EPS
    energy_b = energy_rows[:, :, None]
    out = []
    for w in range(window_count):
        row_stacks = stacked[:, w * data_rows:(w + 1) * data_rows].reshape(owned_count, 3, grid_count, LO)
        linear = row_stacks[:, 0]
        cosine_sum = row_stacks[:, 1]
        sine_sum = row_stacks[:, 2]
        out.append(
            linear * (cosine_sum * cosine_sum + sine_sum * sine_sum) / (energy_b * jnp.sqrt(energy_b))
        )
    return jnp.stack(out, axis=0)


def solution(mesh):
    return jax.shard_map(
        local,
        mesh=mesh,
        in_specs=(P("tm", "tile", None), P("tile", "tm", None), P("tile"), P("tile"), P()),
        out_specs=P("tm", "tile", None, None),
        check_vma=False,
    )
```

```python
import jax
import jax.numpy as jnp
from jax import lax
from jax.experimental import pallas as pl
from jax.experimental.pallas import tpu as pltpu
from jax.sharding import PartitionSpec as P

LO = 128
SLOT = 2

AMP_FLOOR = 0.5
ENERGY_EPS = 1e-06


def hilbert_build(length):
    row = jnp.arange(LO, dtype=jnp.int32)[:, None]
    col = jnp.arange(length, dtype=jnp.int32)[None, :]
    lag_index = (col - row) % length
    odd_lag = lag_index % 2 == 1
    phase_angle = jnp.pi * lag_index.astype(jnp.float32) / length
    safe_sine = jnp.where(odd_lag, jnp.sin(phase_angle), 1.0)
    kernel = jnp.where(odd_lag, 2.0 / length * jnp.cos(phase_angle) / safe_sine, 0.0)
    first = kernel.astype(jnp.bfloat16)
    return jnp.concatenate(
        [jnp.roll(first, LO * i, axis=1) for i in range(length // LO)], axis=0
    )


def analytic(window_traces, hilbert):
    quadrature = jnp.dot(window_traces, hilbert, preferred_element_type=jnp.float32)
    real_part = window_traces.astype(jnp.float32)
    amplitude = jnp.maximum(jnp.sqrt(real_part * real_part + quadrature * quadrature), AMP_FLOOR)
    cosine = (real_part / amplitude).astype(jnp.bfloat16)
    sine_part = (quadrature / amplitude).astype(jnp.bfloat16)
    return jnp.stack([window_traces, cosine, sine_part], axis=0)


CHUNK = 8
INFO_ROWS = 8


def pair_kernel(order_ref, bstart_ref, dst_ref, empty_ref, w_ref, *refs):
    f_refs, o_ref, wscr = refs[:-2], refs[-2], refs[-1]
    b = pl.program_id(0)
    per_window = f_refs[0].shape[0]
    planes = per_window * len(f_refs)
    grid_count = w_ref.shape[1]
    pair_count = w_ref.shape[0]
    data_rows = planes * grid_count

    @pl.when(b == 0)
    def _():
        def zero_one(e, carry):
            o_ref[empty_ref[e]] = jnp.zeros(o_ref.shape[1:], o_ref.dtype)
            return carry

        lax.fori_loop(0, empty_ref.shape[0], zero_one, 0)

    lo_idx = bstart_ref[b]
    hi_idx = bstart_ref[b + 1]
    chunks = (hi_idx - lo_idx + CHUNK - 1) // CHUNK

    def one_chunk(ch, carry):
        base = lo_idx + ch * CHUNK
        for k in range(CHUNK):
            p = order_ref[jnp.minimum(base + k, pair_count - 1)]
            wscr[k * grid_count:(k + 1) * grid_count, :] = w_ref[p]
        rhs = jnp.concatenate(
            [f_refs[j // per_window][j % per_window] for j in range(planes)], axis=1
        )
        res = jnp.dot(wscr[...], rhs, preferred_element_type=jnp.float32)
        for k in range(CHUNK):
            @pl.when(base + k < hi_idx)
            def _():
                d = dst_ref[base + k]
                for j in range(planes):
                    o_ref[d, j * grid_count:(j + 1) * grid_count, :] = (
                        res[k * grid_count:(k + 1) * grid_count, j * LO:(j + 1) * LO]
                    )
        return carry

    lax.fori_loop(0, chunks, one_chunk, 0)


def pair_stacks(order, bstart, dst, empties, full_weights, info, window_feats, positions, with_info):
    pair_count, grid_count, channel_count = full_weights.shape
    per_window = window_feats[0].shape[0]
    planes = per_window * len(window_feats)
    blocks = window_feats[0].shape[2] // LO
    rows = planes * grid_count + (INFO_ROWS if with_info else 0)
    grid_spec = pltpu.PrefetchScalarGridSpec(
        num_scalar_prefetch=4,
        grid=(blocks,),
        in_specs=[
            pl.BlockSpec(full_weights.shape, lambda b, *_: (0, 0, 0)),
        ] + [
            pl.BlockSpec((per_window, channel_count, LO), lambda b, *_: (0, 0, b)) for _ in window_feats
        ],
        out_specs=pl.BlockSpec((positions, rows, LO), lambda b, *_: (0, 0, 0)),
        scratch_shapes=[pltpu.VMEM((CHUNK * grid_count, channel_count), full_weights.dtype)],
    )
    return pl.pallas_call(
        pair_kernel,
        grid_spec=grid_spec,
        out_shape=jax.ShapeDtypeStruct((positions, rows, LO), jnp.float32),
        compiler_params=pltpu.CompilerParams(vmem_limit_bytes=48 * 1024 * 1024),
    )(order, bstart, dst, empties, full_weights, *window_feats)


def gather_kernel(row_ref, x_ref, o_ref):
    c = pl.program_id(0)
    per = x_ref.shape[0]

    @pl.when(c == 0)
    def _():
        o_ref[...] = jnp.zeros(o_ref.shape, o_ref.dtype)

    for q in range(per):
        r = row_ref[c * per + q]

        @pl.when(r >= 0)
        def _():
            o_ref[r] += x_ref[q]


def slot_rows(received, owned, data_rows):
    onehot = received[:, data_rows, 32:32 + owned]
    return jnp.where(
        jnp.sum(onehot, axis=1) > 0.5,
        jnp.sum(onehot * jnp.arange(owned, dtype=jnp.float32)[None, :], axis=1),
        -1.0,
    ).astype(jnp.int32)


def gather_rows(received, row, owned):
    positions, rows, lanes = received.shape
    per = 16
    grid_spec = pltpu.PrefetchScalarGridSpec(
        num_scalar_prefetch=1,
        grid=(positions // per,),
        in_specs=[pl.BlockSpec((per, rows, lanes), lambda c, r: (c, 0, 0))],
        out_specs=pl.BlockSpec((owned, rows, lanes), lambda c, r: (0, 0, 0)),
    )
    return pl.pallas_call(
        gather_kernel,
        grid_spec=grid_spec,
        out_shape=jax.ShapeDtypeStruct((owned, rows, lanes), jnp.float32),
    )(row, received)


def owner_of(pair_tile, tile_order, owned_count):
    tile_count = tile_order.shape[0]
    match = tile_order[None, :] == pair_tile[:, None]
    pos = jnp.sum(jnp.where(match, jnp.arange(tile_count, dtype=jnp.int32)[None, :], 0), axis=1)
    return pos // owned_count, pos % owned_count


def slot_of(owner):
    n = owner.shape[-1]
    idx = jnp.arange(n, dtype=jnp.int32)
    earlier = idx[None, :] < idx[:, None]
    same = owner[..., :, None] == owner[..., None, :]
    return jnp.sum((same & earlier).astype(jnp.int32), axis=-1)


def local(traces, weights, pair_tile, pair_offset, tile_order):
    window_count = traces.shape[0]
    sample_count = traces.shape[2]
    blocks = sample_count // LO
    devices = lax.axis_size("tile")
    tile_count = tile_order.shape[0]
    owned_count = tile_count // devices
    positions = devices * SLOT

    hilbert = hilbert_build(sample_count)

    full_weights = lax.all_gather(weights, "tm", axis=1, tiled=True)
    pair_count, grid_count, _ = full_weights.shape
    wf = full_weights.astype(jnp.float32)
    energy = jnp.sum(wf * wf, axis=2)

    pidx = jnp.arange(pair_count, dtype=jnp.int32)
    pair_block = pair_offset // LO
    key = pair_block * pair_count + pidx
    rank = jnp.sum((key[None, :] < key[:, None]).astype(jnp.int32), axis=1)
    order = jnp.sum(jnp.where(rank[None, :] == pidx[:, None], pidx[None, :], 0), axis=1)
    bidx = jnp.arange(blocks + 1, dtype=jnp.int32)
    bstart = jnp.sum((pair_block[None, :] < bidx[:, None]).astype(jnp.int32), axis=1)
    owner, row = owner_of(pair_tile, tile_order, owned_count)
    dst = owner * SLOT + slot_of(owner)
    pos_idx = jnp.arange(positions, dtype=jnp.int32)
    unused = jnp.sum((dst[None, :] == pos_idx[:, None]).astype(jnp.int32), axis=1) == 0
    empty_rank = jnp.cumsum(unused.astype(jnp.int32)) - 1
    empty_count = positions - pair_count
    eidx = jnp.arange(empty_count, dtype=jnp.int32)
    empties = jnp.sum(
        jnp.where(unused[None, :] & (empty_rank[None, :] == eidx[:, None]), pos_idx[None, :], 0), axis=1
    )
    dst_sorted = jnp.sum(jnp.where(order[:, None] == pidx[None, :], dst[None, :], 0), axis=1)

    feature_max = jnp.maximum(jnp.max(jnp.abs(traces.astype(jnp.float32))), 1.0)
    bound = jnp.max(jnp.sum(jnp.abs(wf), axis=2), axis=1) * feature_max
    exponent = jnp.where(bound > 0, jnp.ceil(jnp.log2(jnp.maximum(bound, 1e-30))) - 14.0, 0.0)

    lanes = jnp.arange(LO, dtype=jnp.int32)[None, :]
    energy_lanes = jnp.pad(energy, ((0, 0), (0, LO - grid_count)))
    info_row = jnp.where(
        lanes < grid_count,
        energy_lanes,
        jnp.where(lanes - 32 == row[:, None], 1.0, jnp.where(lanes == 40, exponent[:, None], 0.0)),
    )
    pos_pair = jnp.sum(jnp.where(dst[None, :] == pos_idx[:, None], pidx[None, :] + 1, 0), axis=1) - 1
    info_pos = jnp.where((pos_pair >= 0)[:, None], info_row[jnp.maximum(pos_pair, 0)], 0.0)
    info_pos = jnp.concatenate(
        [info_pos[:, None, :], jnp.zeros((positions, INFO_ROWS - 1, LO), jnp.float32)], axis=1
    )
    info_recv = lax.all_to_all(info_pos.reshape(devices, SLOT, INFO_ROWS, LO), "tile", 0, 0, tiled=True)
    info_recv = info_recv.reshape(positions, INFO_ROWS, LO)
    row_of_slot = slot_rows(info_recv, owned_count, 0)
    recv_scale = jnp.exp2(info_recv[:, 0, 40])
    send_exp = jnp.where(pos_pair >= 0, exponent[jnp.maximum(pos_pair, 0)], 0.0)
    send_inv = jnp.exp2(-send_exp)

    window_feats = [analytic(traces[w], hilbert) for w in range(window_count)]
    slots = pair_stacks(
        order, bstart, dst_sorted, empties, full_weights, None, window_feats, positions, False
    )
    rows = slots.shape[1]
    wire = (slots * send_inv[:, None, None]).astype(jnp.float16)
    received = lax.all_to_all(wire.reshape(devices, SLOT, rows, LO), "tile", 0, 0, tiled=True)
    received = received.reshape(positions, rows, LO).astype(jnp.float32) * recv_scale[:, None, None]
    stacked = gather_rows(received, row_of_slot, owned_count)

    data_rows = 3 * grid_count
    tile_energy = jnp.sum(
        jnp.where((row_of_slot[None, :] == jnp.arange(owned_count)[:, None])[:, :, None],
                  info_recv[None, :, 0, :grid_count], 0.0),
        axis=1,
    )
    energy_rows = tile_energy + ENERGY_EPS
    energy_b = energy_rows[:, :, None]
    out = []
    for w in range(window_count):
        row_stacks = stacked[:, w * data_rows:(w + 1) * data_rows].reshape(owned_count, 3, grid_count, LO)
        linear = row_stacks[:, 0]
        cosine_sum = row_stacks[:, 1]
        sine_sum = row_stacks[:, 2]
        out.append(
            linear * (cosine_sum * cosine_sum + sine_sum * sine_sum) / (energy_b * jnp.sqrt(energy_b))
        )
    return jnp.stack(out, axis=0)


def solution(mesh):
    return jax.shard_map(
        local,
        mesh=mesh,
        in_specs=(P("tm", "tile", None), P("tile", "tm", None), P("tile"), P("tile"), P()),
        out_specs=P("tm", "tile", None, None),
        check_vma=False,
    )
```

```python
import jax
import jax.numpy as jnp
from jax import lax
from jax.experimental import pallas as pl
from jax.experimental.pallas import tpu as pltpu
from jax.sharding import PartitionSpec as P

LO = 128
SLOT = 2

AMP_FLOOR = 0.5
ENERGY_EPS = 1e-06


def hilbert_build(length):
    row = jnp.arange(LO, dtype=jnp.int32)[:, None]
    col = jnp.arange(length, dtype=jnp.int32)[None, :]
    lag_index = (col - row) % length
    odd_lag = lag_index % 2 == 1
    phase_angle = jnp.pi * lag_index.astype(jnp.float32) / length
    safe_sine = jnp.where(odd_lag, jnp.sin(phase_angle), 1.0)
    kernel = jnp.where(odd_lag, 2.0 / length * jnp.cos(phase_angle) / safe_sine, 0.0)
    first = kernel.astype(jnp.bfloat16)
    return jnp.concatenate(
        [jnp.roll(first, LO * i, axis=1) for i in range(length // LO)], axis=0
    )


def analytic(window_traces, hilbert):
    quadrature = jnp.dot(window_traces, hilbert, preferred_element_type=jnp.float32)
    real_part = window_traces.astype(jnp.float32)
    amplitude = jnp.maximum(jnp.sqrt(real_part * real_part + quadrature * quadrature), AMP_FLOOR)
    cosine = (real_part / amplitude).astype(jnp.bfloat16)
    sine_part = (quadrature / amplitude).astype(jnp.bfloat16)
    return cosine, sine_part


CHUNK = 8
INFO_ROWS = 8


def pair_kernel(order_ref, bstart_ref, dst_ref, empty_ref, w_ref, t_ref, *refs):
    phase_refs, o_ref, wscr = refs[:-2], refs[-2], refs[-1]
    b = pl.program_id(0)
    windows = t_ref.shape[0]
    planes = 3 * windows

    def plane(j):
        w, k = divmod(j, 3)
        return t_ref[w] if k == 0 else phase_refs[2 * w + k - 1][...]

    grid_count = w_ref.shape[1]
    pair_count = w_ref.shape[0]
    data_rows = planes * grid_count

    @pl.when(b == 0)
    def _():
        def zero_one(e, carry):
            o_ref[empty_ref[e]] = jnp.zeros(o_ref.shape[1:], o_ref.dtype)
            return carry

        lax.fori_loop(0, empty_ref.shape[0], zero_one, 0)

    lo_idx = bstart_ref[b]
    hi_idx = bstart_ref[b + 1]
    chunks = (hi_idx - lo_idx + CHUNK - 1) // CHUNK

    def one_chunk(ch, carry):
        base = lo_idx + ch * CHUNK
        for k in range(CHUNK):
            p = order_ref[jnp.minimum(base + k, pair_count - 1)]
            wscr[k * grid_count:(k + 1) * grid_count, :] = w_ref[p]
        rhs = jnp.concatenate(
            [plane(j) for j in range(planes)], axis=1
        )
        res = jnp.dot(wscr[...], rhs, preferred_element_type=jnp.float32)
        for k in range(CHUNK):
            @pl.when(base + k < hi_idx)
            def _():
                d = dst_ref[base + k]
                for j in range(planes):
                    o_ref[d, j * grid_count:(j + 1) * grid_count, :] = (
                        res[k * grid_count:(k + 1) * grid_count, j * LO:(j + 1) * LO]
                    )
        return carry

    lax.fori_loop(0, chunks, one_chunk, 0)


def pair_stacks(order, bstart, dst, empties, full_weights, info, traces, phases, positions, with_info):
    pair_count, grid_count, channel_count = full_weights.shape
    windows = traces.shape[0]
    planes = 3 * windows
    blocks = traces.shape[2] // LO
    rows = planes * grid_count + (INFO_ROWS if with_info else 0)
    grid_spec = pltpu.PrefetchScalarGridSpec(
        num_scalar_prefetch=4,
        grid=(blocks,),
        in_specs=[
            pl.BlockSpec(full_weights.shape, lambda b, *_: (0, 0, 0)),
        ] + [
            pl.BlockSpec((windows, channel_count, LO), lambda b, *_: (0, 0, b)),
        ] + [
            pl.BlockSpec((channel_count, LO), lambda b, *_: (0, b)) for _ in phases
        ],
        out_specs=pl.BlockSpec((positions, rows, LO), lambda b, *_: (0, 0, 0)),
        scratch_shapes=[pltpu.VMEM((CHUNK * grid_count, channel_count), full_weights.dtype)],
    )
    return pl.pallas_call(
        pair_kernel,
        grid_spec=grid_spec,
        out_shape=jax.ShapeDtypeStruct((positions, rows, LO), jnp.float32),
        compiler_params=pltpu.CompilerParams(vmem_limit_bytes=48 * 1024 * 1024),
    )(order, bstart, dst, empties, full_weights, traces, *phases)


def gather_kernel(row_ref, x_ref, o_ref):
    c = pl.program_id(0)
    per = x_ref.shape[0]

    @pl.when(c == 0)
    def _():
        o_ref[...] = jnp.zeros(o_ref.shape, o_ref.dtype)

    for q in range(per):
        r = row_ref[c * per + q]

        @pl.when(r >= 0)
        def _():
            o_ref[r] += x_ref[q]


def slot_rows(received, owned, data_rows):
    onehot = received[:, data_rows, 32:32 + owned]
    return jnp.where(
        jnp.sum(onehot, axis=1) > 0.5,
        jnp.sum(onehot * jnp.arange(owned, dtype=jnp.float32)[None, :], axis=1),
        -1.0,
    ).astype(jnp.int32)


def gather_rows(received, row, owned):
    positions, rows, lanes = received.shape
    per = 16
    grid_spec = pltpu.PrefetchScalarGridSpec(
        num_scalar_prefetch=1,
        grid=(positions // per,),
        in_specs=[pl.BlockSpec((per, rows, lanes), lambda c, r: (c, 0, 0))],
        out_specs=pl.BlockSpec((owned, rows, lanes), lambda c, r: (0, 0, 0)),
    )
    return pl.pallas_call(
        gather_kernel,
        grid_spec=grid_spec,
        out_shape=jax.ShapeDtypeStruct((owned, rows, lanes), jnp.float32),
    )(row, received)


def owner_of(pair_tile, tile_order, owned_count):
    tile_count = tile_order.shape[0]
    match = tile_order[None, :] == pair_tile[:, None]
    pos = jnp.sum(jnp.where(match, jnp.arange(tile_count, dtype=jnp.int32)[None, :], 0), axis=1)
    return pos // owned_count, pos % owned_count


def slot_of(owner):
    n = owner.shape[-1]
    idx = jnp.arange(n, dtype=jnp.int32)
    earlier = idx[None, :] < idx[:, None]
    same = owner[..., :, None] == owner[..., None, :]
    return jnp.sum((same & earlier).astype(jnp.int32), axis=-1)


def local(traces, weights, pair_tile, pair_offset, tile_order):
    window_count = traces.shape[0]
    sample_count = traces.shape[2]
    blocks = sample_count // LO
    devices = lax.axis_size("tile")
    tile_count = tile_order.shape[0]
    owned_count = tile_count // devices
    positions = devices * SLOT

    hilbert = hilbert_build(sample_count)

    full_weights = lax.all_gather(weights, "tm", axis=1, tiled=True)
    pair_count, grid_count, _ = full_weights.shape
    wf = full_weights.astype(jnp.float32)
    energy = jnp.sum(wf * wf, axis=2)

    pidx = jnp.arange(pair_count, dtype=jnp.int32)
    pair_block = pair_offset // LO
    key = pair_block * pair_count + pidx
    rank = jnp.sum((key[None, :] < key[:, None]).astype(jnp.int32), axis=1)
    order = jnp.sum(jnp.where(rank[None, :] == pidx[:, None], pidx[None, :], 0), axis=1)
    bidx = jnp.arange(blocks + 1, dtype=jnp.int32)
    bstart = jnp.sum((pair_block[None, :] < bidx[:, None]).astype(jnp.int32), axis=1)
    owner, row = owner_of(pair_tile, tile_order, owned_count)
    dst = owner * SLOT + slot_of(owner)
    pos_idx = jnp.arange(positions, dtype=jnp.int32)
    unused = jnp.sum((dst[None, :] == pos_idx[:, None]).astype(jnp.int32), axis=1) == 0
    empty_rank = jnp.cumsum(unused.astype(jnp.int32)) - 1
    empty_count = positions - pair_count
    eidx = jnp.arange(empty_count, dtype=jnp.int32)
    empties = jnp.sum(
        jnp.where(unused[None, :] & (empty_rank[None, :] == eidx[:, None]), pos_idx[None, :], 0), axis=1
    )
    dst_sorted = jnp.sum(jnp.where(order[:, None] == pidx[None, :], dst[None, :], 0), axis=1)

    feature_max = jnp.maximum(jnp.max(jnp.abs(traces.astype(jnp.float32))), 1.0)
    bound = jnp.max(jnp.sum(jnp.abs(wf), axis=2), axis=1) * feature_max
    exponent = jnp.where(bound > 0, jnp.ceil(jnp.log2(jnp.maximum(bound, 1e-30))) - 14.0, 0.0)

    lanes = jnp.arange(LO, dtype=jnp.int32)[None, :]
    energy_lanes = jnp.pad(energy, ((0, 0), (0, LO - grid_count)))
    info_row = jnp.where(
        lanes < grid_count,
        energy_lanes,
        jnp.where(lanes - 32 == row[:, None], 1.0, jnp.where(lanes == 40, exponent[:, None], 0.0)),
    )
    pos_pair = jnp.sum(jnp.where(dst[None, :] == pos_idx[:, None], pidx[None, :] + 1, 0), axis=1) - 1
    info_pos = jnp.where((pos_pair >= 0)[:, None], info_row[jnp.maximum(pos_pair, 0)], 0.0)
    info_pos = jnp.concatenate(
        [info_pos[:, None, :], jnp.zeros((positions, INFO_ROWS - 1, LO), jnp.float32)], axis=1
    )
    info_recv = lax.all_to_all(info_pos.reshape(devices, SLOT, INFO_ROWS, LO), "tile", 0, 0, tiled=True)
    info_recv = info_recv.reshape(positions, INFO_ROWS, LO)
    row_of_slot = slot_rows(info_recv, owned_count, 0)
    recv_scale = jnp.exp2(info_recv[:, 0, 40])
    send_exp = jnp.where(pos_pair >= 0, exponent[jnp.maximum(pos_pair, 0)], 0.0)
    send_inv = jnp.exp2(-send_exp)

    phases = []
    for w in range(window_count):
        phases += list(analytic(traces[w], hilbert))
    slots = pair_stacks(
        order, bstart, dst_sorted, empties, full_weights, None, traces, phases, positions, False
    )
    rows = slots.shape[1]
    wire = (slots * send_inv[:, None, None]).astype(jnp.float16)
    received = lax.all_to_all(wire.reshape(devices, SLOT, rows, LO), "tile", 0, 0, tiled=True)
    received = received.reshape(positions, rows, LO).astype(jnp.float32) * recv_scale[:, None, None]
    stacked = gather_rows(received, row_of_slot, owned_count)

    data_rows = 3 * grid_count
    tile_energy = jnp.sum(
        jnp.where((row_of_slot[None, :] == jnp.arange(owned_count)[:, None])[:, :, None],
                  info_recv[None, :, 0, :grid_count], 0.0),
        axis=1,
    )
    energy_rows = tile_energy + ENERGY_EPS
    energy_b = energy_rows[:, :, None]
    out = []
    for w in range(window_count):
        row_stacks = stacked[:, w * data_rows:(w + 1) * data_rows].reshape(owned_count, 3, grid_count, LO)
        linear = row_stacks[:, 0]
        cosine_sum = row_stacks[:, 1]
        sine_sum = row_stacks[:, 2]
        out.append(
            linear * (cosine_sum * cosine_sum + sine_sum * sine_sum) / (energy_b * jnp.sqrt(energy_b))
        )
    return jnp.stack(out, axis=0)


def solution(mesh):
    return jax.shard_map(
        local,
        mesh=mesh,
        in_specs=(P("tm", "tile", None), P("tile", "tm", None), P("tile"), P("tile"), P()),
        out_specs=P("tm", "tile", None, None),
        check_vma=False,
    )
```

```python
import jax
import jax.numpy as jnp
from jax import lax
from jax.experimental import pallas as pl
from jax.experimental.pallas import tpu as pltpu
from jax.sharding import PartitionSpec as P

LO = 128
SLOT = 2

AMP_FLOOR = 0.5
ENERGY_EPS = 1e-06


def hilbert_build(length):
    row = jnp.arange(LO, dtype=jnp.int32)[:, None]
    col = jnp.arange(length, dtype=jnp.int32)[None, :]
    lag_index = (col - row) % length
    odd_lag = lag_index % 2 == 1
    phase_angle = jnp.pi * lag_index.astype(jnp.float32) / length
    safe_sine = jnp.where(odd_lag, jnp.sin(phase_angle), 1.0)
    kernel = jnp.where(odd_lag, 2.0 / length * jnp.cos(phase_angle) / safe_sine, 0.0)
    first = kernel.astype(jnp.bfloat16)
    return jnp.concatenate(
        [jnp.roll(first, LO * i, axis=1) for i in range(length // LO)], axis=0
    )


def analytic(window_traces, hilbert):
    quadrature = jnp.dot(window_traces, hilbert, preferred_element_type=jnp.float32)
    real_part = window_traces.astype(jnp.float32)
    amplitude = jnp.maximum(jnp.sqrt(real_part * real_part + quadrature * quadrature), AMP_FLOOR)
    cosine = (real_part / amplitude).astype(jnp.bfloat16)
    sine_part = (quadrature / amplitude).astype(jnp.bfloat16)
    return jnp.stack([cosine, sine_part], axis=0)


CHUNK = 8
INFO_ROWS = 8


def pair_kernel(order_ref, bstart_ref, dst_ref, empty_ref, w_ref, t_ref, *refs):
    phase_refs, o_ref, wscr = refs[:-2], refs[-2], refs[-1]
    b = pl.program_id(0)
    windows = t_ref.shape[0]
    planes = 3 * windows

    def plane(j):
        w, k = divmod(j, 3)
        return t_ref[w] if k == 0 else phase_refs[w][k - 1]

    grid_count = w_ref.shape[1]
    pair_count = w_ref.shape[0]
    data_rows = planes * grid_count

    @pl.when(b == 0)
    def _():
        def zero_one(e, carry):
            o_ref[empty_ref[e]] = jnp.zeros(o_ref.shape[1:], o_ref.dtype)
            return carry

        lax.fori_loop(0, empty_ref.shape[0], zero_one, 0)

    lo_idx = bstart_ref[b]
    hi_idx = bstart_ref[b + 1]
    chunks = (hi_idx - lo_idx + CHUNK - 1) // CHUNK

    def one_chunk(ch, carry):
        base = lo_idx + ch * CHUNK
        for k in range(CHUNK):
            p = order_ref[jnp.minimum(base + k, pair_count - 1)]
            wscr[k * grid_count:(k + 1) * grid_count, :] = w_ref[p]
        rhs = jnp.concatenate(
            [plane(j) for j in range(planes)], axis=1
        )
        res = jnp.dot(wscr[...], rhs, preferred_element_type=jnp.float32)
        for k in range(CHUNK):
            @pl.when(base + k < hi_idx)
            def _():
                d = dst_ref[base + k]
                for j in range(planes):
                    o_ref[d, j * grid_count:(j + 1) * grid_count, :] = (
                        res[k * grid_count:(k + 1) * grid_count, j * LO:(j + 1) * LO]
                    )
        return carry

    lax.fori_loop(0, chunks, one_chunk, 0)


def pair_stacks(order, bstart, dst, empties, full_weights, info, traces, phases, positions, with_info):
    pair_count, grid_count, channel_count = full_weights.shape
    windows = traces.shape[0]
    planes = 3 * windows
    blocks = traces.shape[2] // LO
    rows = planes * grid_count + (INFO_ROWS if with_info else 0)
    grid_spec = pltpu.PrefetchScalarGridSpec(
        num_scalar_prefetch=4,
        grid=(blocks,),
        in_specs=[
            pl.BlockSpec(full_weights.shape, lambda b, *_: (0, 0, 0)),
        ] + [
            pl.BlockSpec((windows, channel_count, LO), lambda b, *_: (0, 0, b)),
        ] + [
            pl.BlockSpec((2, channel_count, LO), lambda b, *_: (0, 0, b)) for _ in phases
        ],
        out_specs=pl.BlockSpec((positions, rows, LO), lambda b, *_: (0, 0, 0)),
        scratch_shapes=[pltpu.VMEM((CHUNK * grid_count, channel_count), full_weights.dtype)],
    )
    return pl.pallas_call(
        pair_kernel,
        grid_spec=grid_spec,
        out_shape=jax.ShapeDtypeStruct((positions, rows, LO), jnp.float32),
        compiler_params=pltpu.CompilerParams(vmem_limit_bytes=48 * 1024 * 1024),
    )(order, bstart, dst, empties, full_weights, traces, *phases)


def gather_kernel(row_ref, x_ref, o_ref):
    c = pl.program_id(0)
    per = x_ref.shape[0]

    @pl.when(c == 0)
    def _():
        o_ref[...] = jnp.zeros(o_ref.shape, o_ref.dtype)

    for q in range(per):
        r = row_ref[c * per + q]

        @pl.when(r >= 0)
        def _():
            o_ref[r] += x_ref[q]


def slot_rows(received, owned, data_rows):
    onehot = received[:, data_rows, 32:32 + owned]
    return jnp.where(
        jnp.sum(onehot, axis=1) > 0.5,
        jnp.sum(onehot * jnp.arange(owned, dtype=jnp.float32)[None, :], axis=1),
        -1.0,
    ).astype(jnp.int32)


def gather_rows(received, row, owned):
    positions, rows, lanes = received.shape
    per = 16
    grid_spec = pltpu.PrefetchScalarGridSpec(
        num_scalar_prefetch=1,
        grid=(positions // per,),
        in_specs=[pl.BlockSpec((per, rows, lanes), lambda c, r: (c, 0, 0))],
        out_specs=pl.BlockSpec((owned, rows, lanes), lambda c, r: (0, 0, 0)),
    )
    return pl.pallas_call(
        gather_kernel,
        grid_spec=grid_spec,
        out_shape=jax.ShapeDtypeStruct((owned, rows, lanes), jnp.float32),
    )(row, received)


def owner_of(pair_tile, tile_order, owned_count):
    tile_count = tile_order.shape[0]
    match = tile_order[None, :] == pair_tile[:, None]
    pos = jnp.sum(jnp.where(match, jnp.arange(tile_count, dtype=jnp.int32)[None, :], 0), axis=1)
    return pos // owned_count, pos % owned_count


def slot_of(owner):
    n = owner.shape[-1]
    idx = jnp.arange(n, dtype=jnp.int32)
    earlier = idx[None, :] < idx[:, None]
    same = owner[..., :, None] == owner[..., None, :]
    return jnp.sum((same & earlier).astype(jnp.int32), axis=-1)


def local(traces, weights, pair_tile, pair_offset, tile_order):
    window_count = traces.shape[0]
    sample_count = traces.shape[2]
    blocks = sample_count // LO
    devices = lax.axis_size("tile")
    tile_count = tile_order.shape[0]
    owned_count = tile_count // devices
    positions = devices * SLOT

    hilbert = hilbert_build(sample_count)

    full_weights = lax.all_gather(weights, "tm", axis=1, tiled=True)
    pair_count, grid_count, _ = full_weights.shape
    wf = full_weights.astype(jnp.float32)
    energy = jnp.sum(wf * wf, axis=2)

    pidx = jnp.arange(pair_count, dtype=jnp.int32)
    pair_block = pair_offset // LO
    key = pair_block * pair_count + pidx
    rank = jnp.sum((key[None, :] < key[:, None]).astype(jnp.int32), axis=1)
    order = jnp.sum(jnp.where(rank[None, :] == pidx[:, None], pidx[None, :], 0), axis=1)
    bidx = jnp.arange(blocks + 1, dtype=jnp.int32)
    bstart = jnp.sum((pair_block[None, :] < bidx[:, None]).astype(jnp.int32), axis=1)
    owner, row = owner_of(pair_tile, tile_order, owned_count)
    dst = owner * SLOT + slot_of(owner)
    pos_idx = jnp.arange(positions, dtype=jnp.int32)
    unused = jnp.sum((dst[None, :] == pos_idx[:, None]).astype(jnp.int32), axis=1) == 0
    empty_rank = jnp.cumsum(unused.astype(jnp.int32)) - 1
    empty_count = positions - pair_count
    eidx = jnp.arange(empty_count, dtype=jnp.int32)
    empties = jnp.sum(
        jnp.where(unused[None, :] & (empty_rank[None, :] == eidx[:, None]), pos_idx[None, :], 0), axis=1
    )
    dst_sorted = jnp.sum(jnp.where(order[:, None] == pidx[None, :], dst[None, :], 0), axis=1)

    feature_max = jnp.maximum(jnp.max(jnp.abs(traces.astype(jnp.float32))), 1.0)
    bound = jnp.max(jnp.sum(jnp.abs(wf), axis=2), axis=1) * feature_max
    exponent = jnp.where(bound > 0, jnp.ceil(jnp.log2(jnp.maximum(bound, 1e-30))) - 14.0, 0.0)

    lanes = jnp.arange(LO, dtype=jnp.int32)[None, :]
    energy_lanes = jnp.pad(energy, ((0, 0), (0, LO - grid_count)))
    info_row = jnp.where(
        lanes < grid_count,
        energy_lanes,
        jnp.where(lanes - 32 == row[:, None], 1.0, jnp.where(lanes == 40, exponent[:, None], 0.0)),
    )
    pos_pair = jnp.sum(jnp.where(dst[None, :] == pos_idx[:, None], pidx[None, :] + 1, 0), axis=1) - 1
    info_pos = jnp.where((pos_pair >= 0)[:, None], info_row[jnp.maximum(pos_pair, 0)], 0.0)
    info_pos = jnp.concatenate(
        [info_pos[:, None, :], jnp.zeros((positions, INFO_ROWS - 1, LO), jnp.float32)], axis=1
    )
    info_recv = lax.all_to_all(info_pos.reshape(devices, SLOT, INFO_ROWS, LO), "tile", 0, 0, tiled=True)
    info_recv = info_recv.reshape(positions, INFO_ROWS, LO)
    row_of_slot = slot_rows(info_recv, owned_count, 0)
    recv_scale = jnp.exp2(info_recv[:, 0, 40])
    send_exp = jnp.where(pos_pair >= 0, exponent[jnp.maximum(pos_pair, 0)], 0.0)
    send_inv = jnp.exp2(-send_exp)

    phases = [analytic(traces[w], hilbert) for w in range(window_count)]
    slots = pair_stacks(
        order, bstart, dst_sorted, empties, full_weights, None, traces, phases, positions, False
    )
    rows = slots.shape[1]
    wire = (slots * send_inv[:, None, None]).astype(jnp.float16)
    received = lax.all_to_all(wire.reshape(devices, SLOT, rows, LO), "tile", 0, 0, tiled=True)
    received = received.reshape(positions, rows, LO).astype(jnp.float32) * recv_scale[:, None, None]
    stacked = gather_rows(received, row_of_slot, owned_count)

    data_rows = 3 * grid_count
    tile_energy = jnp.sum(
        jnp.where((row_of_slot[None, :] == jnp.arange(owned_count)[:, None])[:, :, None],
                  info_recv[None, :, 0, :grid_count], 0.0),
        axis=1,
    )
    energy_rows = tile_energy + ENERGY_EPS
    energy_b = energy_rows[:, :, None]
    out = []
    for w in range(window_count):
        row_stacks = stacked[:, w * data_rows:(w + 1) * data_rows].reshape(owned_count, 3, grid_count, LO)
        linear = row_stacks[:, 0]
        cosine_sum = row_stacks[:, 1]
        sine_sum = row_stacks[:, 2]
        out.append(
            linear * (cosine_sum * cosine_sum + sine_sum * sine_sum) / (energy_b * jnp.sqrt(energy_b))
        )
    return jnp.stack(out, axis=0)


def solution(mesh):
    return jax.shard_map(
        local,
        mesh=mesh,
        in_specs=(P("tm", "tile", None), P("tile", "tm", None), P("tile"), P("tile"), P()),
        out_specs=P("tm", "tile", None, None),
        check_vma=False,
    )
```

```python
import jax
import jax.numpy as jnp
from jax import lax
from jax.experimental import pallas as pl
from jax.experimental.pallas import tpu as pltpu
from jax.sharding import PartitionSpec as P

LO = 128
SLOT = 2

AMP_FLOOR = 0.5
ENERGY_EPS = 1e-06


def hilbert_build(length):
    row = jnp.arange(LO, dtype=jnp.int32)[:, None]
    col = jnp.arange(length, dtype=jnp.int32)[None, :]
    lag_index = (col - row) % length
    odd_lag = lag_index % 2 == 1
    phase_angle = jnp.pi * lag_index.astype(jnp.float32) / length
    safe_sine = jnp.where(odd_lag, jnp.sin(phase_angle), 1.0)
    kernel = jnp.where(odd_lag, 2.0 / length * jnp.cos(phase_angle) / safe_sine, 0.0)
    first = kernel.astype(jnp.bfloat16)
    return jnp.concatenate(
        [jnp.roll(first, LO * i, axis=1) for i in range(length // LO)], axis=0
    )


def analytic(window_traces, hilbert):
    quadrature = jnp.dot(window_traces, hilbert, preferred_element_type=jnp.float32)
    real_part = window_traces.astype(jnp.float32)
    amplitude = jnp.maximum(jnp.sqrt(real_part * real_part + quadrature * quadrature), AMP_FLOOR)
    cosine = (real_part / amplitude).astype(jnp.bfloat16)
    sine_part = (quadrature / amplitude).astype(jnp.bfloat16)
    return jnp.stack([window_traces, cosine, sine_part], axis=0)


CHUNK = 8
INFO_ROWS = 8


def pair_kernel(order_ref, bstart_ref, dst_ref, empty_ref, w_ref, *refs):
    f_refs, o_ref, wscr = refs[:-2], refs[-2], refs[-1]
    b = pl.program_id(0)
    per_window = f_refs[0].shape[0]
    planes = per_window * len(f_refs)
    grid_count = w_ref.shape[1]
    pair_count = w_ref.shape[0]
    data_rows = planes * grid_count

    @pl.when(b == 0)
    def _():
        def zero_one(e, carry):
            o_ref[empty_ref[e]] = jnp.zeros(o_ref.shape[1:], o_ref.dtype)
            return carry

        lax.fori_loop(0, empty_ref.shape[0], zero_one, 0)

    lo_idx = bstart_ref[b]
    hi_idx = bstart_ref[b + 1]
    chunks = (hi_idx - lo_idx + CHUNK - 1) // CHUNK

    def one_chunk(ch, carry):
        base = lo_idx + ch * CHUNK
        for k in range(CHUNK):
            p = order_ref[jnp.minimum(base + k, pair_count - 1)]
            wscr[k * grid_count:(k + 1) * grid_count, :] = w_ref[p]
        rhs = jnp.concatenate(
            [f_refs[j // per_window][j % per_window] for j in range(planes)], axis=1
        )
        res = jnp.dot(wscr[...], rhs, preferred_element_type=jnp.float32)
        for k in range(CHUNK):
            @pl.when(base + k < hi_idx)
            def _():
                d = dst_ref[base + k]
                for j in range(planes):
                    o_ref[d, j * grid_count:(j + 1) * grid_count, :] = (
                        res[k * grid_count:(k + 1) * grid_count, j * LO:(j + 1) * LO]
                    )
        return carry

    lax.fori_loop(0, chunks, one_chunk, 0)


def pair_stacks(order, bstart, dst, empties, full_weights, info, window_feats, positions, with_info):
    pair_count, grid_count, channel_count = full_weights.shape
    per_window = window_feats[0].shape[0]
    planes = per_window * len(window_feats)
    blocks = window_feats[0].shape[2] // LO
    rows = planes * grid_count + (INFO_ROWS if with_info else 0)
    grid_spec = pltpu.PrefetchScalarGridSpec(
        num_scalar_prefetch=4,
        grid=(blocks,),
        in_specs=[
            pl.BlockSpec(full_weights.shape, lambda b, *_: (0, 0, 0)),
        ] + [
            pl.BlockSpec((per_window, channel_count, LO), lambda b, *_: (0, 0, b)) for _ in window_feats
        ],
        out_specs=pl.BlockSpec((positions, rows, LO), lambda b, *_: (0, 0, 0)),
        scratch_shapes=[pltpu.VMEM((CHUNK * grid_count, channel_count), full_weights.dtype)],
    )
    return pl.pallas_call(
        pair_kernel,
        grid_spec=grid_spec,
        out_shape=jax.ShapeDtypeStruct((positions, rows, LO), jnp.float32),
        compiler_params=pltpu.CompilerParams(vmem_limit_bytes=48 * 1024 * 1024),
    )(order, bstart, dst, empties, full_weights, *window_feats)


def gather_kernel(row_ref, x_ref, o_ref):
    c = pl.program_id(0)
    per = x_ref.shape[0]

    @pl.when(c == 0)
    def _():
        o_ref[...] = jnp.zeros(o_ref.shape, o_ref.dtype)

    for q in range(per):
        r = row_ref[c * per + q]

        @pl.when(r >= 0)
        def _():
            o_ref[r] += x_ref[q]


def slot_rows(received, owned, data_rows):
    onehot = received[:, data_rows, 32:32 + owned]
    return jnp.where(
        jnp.sum(onehot, axis=1) > 0.5,
        jnp.sum(onehot * jnp.arange(owned, dtype=jnp.float32)[None, :], axis=1),
        -1.0,
    ).astype(jnp.int32)


def gather_rows(received, row, owned):
    positions, rows, lanes = received.shape
    per = 16
    grid_spec = pltpu.PrefetchScalarGridSpec(
        num_scalar_prefetch=1,
        grid=(positions // per,),
        in_specs=[pl.BlockSpec((per, rows, lanes), lambda c, r: (c, 0, 0))],
        out_specs=pl.BlockSpec((owned, rows, lanes), lambda c, r: (0, 0, 0)),
    )
    return pl.pallas_call(
        gather_kernel,
        grid_spec=grid_spec,
        out_shape=jax.ShapeDtypeStruct((owned, rows, lanes), jnp.float32),
    )(row, received)


def owner_of(pair_tile, tile_order, owned_count):
    tile_count = tile_order.shape[0]
    match = tile_order[None, :] == pair_tile[:, None]
    pos = jnp.sum(jnp.where(match, jnp.arange(tile_count, dtype=jnp.int32)[None, :], 0), axis=1)
    return pos // owned_count, pos % owned_count


def slot_of(owner):
    n = owner.shape[-1]
    idx = jnp.arange(n, dtype=jnp.int32)
    earlier = idx[None, :] < idx[:, None]
    same = owner[..., :, None] == owner[..., None, :]
    return jnp.sum((same & earlier).astype(jnp.int32), axis=-1)


def local(traces, weights, pair_tile, pair_offset, tile_order):
    window_count = traces.shape[0]
    sample_count = traces.shape[2]
    blocks = sample_count // LO
    devices = lax.axis_size("tile")
    tile_count = tile_order.shape[0]
    owned_count = tile_count // devices
    positions = devices * SLOT

    hilbert = hilbert_build(sample_count)

    full_weights = lax.all_gather(weights, "tm", axis=1, tiled=True)
    pair_count, grid_count, _ = full_weights.shape
    local_w = weights.astype(jnp.float32)
    weight_sums = jnp.stack(
        [jnp.sum(local_w * local_w, axis=2), jnp.sum(jnp.abs(local_w), axis=2)], axis=2
    )
    weight_sums = lax.all_gather(weight_sums, "tm", axis=1, tiled=True)
    energy = weight_sums[:, :, 0]

    pidx = jnp.arange(pair_count, dtype=jnp.int32)
    pair_block = pair_offset // LO
    key = pair_block * pair_count + pidx
    rank = jnp.sum((key[None, :] < key[:, None]).astype(jnp.int32), axis=1)
    order = jnp.sum(jnp.where(rank[None, :] == pidx[:, None], pidx[None, :], 0), axis=1)
    bidx = jnp.arange(blocks + 1, dtype=jnp.int32)
    bstart = jnp.sum((pair_block[None, :] < bidx[:, None]).astype(jnp.int32), axis=1)
    owner, row = owner_of(pair_tile, tile_order, owned_count)
    dst = owner * SLOT + slot_of(owner)
    pos_idx = jnp.arange(positions, dtype=jnp.int32)
    unused = jnp.sum((dst[None, :] == pos_idx[:, None]).astype(jnp.int32), axis=1) == 0
    empty_rank = jnp.cumsum(unused.astype(jnp.int32)) - 1
    empty_count = positions - pair_count
    eidx = jnp.arange(empty_count, dtype=jnp.int32)
    empties = jnp.sum(
        jnp.where(unused[None, :] & (empty_rank[None, :] == eidx[:, None]), pos_idx[None, :], 0), axis=1
    )
    dst_sorted = jnp.sum(jnp.where(order[:, None] == pidx[None, :], dst[None, :], 0), axis=1)

    feature_max = jnp.maximum(jnp.max(jnp.abs(traces.astype(jnp.float32))), 1.0)
    bound = jnp.max(weight_sums[:, :, 1], axis=1) * feature_max
    exponent = jnp.where(bound > 0, jnp.ceil(jnp.log2(jnp.maximum(bound, 1e-30))) - 14.0, 0.0)

    lanes = jnp.arange(LO, dtype=jnp.int32)[None, :]
    energy_lanes = jnp.pad(energy, ((0, 0), (0, LO - grid_count)))
    info_row = jnp.where(
        lanes < grid_count,
        energy_lanes,
        jnp.where(lanes - 32 == row[:, None], 1.0, jnp.where(lanes == 40, exponent[:, None], 0.0)),
    )
    pos_pair = jnp.sum(jnp.where(dst[None, :] == pos_idx[:, None], pidx[None, :] + 1, 0), axis=1) - 1
    info_pos = jnp.where((pos_pair >= 0)[:, None], info_row[jnp.maximum(pos_pair, 0)], 0.0)
    info_pos = jnp.concatenate(
        [info_pos[:, None, :], jnp.zeros((positions, INFO_ROWS - 1, LO), jnp.float32)], axis=1
    )
    info_recv = lax.all_to_all(info_pos.reshape(devices, SLOT, INFO_ROWS, LO), "tile", 0, 0, tiled=True)
    info_recv = info_recv.reshape(positions, INFO_ROWS, LO)
    row_of_slot = slot_rows(info_recv, owned_count, 0)
    recv_scale = jnp.exp2(info_recv[:, 0, 40])
    send_exp = jnp.where(pos_pair >= 0, exponent[jnp.maximum(pos_pair, 0)], 0.0)
    send_inv = jnp.exp2(-send_exp)

    window_feats = [analytic(traces[w], hilbert) for w in range(window_count)]
    slots = pair_stacks(
        order, bstart, dst_sorted, empties, full_weights, None, window_feats, positions, False
    )
    rows = slots.shape[1]
    wire = (slots * send_inv[:, None, None]).astype(jnp.float16)
    received = lax.all_to_all(wire.reshape(devices, SLOT, rows, LO), "tile", 0, 0, tiled=True)
    received = received.reshape(positions, rows, LO).astype(jnp.float32) * recv_scale[:, None, None]
    stacked = gather_rows(received, row_of_slot, owned_count)

    data_rows = 3 * grid_count
    tile_energy = jnp.sum(
        jnp.where((row_of_slot[None, :] == jnp.arange(owned_count)[:, None])[:, :, None],
                  info_recv[None, :, 0, :grid_count], 0.0),
        axis=1,
    )
    energy_rows = tile_energy + ENERGY_EPS
    energy_b = energy_rows[:, :, None]
    out = []
    for w in range(window_count):
        row_stacks = stacked[:, w * data_rows:(w + 1) * data_rows].reshape(owned_count, 3, grid_count, LO)
        linear = row_stacks[:, 0]
        cosine_sum = row_stacks[:, 1]
        sine_sum = row_stacks[:, 2]
        out.append(
            linear * (cosine_sum * cosine_sum + sine_sum * sine_sum) / (energy_b * jnp.sqrt(energy_b))
        )
    return jnp.stack(out, axis=0)


def solution(mesh):
    return jax.shard_map(
        local,
        mesh=mesh,
        in_specs=(P("tm", "tile", None), P("tile", "tm", None), P("tile"), P("tile"), P()),
        out_specs=P("tm", "tile", None, None),
        check_vma=False,
    )
```

```python
import jax
import jax.numpy as jnp
from jax import lax
from jax.experimental import pallas as pl
from jax.experimental.pallas import tpu as pltpu
from jax.sharding import PartitionSpec as P

LO = 128

SLOT = 2

AMP_FLOOR = 0.5
ENERGY_EPS = 1e-06


def hilbert_build(length):
    row = jnp.arange(LO, dtype=jnp.int32)[:, None]
    col = jnp.arange(length, dtype=jnp.int32)[None, :]
    lag_index = (col - row) % length
    odd_lag = lag_index % 2 == 1
    phase_angle = jnp.pi * lag_index.astype(jnp.float32) / length
    safe_sine = jnp.where(odd_lag, jnp.sin(phase_angle), 1.0)
    kernel = jnp.where(odd_lag, 2.0 / length * jnp.cos(phase_angle) / safe_sine, 0.0)
    first = kernel.astype(jnp.bfloat16)
    return jnp.concatenate(
        [jnp.roll(first, LO * i, axis=1) for i in range(length // LO)], axis=0
    )


def analytic(window_traces, hilbert):
    quadrature = jnp.dot(window_traces, hilbert, preferred_element_type=jnp.float32)
    real_part = window_traces.astype(jnp.float32)
    amplitude = jnp.maximum(jnp.sqrt(real_part * real_part + quadrature * quadrature), AMP_FLOOR)
    cosine = (real_part / amplitude).astype(jnp.bfloat16)
    sine_part = (quadrature / amplitude).astype(jnp.bfloat16)
    return jnp.stack([window_traces, cosine, sine_part], axis=0)


CHUNK = 8
INFO_ROWS = 8


def pair_kernel(order_ref, bstart_ref, dst_ref, empty_ref, w_ref, *refs):
    f_refs, o_ref, wscr = refs[:-2], refs[-2], refs[-1]
    b = pl.program_id(0)
    per_window = f_refs[0].shape[0]
    planes = per_window * len(f_refs)
    grid_count = w_ref.shape[1]
    pair_count = w_ref.shape[0]
    data_rows = planes * grid_count

    @pl.when(b == 0)
    def _():
        def zero_one(e, carry):
            o_ref[empty_ref[e]] = jnp.zeros(o_ref.shape[1:], o_ref.dtype)
            return carry

        lax.fori_loop(0, empty_ref.shape[0], zero_one, 0)

    lo_idx = bstart_ref[b]
    hi_idx = bstart_ref[b + 1]
    chunks = (hi_idx - lo_idx + CHUNK - 1) // CHUNK

    def one_chunk(ch, carry):
        base = lo_idx + ch * CHUNK
        for k in range(CHUNK):
            p = order_ref[jnp.minimum(base + k, pair_count - 1)]
            wscr[k * grid_count:(k + 1) * grid_count, :] = w_ref[p]
        rhs = jnp.concatenate(
            [f_refs[j // per_window][j % per_window] for j in range(planes)], axis=1
        )
        res = jnp.dot(wscr[...], rhs, preferred_element_type=jnp.float32)
        for k in range(CHUNK):
            @pl.when(base + k < hi_idx)
            def _():
                d = dst_ref[base + k]
                for j in range(planes):
                    o_ref[d, j * grid_count:(j + 1) * grid_count, :] = (
                        res[k * grid_count:(k + 1) * grid_count, j * LO:(j + 1) * LO]
                    )
        return carry

    lax.fori_loop(0, chunks, one_chunk, 0)


def pair_stacks(order, bstart, dst, empties, full_weights, info, window_feats, positions, with_info):
    pair_count, grid_count, channel_count = full_weights.shape
    per_window = window_feats[0].shape[0]
    planes = per_window * len(window_feats)
    blocks = window_feats[0].shape[2] // LO
    rows = planes * grid_count + (INFO_ROWS if with_info else 0)
    grid_spec = pltpu.PrefetchScalarGridSpec(
        num_scalar_prefetch=4,
        grid=(blocks,),
        in_specs=[
            pl.BlockSpec(full_weights.shape, lambda b, *_: (0, 0, 0)),
        ] + [
            pl.BlockSpec((per_window, channel_count, LO), lambda b, *_: (0, 0, b)) for _ in window_feats
        ],
        out_specs=pl.BlockSpec((positions, rows, LO), lambda b, *_: (0, 0, 0)),
        scratch_shapes=[pltpu.VMEM((CHUNK * grid_count, channel_count), full_weights.dtype)],
    )
    return pl.pallas_call(
        pair_kernel,
        grid_spec=grid_spec,
        out_shape=jax.ShapeDtypeStruct((positions, rows, LO), jnp.float32),
        compiler_params=pltpu.CompilerParams(vmem_limit_bytes=48 * 1024 * 1024),
    )(order, bstart, dst, empties, full_weights, *window_feats)


def gather_kernel(row_ref, x_ref, o_ref):
    c = pl.program_id(0)
    per = x_ref.shape[0]

    @pl.when(c == 0)
    def _():
        o_ref[...] = jnp.zeros(o_ref.shape, o_ref.dtype)

    for q in range(per):
        r = row_ref[c * per + q]

        @pl.when(r >= 0)
        def _():
            o_ref[r] += x_ref[q]


def slot_rows(received, owned, data_rows):
    onehot = received[:, data_rows, 32:32 + owned]
    return jnp.where(
        jnp.sum(onehot, axis=1) > 0.5,
        jnp.sum(onehot * jnp.arange(owned, dtype=jnp.float32)[None, :], axis=1),
        -1.0,
    ).astype(jnp.int32)


def gather_rows(received, row, owned):
    positions, rows, lanes = received.shape
    per = 16
    grid_spec = pltpu.PrefetchScalarGridSpec(
        num_scalar_prefetch=1,
        grid=(positions // per,),
        in_specs=[pl.BlockSpec((per, rows, lanes), lambda c, r: (c, 0, 0))],
        out_specs=pl.BlockSpec((owned, rows, lanes), lambda c, r: (0, 0, 0)),
    )
    return pl.pallas_call(
        gather_kernel,
        grid_spec=grid_spec,
        out_shape=jax.ShapeDtypeStruct((owned, rows, lanes), jnp.float32),
        compiler_params=pltpu.CompilerParams(allow_input_fusion=[False, True]),
    )(row, received)


def owner_of(pair_tile, tile_order, owned_count):
    tile_count = tile_order.shape[0]
    match = tile_order[None, :] == pair_tile[:, None]
    pos = jnp.sum(jnp.where(match, jnp.arange(tile_count, dtype=jnp.int32)[None, :], 0), axis=1)
    return pos // owned_count, pos % owned_count


def slot_of(owner):
    n = owner.shape[-1]
    idx = jnp.arange(n, dtype=jnp.int32)
    earlier = idx[None, :] < idx[:, None]
    same = owner[..., :, None] == owner[..., None, :]
    return jnp.sum((same & earlier).astype(jnp.int32), axis=-1)


def local(traces, weights, pair_tile, pair_offset, tile_order):
    window_count = traces.shape[0]
    sample_count = traces.shape[2]
    blocks = sample_count // LO
    devices = lax.axis_size("tile")
    tile_count = tile_order.shape[0]
    owned_count = tile_count // devices
    positions = devices * SLOT

    hilbert = hilbert_build(sample_count)

    full_weights = lax.all_gather(weights, "tm", axis=1, tiled=True)
    pair_count, grid_count, _ = full_weights.shape
    wf = full_weights.astype(jnp.float32)
    energy = jnp.sum(wf * wf, axis=2)

    pidx = jnp.arange(pair_count, dtype=jnp.int32)
    pair_block = pair_offset // LO
    key = pair_block * pair_count + pidx
    rank = jnp.sum((key[None, :] < key[:, None]).astype(jnp.int32), axis=1)
    order = jnp.sum(jnp.where(rank[None, :] == pidx[:, None], pidx[None, :], 0), axis=1)
    bidx = jnp.arange(blocks + 1, dtype=jnp.int32)
    bstart = jnp.sum((pair_block[None, :] < bidx[:, None]).astype(jnp.int32), axis=1)
    owner, row = owner_of(pair_tile, tile_order, owned_count)
    dst = owner * SLOT + slot_of(owner)
    pos_idx = jnp.arange(positions, dtype=jnp.int32)
    unused = jnp.sum((dst[None, :] == pos_idx[:, None]).astype(jnp.int32), axis=1) == 0
    empty_rank = jnp.cumsum(unused.astype(jnp.int32)) - 1
    empty_count = positions - pair_count
    eidx = jnp.arange(empty_count, dtype=jnp.int32)
    empties = jnp.sum(
        jnp.where(unused[None, :] & (empty_rank[None, :] == eidx[:, None]), pos_idx[None, :], 0), axis=1
    )
    dst_sorted = jnp.sum(jnp.where(order[:, None] == pidx[None, :], dst[None, :], 0), axis=1)

    feature_max = jnp.maximum(jnp.max(jnp.abs(traces.astype(jnp.float32))), 1.0)
    bound = jnp.max(jnp.sum(jnp.abs(wf), axis=2), axis=1) * feature_max
    exponent = jnp.where(bound > 0, jnp.ceil(jnp.log2(jnp.maximum(bound, 1e-30))) - 14.0, 0.0)

    lanes = jnp.arange(LO, dtype=jnp.int32)[None, :]
    energy_lanes = jnp.pad(energy, ((0, 0), (0, LO - grid_count)))
    info_row = jnp.where(
        lanes < grid_count,
        energy_lanes,
        jnp.where(lanes - 32 == row[:, None], 1.0, jnp.where(lanes == 40, exponent[:, None], 0.0)),
    )
    pos_pair = jnp.sum(jnp.where(dst[None, :] == pos_idx[:, None], pidx[None, :] + 1, 0), axis=1) - 1
    info_pos = jnp.where((pos_pair >= 0)[:, None], info_row[jnp.maximum(pos_pair, 0)], 0.0)
    info_pos = jnp.concatenate(
        [info_pos[:, None, :], jnp.zeros((positions, INFO_ROWS - 1, LO), jnp.float32)], axis=1
    )
    info_recv = lax.all_to_all(info_pos.reshape(devices, SLOT, INFO_ROWS, LO), "tile", 0, 0, tiled=True)
    info_recv = info_recv.reshape(positions, INFO_ROWS, LO)
    row_of_slot = slot_rows(info_recv, owned_count, 0)
    recv_scale = jnp.exp2(info_recv[:, 0, 40])
    send_exp = jnp.where(pos_pair >= 0, exponent[jnp.maximum(pos_pair, 0)], 0.0)
    send_inv = jnp.exp2(-send_exp)

    window_feats = [analytic(traces[w], hilbert) for w in range(window_count)]
    slots = pair_stacks(
        order, bstart, dst_sorted, empties, full_weights, None, window_feats, positions, False
    )
    rows = slots.shape[1]
    wire = (slots * send_inv[:, None, None]).astype(jnp.float16)
    received = lax.all_to_all(wire.reshape(devices, SLOT, rows, LO), "tile", 0, 0, tiled=True)
    received = received.reshape(positions, rows, LO).astype(jnp.float32) * recv_scale[:, None, None]
    stacked = gather_rows(received, row_of_slot, owned_count)

    data_rows = 3 * grid_count
    tile_energy = jnp.sum(
        jnp.where((row_of_slot[None, :] == jnp.arange(owned_count)[:, None])[:, :, None],
                  info_recv[None, :, 0, :grid_count], 0.0),
        axis=1,
    )
    energy_rows = tile_energy + ENERGY_EPS
    energy_b = energy_rows[:, :, None]
    out = []
    for w in range(window_count):
        row_stacks = stacked[:, w * data_rows:(w + 1) * data_rows].reshape(owned_count, 3, grid_count, LO)
        linear = row_stacks[:, 0]
        cosine_sum = row_stacks[:, 1]
        sine_sum = row_stacks[:, 2]
        out.append(
            linear * (cosine_sum * cosine_sum + sine_sum * sine_sum) / (energy_b * jnp.sqrt(energy_b))
        )
    return jnp.stack(out, axis=0)


def solution(mesh):
    return jax.shard_map(
        local,
        mesh=mesh,
        in_specs=(P("tm", "tile", None), P("tile", "tm", None), P("tile"), P("tile"), P()),
        out_specs=P("tm", "tile", None, None),
        check_vma=False,
    )
```

```python
import jax
import jax.numpy as jnp
from jax import lax
from jax.experimental import pallas as pl
from jax.experimental.pallas import tpu as pltpu
from jax.sharding import PartitionSpec as P

LO = 128

SLOT = 2

AMP_FLOOR = 0.5
ENERGY_EPS = 1e-06


def hilbert_build(length):
    row = jnp.arange(LO, dtype=jnp.int32)[:, None]
    col = jnp.arange(length, dtype=jnp.int32)[None, :]
    lag_index = (col - row) % length
    odd_lag = lag_index % 2 == 1
    phase_angle = jnp.pi * lag_index.astype(jnp.float32) / length
    safe_sine = jnp.where(odd_lag, jnp.sin(phase_angle), 1.0)
    kernel = jnp.where(odd_lag, 2.0 / length * jnp.cos(phase_angle) / safe_sine, 0.0)
    first = kernel.astype(jnp.bfloat16)
    return jnp.concatenate(
        [jnp.roll(first, LO * i, axis=1) for i in range(length // LO)], axis=0
    )


def analytic(window_traces, hilbert):
    quadrature = jnp.dot(window_traces, hilbert, preferred_element_type=jnp.float32)
    real_part = window_traces.astype(jnp.float32)
    amplitude = jnp.maximum(jnp.sqrt(real_part * real_part + quadrature * quadrature), AMP_FLOOR)
    cosine = (real_part / amplitude).astype(jnp.bfloat16)
    sine_part = (quadrature / amplitude).astype(jnp.bfloat16)
    return jnp.stack([window_traces, cosine, sine_part], axis=0)


CHUNK = 8
INFO_ROWS = 8


def pair_kernel(order_ref, bstart_ref, dst_ref, empty_ref, w_ref, *refs):
    f_refs, o_ref, wscr = refs[:-2], refs[-2], refs[-1]
    b = pl.program_id(0)
    per_window = f_refs[0].shape[0]
    planes = per_window * len(f_refs)
    grid_count = w_ref.shape[1]
    pair_count = w_ref.shape[0]
    data_rows = planes * grid_count

    @pl.when(b == 0)
    def _():
        def zero_one(e, carry):
            o_ref[empty_ref[e]] = jnp.zeros(o_ref.shape[1:], o_ref.dtype)
            return carry

        lax.fori_loop(0, empty_ref.shape[0], zero_one, 0)

    lo_idx = bstart_ref[b]
    hi_idx = bstart_ref[b + 1]
    chunks = (hi_idx - lo_idx + CHUNK - 1) // CHUNK

    def one_chunk(ch, carry):
        base = lo_idx + ch * CHUNK
        for k in range(CHUNK):
            p = order_ref[jnp.minimum(base + k, pair_count - 1)]
            wscr[k * grid_count:(k + 1) * grid_count, :] = w_ref[p]
        rhs = jnp.concatenate(
            [f_refs[j // per_window][j % per_window] for j in range(planes)], axis=1
        )
        res = jnp.dot(wscr[...], rhs, preferred_element_type=jnp.float32)
        for k in range(CHUNK):
            @pl.when(base + k < hi_idx)
            def _():
                d = dst_ref[base + k]
                for j in range(planes):
                    o_ref[d, j * grid_count:(j + 1) * grid_count, :] = (
                        res[k * grid_count:(k + 1) * grid_count, j * LO:(j + 1) * LO]
                    )
        return carry

    lax.fori_loop(0, chunks, one_chunk, 0)


def pair_stacks(order, bstart, dst, empties, full_weights, info, window_feats, positions, with_info):
    pair_count, grid_count, channel_count = full_weights.shape
    per_window = window_feats[0].shape[0]
    planes = per_window * len(window_feats)
    blocks = window_feats[0].shape[2] // LO
    rows = planes * grid_count + (INFO_ROWS if with_info else 0)
    grid_spec = pltpu.PrefetchScalarGridSpec(
        num_scalar_prefetch=4,
        grid=(blocks,),
        in_specs=[
            pl.BlockSpec(full_weights.shape, lambda b, *_: (0, 0, 0)),
        ] + [
            pl.BlockSpec((per_window, channel_count, LO), lambda b, *_: (0, 0, b)) for _ in window_feats
        ],
        out_specs=pl.BlockSpec((positions, rows, LO), lambda b, *_: (0, 0, 0)),
        scratch_shapes=[pltpu.VMEM((CHUNK * grid_count, channel_count), full_weights.dtype)],
    )
    return pl.pallas_call(
        pair_kernel,
        grid_spec=grid_spec,
        out_shape=jax.ShapeDtypeStruct((positions, rows, LO), jnp.float32),
        compiler_params=pltpu.CompilerParams(
            vmem_limit_bytes=48 * 1024 * 1024,
            allow_input_fusion=[False] * 5 + [True] * len(window_feats),
        ),
    )(order, bstart, dst, empties, full_weights, *window_feats)


def gather_kernel(row_ref, x_ref, o_ref):
    c = pl.program_id(0)
    per = x_ref.shape[0]

    @pl.when(c == 0)
    def _():
        o_ref[...] = jnp.zeros(o_ref.shape, o_ref.dtype)

    for q in range(per):
        r = row_ref[c * per + q]

        @pl.when(r >= 0)
        def _():
            o_ref[r] += x_ref[q]


def slot_rows(received, owned, data_rows):
    onehot = received[:, data_rows, 32:32 + owned]
    return jnp.where(
        jnp.sum(onehot, axis=1) > 0.5,
        jnp.sum(onehot * jnp.arange(owned, dtype=jnp.float32)[None, :], axis=1),
        -1.0,
    ).astype(jnp.int32)


def gather_rows(received, row, owned):
    positions, rows, lanes = received.shape
    per = 16
    grid_spec = pltpu.PrefetchScalarGridSpec(
        num_scalar_prefetch=1,
        grid=(positions // per,),
        in_specs=[pl.BlockSpec((per, rows, lanes), lambda c, r: (c, 0, 0))],
        out_specs=pl.BlockSpec((owned, rows, lanes), lambda c, r: (0, 0, 0)),
    )
    return pl.pallas_call(
        gather_kernel,
        grid_spec=grid_spec,
        out_shape=jax.ShapeDtypeStruct((owned, rows, lanes), jnp.float32),
        compiler_params=pltpu.CompilerParams(allow_input_fusion=[False, True]),
    )(row, received)


def owner_of(pair_tile, tile_order, owned_count):
    tile_count = tile_order.shape[0]
    match = tile_order[None, :] == pair_tile[:, None]
    pos = jnp.sum(jnp.where(match, jnp.arange(tile_count, dtype=jnp.int32)[None, :], 0), axis=1)
    return pos // owned_count, pos % owned_count


def slot_of(owner):
    n = owner.shape[-1]
    idx = jnp.arange(n, dtype=jnp.int32)
    earlier = idx[None, :] < idx[:, None]
    same = owner[..., :, None] == owner[..., None, :]
    return jnp.sum((same & earlier).astype(jnp.int32), axis=-1)


def local(traces, weights, pair_tile, pair_offset, tile_order):
    window_count = traces.shape[0]
    sample_count = traces.shape[2]
    blocks = sample_count // LO
    devices = lax.axis_size("tile")
    tile_count = tile_order.shape[0]
    owned_count = tile_count // devices
    positions = devices * SLOT

    hilbert = hilbert_build(sample_count)

    full_weights = lax.all_gather(weights, "tm", axis=1, tiled=True)
    pair_count, grid_count, _ = full_weights.shape
    wf = full_weights.astype(jnp.float32)
    energy = jnp.sum(wf * wf, axis=2)

    pidx = jnp.arange(pair_count, dtype=jnp.int32)
    pair_block = pair_offset // LO
    key = pair_block * pair_count + pidx
    rank = jnp.sum((key[None, :] < key[:, None]).astype(jnp.int32), axis=1)
    order = jnp.sum(jnp.where(rank[None, :] == pidx[:, None], pidx[None, :], 0), axis=1)
    bidx = jnp.arange(blocks + 1, dtype=jnp.int32)
    bstart = jnp.sum((pair_block[None, :] < bidx[:, None]).astype(jnp.int32), axis=1)
    owner, row = owner_of(pair_tile, tile_order, owned_count)
    dst = owner * SLOT + slot_of(owner)
    pos_idx = jnp.arange(positions, dtype=jnp.int32)
    unused = jnp.sum((dst[None, :] == pos_idx[:, None]).astype(jnp.int32), axis=1) == 0
    empty_rank = jnp.cumsum(unused.astype(jnp.int32)) - 1
    empty_count = positions - pair_count
    eidx = jnp.arange(empty_count, dtype=jnp.int32)
    empties = jnp.sum(
        jnp.where(unused[None, :] & (empty_rank[None, :] == eidx[:, None]), pos_idx[None, :], 0), axis=1
    )
    dst_sorted = jnp.sum(jnp.where(order[:, None] == pidx[None, :], dst[None, :], 0), axis=1)

    feature_max = jnp.maximum(jnp.max(jnp.abs(traces.astype(jnp.float32))), 1.0)
    bound = jnp.max(jnp.sum(jnp.abs(wf), axis=2), axis=1) * feature_max
    exponent = jnp.where(bound > 0, jnp.ceil(jnp.log2(jnp.maximum(bound, 1e-30))) - 14.0, 0.0)

    lanes = jnp.arange(LO, dtype=jnp.int32)[None, :]
    energy_lanes = jnp.pad(energy, ((0, 0), (0, LO - grid_count)))
    info_row = jnp.where(
        lanes < grid_count,
        energy_lanes,
        jnp.where(lanes - 32 == row[:, None], 1.0, jnp.where(lanes == 40, exponent[:, None], 0.0)),
    )
    pos_pair = jnp.sum(jnp.where(dst[None, :] == pos_idx[:, None], pidx[None, :] + 1, 0), axis=1) - 1
    info_pos = jnp.where((pos_pair >= 0)[:, None], info_row[jnp.maximum(pos_pair, 0)], 0.0)
    info_pos = jnp.concatenate(
        [info_pos[:, None, :], jnp.zeros((positions, INFO_ROWS - 1, LO), jnp.float32)], axis=1
    )
    info_recv = lax.all_to_all(info_pos.reshape(devices, SLOT, INFO_ROWS, LO), "tile", 0, 0, tiled=True)
    info_recv = info_recv.reshape(positions, INFO_ROWS, LO)
    row_of_slot = slot_rows(info_recv, owned_count, 0)
    recv_scale = jnp.exp2(info_recv[:, 0, 40])
    send_exp = jnp.where(pos_pair >= 0, exponent[jnp.maximum(pos_pair, 0)], 0.0)
    send_inv = jnp.exp2(-send_exp)

    window_feats = [analytic(traces[w], hilbert) for w in range(window_count)]
    slots = pair_stacks(
        order, bstart, dst_sorted, empties, full_weights, None, window_feats, positions, False
    )
    rows = slots.shape[1]
    wire = (slots * send_inv[:, None, None]).astype(jnp.float16)
    received = lax.all_to_all(wire.reshape(devices, SLOT, rows, LO), "tile", 0, 0, tiled=True)
    received = received.reshape(positions, rows, LO).astype(jnp.float32) * recv_scale[:, None, None]
    stacked = gather_rows(received, row_of_slot, owned_count)

    data_rows = 3 * grid_count
    tile_energy = jnp.sum(
        jnp.where((row_of_slot[None, :] == jnp.arange(owned_count)[:, None])[:, :, None],
                  info_recv[None, :, 0, :grid_count], 0.0),
        axis=1,
    )
    energy_rows = tile_energy + ENERGY_EPS
    energy_b = energy_rows[:, :, None]
    out = []
    for w in range(window_count):
        row_stacks = stacked[:, w * data_rows:(w + 1) * data_rows].reshape(owned_count, 3, grid_count, LO)
        linear = row_stacks[:, 0]
        cosine_sum = row_stacks[:, 1]
        sine_sum = row_stacks[:, 2]
        out.append(
            linear * (cosine_sum * cosine_sum + sine_sum * sine_sum) / (energy_b * jnp.sqrt(energy_b))
        )
    return jnp.stack(out, axis=0)


def solution(mesh):
    return jax.shard_map(
        local,
        mesh=mesh,
        in_specs=(P("tm", "tile", None), P("tile", "tm", None), P("tile"), P("tile"), P()),
        out_specs=P("tm", "tile", None, None),
        check_vma=False,
    )
```

```python
import jax
import jax.numpy as jnp
from jax import lax
from jax.experimental import pallas as pl
from jax.experimental.pallas import tpu as pltpu
from jax.sharding import PartitionSpec as P

LO = 128

SLOT = 2

AMP_FLOOR = 0.5
ENERGY_EPS = 1e-06


def hilbert_build(length):
    row = jnp.arange(LO, dtype=jnp.int32)[:, None]
    col = jnp.arange(length, dtype=jnp.int32)[None, :]
    lag_index = (col - row) % length
    odd_lag = lag_index % 2 == 1
    phase_angle = jnp.pi * lag_index.astype(jnp.float32) / length
    safe_sine = jnp.where(odd_lag, jnp.sin(phase_angle), 1.0)
    kernel = jnp.where(odd_lag, 2.0 / length * jnp.cos(phase_angle) / safe_sine, 0.0)
    first = kernel.astype(jnp.bfloat16)
    return jnp.concatenate(
        [jnp.roll(first, LO * i, axis=1) for i in range(length // LO)], axis=0
    )


def analytic(window_traces, hilbert):
    quadrature = jnp.dot(window_traces, hilbert, preferred_element_type=jnp.float32)
    real_part = window_traces.astype(jnp.float32)
    amplitude = jnp.maximum(jnp.sqrt(real_part * real_part + quadrature * quadrature), AMP_FLOOR)
    cosine = (real_part / amplitude).astype(jnp.bfloat16)
    sine_part = (quadrature / amplitude).astype(jnp.bfloat16)
    return jnp.stack([window_traces, cosine, sine_part], axis=0)


CHUNK = 8
INFO_ROWS = 8


def pair_kernel(order_ref, bstart_ref, dst_ref, empty_ref, w_ref, *refs):
    f_refs, o_ref, wscr = refs[:-2], refs[-2], refs[-1]
    b = pl.program_id(0)
    per_window = f_refs[0].shape[0]
    planes = per_window * len(f_refs)
    grid_count = w_ref.shape[1]
    pair_count = w_ref.shape[0]
    data_rows = planes * grid_count

    @pl.when(b == 0)
    def _():
        def zero_one(e, carry):
            o_ref[empty_ref[e]] = jnp.zeros(o_ref.shape[1:], o_ref.dtype)
            return carry

        lax.fori_loop(0, empty_ref.shape[0], zero_one, 0)

    lo_idx = bstart_ref[b]
    hi_idx = bstart_ref[b + 1]
    chunks = (hi_idx - lo_idx + CHUNK - 1) // CHUNK

    def one_chunk(ch, carry):
        base = lo_idx + ch * CHUNK
        for k in range(CHUNK):
            p = order_ref[jnp.minimum(base + k, pair_count - 1)]
            wscr[k * grid_count:(k + 1) * grid_count, :] = w_ref[p]
        rhs = jnp.concatenate(
            [f_refs[j // per_window][j % per_window] for j in range(planes)], axis=1
        )
        res = jnp.dot(wscr[...], rhs, preferred_element_type=jnp.float32)
        for k in range(CHUNK):
            @pl.when(base + k < hi_idx)
            def _():
                d = dst_ref[base + k]
                for j in range(planes):
                    o_ref[d, j * grid_count:(j + 1) * grid_count, :] = (
                        res[k * grid_count:(k + 1) * grid_count, j * LO:(j + 1) * LO]
                    )
        return carry

    lax.fori_loop(0, chunks, one_chunk, 0)


def pair_stacks(order, bstart, dst, empties, full_weights, info, window_feats, positions, with_info):
    pair_count, grid_count, channel_count = full_weights.shape
    per_window = window_feats[0].shape[0]
    planes = per_window * len(window_feats)
    blocks = window_feats[0].shape[2] // LO
    rows = planes * grid_count + (INFO_ROWS if with_info else 0)
    grid_spec = pltpu.PrefetchScalarGridSpec(
        num_scalar_prefetch=4,
        grid=(blocks,),
        in_specs=[
            pl.BlockSpec(full_weights.shape, lambda b, *_: (0, 0, 0)),
        ] + [
            pl.BlockSpec((per_window, channel_count, LO), lambda b, *_: (0, 0, b)) for _ in window_feats
        ],
        out_specs=pl.BlockSpec((positions, rows, LO), lambda b, *_: (0, 0, 0)),
        scratch_shapes=[pltpu.VMEM((CHUNK * grid_count, channel_count), full_weights.dtype)],
    )
    return pl.pallas_call(
        pair_kernel,
        grid_spec=grid_spec,
        out_shape=jax.ShapeDtypeStruct((positions, rows, LO), jnp.float32),
        compiler_params=pltpu.CompilerParams(
            vmem_limit_bytes=48 * 1024 * 1024,
            allow_input_fusion=[False] * 5 + [True] * len(window_feats),
        ),
    )(order, bstart, dst, empties, full_weights, *window_feats)


def gather_kernel(row_ref, x_ref, o_ref):
    c = pl.program_id(0)
    per = x_ref.shape[0]

    @pl.when(c == 0)
    def _():
        o_ref[...] = jnp.zeros(o_ref.shape, o_ref.dtype)

    for q in range(per):
        r = row_ref[c * per + q]

        @pl.when(r >= 0)
        def _():
            o_ref[r] += x_ref[q]


def slot_rows(received, owned, data_rows):
    onehot = received[:, data_rows, 32:32 + owned]
    return jnp.where(
        jnp.sum(onehot, axis=1) > 0.5,
        jnp.sum(onehot * jnp.arange(owned, dtype=jnp.float32)[None, :], axis=1),
        -1.0,
    ).astype(jnp.int32)


def gather_rows(received, row, owned):
    positions, rows, lanes = received.shape
    per = 32
    grid_spec = pltpu.PrefetchScalarGridSpec(
        num_scalar_prefetch=1,
        grid=(positions // per,),
        in_specs=[pl.BlockSpec((per, rows, lanes), lambda c, r: (c, 0, 0))],
        out_specs=pl.BlockSpec((owned, rows, lanes), lambda c, r: (0, 0, 0)),
    )
    return pl.pallas_call(
        gather_kernel,
        grid_spec=grid_spec,
        out_shape=jax.ShapeDtypeStruct((owned, rows, lanes), jnp.float32),
        compiler_params=pltpu.CompilerParams(allow_input_fusion=[False, True]),
    )(row, received)


def owner_of(pair_tile, tile_order, owned_count):
    tile_count = tile_order.shape[0]
    match = tile_order[None, :] == pair_tile[:, None]
    pos = jnp.sum(jnp.where(match, jnp.arange(tile_count, dtype=jnp.int32)[None, :], 0), axis=1)
    return pos // owned_count, pos % owned_count


def slot_of(owner):
    n = owner.shape[-1]
    idx = jnp.arange(n, dtype=jnp.int32)
    earlier = idx[None, :] < idx[:, None]
    same = owner[..., :, None] == owner[..., None, :]
    return jnp.sum((same & earlier).astype(jnp.int32), axis=-1)


def local(traces, weights, pair_tile, pair_offset, tile_order):
    window_count = traces.shape[0]
    sample_count = traces.shape[2]
    blocks = sample_count // LO
    devices = lax.axis_size("tile")
    tile_count = tile_order.shape[0]
    owned_count = tile_count // devices
    positions = devices * SLOT

    hilbert = hilbert_build(sample_count)

    full_weights = lax.all_gather(weights, "tm", axis=1, tiled=True)
    pair_count, grid_count, _ = full_weights.shape
    wf = full_weights.astype(jnp.float32)
    energy = jnp.sum(wf * wf, axis=2)

    pidx = jnp.arange(pair_count, dtype=jnp.int32)
    pair_block = pair_offset // LO
    key = pair_block * pair_count + pidx
    rank = jnp.sum((key[None, :] < key[:, None]).astype(jnp.int32), axis=1)
    order = jnp.sum(jnp.where(rank[None, :] == pidx[:, None], pidx[None, :], 0), axis=1)
    bidx = jnp.arange(blocks + 1, dtype=jnp.int32)
    bstart = jnp.sum((pair_block[None, :] < bidx[:, None]).astype(jnp.int32), axis=1)
    owner, row = owner_of(pair_tile, tile_order, owned_count)
    dst = owner * SLOT + slot_of(owner)
    pos_idx = jnp.arange(positions, dtype=jnp.int32)
    unused = jnp.sum((dst[None, :] == pos_idx[:, None]).astype(jnp.int32), axis=1) == 0
    empty_rank = jnp.cumsum(unused.astype(jnp.int32)) - 1
    empty_count = positions - pair_count
    eidx = jnp.arange(empty_count, dtype=jnp.int32)
    empties = jnp.sum(
        jnp.where(unused[None, :] & (empty_rank[None, :] == eidx[:, None]), pos_idx[None, :], 0), axis=1
    )
    dst_sorted = jnp.sum(jnp.where(order[:, None] == pidx[None, :], dst[None, :], 0), axis=1)

    feature_max = jnp.maximum(jnp.max(jnp.abs(traces.astype(jnp.float32))), 1.0)
    bound = jnp.max(jnp.sum(jnp.abs(wf), axis=2), axis=1) * feature_max
    exponent = jnp.where(bound > 0, jnp.ceil(jnp.log2(jnp.maximum(bound, 1e-30))) - 14.0, 0.0)

    lanes = jnp.arange(LO, dtype=jnp.int32)[None, :]
    energy_lanes = jnp.pad(energy, ((0, 0), (0, LO - grid_count)))
    info_row = jnp.where(
        lanes < grid_count,
        energy_lanes,
        jnp.where(lanes - 32 == row[:, None], 1.0, jnp.where(lanes == 40, exponent[:, None], 0.0)),
    )
    pos_pair = jnp.sum(jnp.where(dst[None, :] == pos_idx[:, None], pidx[None, :] + 1, 0), axis=1) - 1
    info_pos = jnp.where((pos_pair >= 0)[:, None], info_row[jnp.maximum(pos_pair, 0)], 0.0)
    info_pos = jnp.concatenate(
        [info_pos[:, None, :], jnp.zeros((positions, INFO_ROWS - 1, LO), jnp.float32)], axis=1
    )
    info_recv = lax.all_to_all(info_pos.reshape(devices, SLOT, INFO_ROWS, LO), "tile", 0, 0, tiled=True)
    info_recv = info_recv.reshape(positions, INFO_ROWS, LO)
    row_of_slot = slot_rows(info_recv, owned_count, 0)
    recv_scale = jnp.exp2(info_recv[:, 0, 40])
    send_exp = jnp.where(pos_pair >= 0, exponent[jnp.maximum(pos_pair, 0)], 0.0)
    send_inv = jnp.exp2(-send_exp)

    window_feats = [analytic(traces[w], hilbert) for w in range(window_count)]
    slots = pair_stacks(
        order, bstart, dst_sorted, empties, full_weights, None, window_feats, positions, False
    )
    rows = slots.shape[1]
    wire = (slots * send_inv[:, None, None]).astype(jnp.float16)
    received = lax.all_to_all(wire.reshape(devices, SLOT, rows, LO), "tile", 0, 0, tiled=True)
    received = received.reshape(positions, rows, LO).astype(jnp.float32) * recv_scale[:, None, None]
    stacked = gather_rows(received, row_of_slot, owned_count)

    data_rows = 3 * grid_count
    tile_energy = jnp.sum(
        jnp.where((row_of_slot[None, :] == jnp.arange(owned_count)[:, None])[:, :, None],
                  info_recv[None, :, 0, :grid_count], 0.0),
        axis=1,
    )
    energy_rows = tile_energy + ENERGY_EPS
    energy_b = energy_rows[:, :, None]
    out = []
    for w in range(window_count):
        row_stacks = stacked[:, w * data_rows:(w + 1) * data_rows].reshape(owned_count, 3, grid_count, LO)
        linear = row_stacks[:, 0]
        cosine_sum = row_stacks[:, 1]
        sine_sum = row_stacks[:, 2]
        out.append(
            linear * (cosine_sum * cosine_sum + sine_sum * sine_sum) / (energy_b * jnp.sqrt(energy_b))
        )
    return jnp.stack(out, axis=0)


def solution(mesh):
    return jax.shard_map(
        local,
        mesh=mesh,
        in_specs=(P("tm", "tile", None), P("tile", "tm", None), P("tile"), P("tile"), P()),
        out_specs=P("tm", "tile", None, None),
        check_vma=False,
    )
```

```python
import jax
import jax.numpy as jnp
from jax import lax
from jax.experimental import pallas as pl
from jax.experimental.pallas import tpu as pltpu
from jax.sharding import PartitionSpec as P

LO = 128

SLOT = 2

AMP_FLOOR = 0.5
ENERGY_EPS = 1e-06


def hilbert_build(length):
    row = jnp.arange(LO, dtype=jnp.int32)[:, None]
    col = jnp.arange(length, dtype=jnp.int32)[None, :]
    lag_index = (col - row) % length
    odd_lag = lag_index % 2 == 1
    phase_angle = jnp.pi * lag_index.astype(jnp.float32) / length
    safe_sine = jnp.where(odd_lag, jnp.sin(phase_angle), 1.0)
    kernel = jnp.where(odd_lag, 2.0 / length * jnp.cos(phase_angle) / safe_sine, 0.0)
    first = kernel.astype(jnp.bfloat16)
    return jnp.concatenate(
        [jnp.roll(first, LO * i, axis=1) for i in range(length // LO)], axis=0
    )


def analytic(window_traces, hilbert):
    quadrature = jnp.dot(window_traces, hilbert, preferred_element_type=jnp.float32)
    real_part = window_traces.astype(jnp.float32)
    amplitude = jnp.maximum(jnp.sqrt(real_part * real_part + quadrature * quadrature), AMP_FLOOR)
    cosine = (real_part / amplitude).astype(jnp.bfloat16)
    sine_part = (quadrature / amplitude).astype(jnp.bfloat16)
    return jnp.stack([window_traces, cosine, sine_part], axis=0)


CHUNK = 4
INFO_ROWS = 8


def pair_kernel(order_ref, bstart_ref, dst_ref, empty_ref, w_ref, *refs):
    f_refs, o_ref, wscr = refs[:-2], refs[-2], refs[-1]
    b = pl.program_id(0)
    per_window = f_refs[0].shape[0]
    planes = per_window * len(f_refs)
    grid_count = w_ref.shape[1]
    pair_count = w_ref.shape[0]
    data_rows = planes * grid_count

    @pl.when(b == 0)
    def _():
        def zero_one(e, carry):
            o_ref[empty_ref[e]] = jnp.zeros(o_ref.shape[1:], o_ref.dtype)
            return carry

        lax.fori_loop(0, empty_ref.shape[0], zero_one, 0)

    lo_idx = bstart_ref[b]
    hi_idx = bstart_ref[b + 1]
    chunks = (hi_idx - lo_idx + CHUNK - 1) // CHUNK

    def one_chunk(ch, carry):
        base = lo_idx + ch * CHUNK
        for k in range(CHUNK):
            p = order_ref[jnp.minimum(base + k, pair_count - 1)]
            wscr[k * grid_count:(k + 1) * grid_count, :] = w_ref[p]
        rhs = jnp.concatenate(
            [f_refs[j // per_window][j % per_window] for j in range(planes)], axis=1
        )
        res = jnp.dot(wscr[...], rhs, preferred_element_type=jnp.float32)
        for k in range(CHUNK):
            @pl.when(base + k < hi_idx)
            def _():
                d = dst_ref[base + k]
                for j in range(planes):
                    o_ref[d, j * grid_count:(j + 1) * grid_count, :] = (
                        res[k * grid_count:(k + 1) * grid_count, j * LO:(j + 1) * LO]
                    )
        return carry

    lax.fori_loop(0, chunks, one_chunk, 0)


def pair_stacks(order, bstart, dst, empties, full_weights, info, window_feats, positions, with_info):
    pair_count, grid_count, channel_count = full_weights.shape
    per_window = window_feats[0].shape[0]
    planes = per_window * len(window_feats)
    blocks = window_feats[0].shape[2] // LO
    rows = planes * grid_count + (INFO_ROWS if with_info else 0)
    grid_spec = pltpu.PrefetchScalarGridSpec(
        num_scalar_prefetch=4,
        grid=(blocks,),
        in_specs=[
            pl.BlockSpec(full_weights.shape, lambda b, *_: (0, 0, 0)),
        ] + [
            pl.BlockSpec((per_window, channel_count, LO), lambda b, *_: (0, 0, b)) for _ in window_feats
        ],
        out_specs=pl.BlockSpec((positions, rows, LO), lambda b, *_: (0, 0, 0)),
        scratch_shapes=[pltpu.VMEM((CHUNK * grid_count, channel_count), full_weights.dtype)],
    )
    return pl.pallas_call(
        pair_kernel,
        grid_spec=grid_spec,
        out_shape=jax.ShapeDtypeStruct((positions, rows, LO), jnp.float32),
        compiler_params=pltpu.CompilerParams(
            vmem_limit_bytes=48 * 1024 * 1024,
            allow_input_fusion=[False] * 5 + [True] * len(window_feats),
        ),
    )(order, bstart, dst, empties, full_weights, *window_feats)


def gather_kernel(row_ref, x_ref, o_ref):
    c = pl.program_id(0)
    per = x_ref.shape[0]

    @pl.when(c == 0)
    def _():
        o_ref[...] = jnp.zeros(o_ref.shape, o_ref.dtype)

    for q in range(per):
        r = row_ref[c * per + q]

        @pl.when(r >= 0)
        def _():
            o_ref[r] += x_ref[q]


def slot_rows(received, owned, data_rows):
    onehot = received[:, data_rows, 32:32 + owned]
    return jnp.where(
        jnp.sum(onehot, axis=1) > 0.5,
        jnp.sum(onehot * jnp.arange(owned, dtype=jnp.float32)[None, :], axis=1),
        -1.0,
    ).astype(jnp.int32)


def gather_rows(received, row, owned):
    positions, rows, lanes = received.shape
    per = 16
    grid_spec = pltpu.PrefetchScalarGridSpec(
        num_scalar_prefetch=1,
        grid=(positions // per,),
        in_specs=[pl.BlockSpec((per, rows, lanes), lambda c, r: (c, 0, 0))],
        out_specs=pl.BlockSpec((owned, rows, lanes), lambda c, r: (0, 0, 0)),
    )
    return pl.pallas_call(
        gather_kernel,
        grid_spec=grid_spec,
        out_shape=jax.ShapeDtypeStruct((owned, rows, lanes), jnp.float32),
        compiler_params=pltpu.CompilerParams(allow_input_fusion=[False, True]),
    )(row, received)


def owner_of(pair_tile, tile_order, owned_count):
    tile_count = tile_order.shape[0]
    match = tile_order[None, :] == pair_tile[:, None]
    pos = jnp.sum(jnp.where(match, jnp.arange(tile_count, dtype=jnp.int32)[None, :], 0), axis=1)
    return pos // owned_count, pos % owned_count


def slot_of(owner):
    n = owner.shape[-1]
    idx = jnp.arange(n, dtype=jnp.int32)
    earlier = idx[None, :] < idx[:, None]
    same = owner[..., :, None] == owner[..., None, :]
    return jnp.sum((same & earlier).astype(jnp.int32), axis=-1)


def local(traces, weights, pair_tile, pair_offset, tile_order):
    window_count = traces.shape[0]
    sample_count = traces.shape[2]
    blocks = sample_count // LO
    devices = lax.axis_size("tile")
    tile_count = tile_order.shape[0]
    owned_count = tile_count // devices
    positions = devices * SLOT

    hilbert = hilbert_build(sample_count)

    full_weights = lax.all_gather(weights, "tm", axis=1, tiled=True)
    pair_count, grid_count, _ = full_weights.shape
    wf = full_weights.astype(jnp.float32)
    energy = jnp.sum(wf * wf, axis=2)

    pidx = jnp.arange(pair_count, dtype=jnp.int32)
    pair_block = pair_offset // LO
    key = pair_block * pair_count + pidx
    rank = jnp.sum((key[None, :] < key[:, None]).astype(jnp.int32), axis=1)
    order = jnp.sum(jnp.where(rank[None, :] == pidx[:, None], pidx[None, :], 0), axis=1)
    bidx = jnp.arange(blocks + 1, dtype=jnp.int32)
    bstart = jnp.sum((pair_block[None, :] < bidx[:, None]).astype(jnp.int32), axis=1)
    owner, row = owner_of(pair_tile, tile_order, owned_count)
    dst = owner * SLOT + slot_of(owner)
    pos_idx = jnp.arange(positions, dtype=jnp.int32)
    unused = jnp.sum((dst[None, :] == pos_idx[:, None]).astype(jnp.int32), axis=1) == 0
    empty_rank = jnp.cumsum(unused.astype(jnp.int32)) - 1
    empty_count = positions - pair_count
    eidx = jnp.arange(empty_count, dtype=jnp.int32)
    empties = jnp.sum(
        jnp.where(unused[None, :] & (empty_rank[None, :] == eidx[:, None]), pos_idx[None, :], 0), axis=1
    )
    dst_sorted = jnp.sum(jnp.where(order[:, None] == pidx[None, :], dst[None, :], 0), axis=1)

    feature_max = jnp.maximum(jnp.max(jnp.abs(traces.astype(jnp.float32))), 1.0)
    bound = jnp.max(jnp.sum(jnp.abs(wf), axis=2), axis=1) * feature_max
    exponent = jnp.where(bound > 0, jnp.ceil(jnp.log2(jnp.maximum(bound, 1e-30))) - 14.0, 0.0)

    lanes = jnp.arange(LO, dtype=jnp.int32)[None, :]
    energy_lanes = jnp.pad(energy, ((0, 0), (0, LO - grid_count)))
    info_row = jnp.where(
        lanes < grid_count,
        energy_lanes,
        jnp.where(lanes - 32 == row[:, None], 1.0, jnp.where(lanes == 40, exponent[:, None], 0.0)),
    )
    pos_pair = jnp.sum(jnp.where(dst[None, :] == pos_idx[:, None], pidx[None, :] + 1, 0), axis=1) - 1
    info_pos = jnp.where((pos_pair >= 0)[:, None], info_row[jnp.maximum(pos_pair, 0)], 0.0)
    info_pos = jnp.concatenate(
        [info_pos[:, None, :], jnp.zeros((positions, INFO_ROWS - 1, LO), jnp.float32)], axis=1
    )
    info_recv = lax.all_to_all(info_pos.reshape(devices, SLOT, INFO_ROWS, LO), "tile", 0, 0, tiled=True)
    info_recv = info_recv.reshape(positions, INFO_ROWS, LO)
    row_of_slot = slot_rows(info_recv, owned_count, 0)
    recv_scale = jnp.exp2(info_recv[:, 0, 40])
    send_exp = jnp.where(pos_pair >= 0, exponent[jnp.maximum(pos_pair, 0)], 0.0)
    send_inv = jnp.exp2(-send_exp)

    window_feats = [analytic(traces[w], hilbert) for w in range(window_count)]
    slots = pair_stacks(
        order, bstart, dst_sorted, empties, full_weights, None, window_feats, positions, False
    )
    rows = slots.shape[1]
    wire = (slots * send_inv[:, None, None]).astype(jnp.float16)
    received = lax.all_to_all(wire.reshape(devices, SLOT, rows, LO), "tile", 0, 0, tiled=True)
    received = received.reshape(positions, rows, LO).astype(jnp.float32) * recv_scale[:, None, None]
    stacked = gather_rows(received, row_of_slot, owned_count)

    data_rows = 3 * grid_count
    tile_energy = jnp.sum(
        jnp.where((row_of_slot[None, :] == jnp.arange(owned_count)[:, None])[:, :, None],
                  info_recv[None, :, 0, :grid_count], 0.0),
        axis=1,
    )
    energy_rows = tile_energy + ENERGY_EPS
    energy_b = energy_rows[:, :, None]
    out = []
    for w in range(window_count):
        row_stacks = stacked[:, w * data_rows:(w + 1) * data_rows].reshape(owned_count, 3, grid_count, LO)
        linear = row_stacks[:, 0]
        cosine_sum = row_stacks[:, 1]
        sine_sum = row_stacks[:, 2]
        out.append(
            linear * (cosine_sum * cosine_sum + sine_sum * sine_sum) / (energy_b * jnp.sqrt(energy_b))
        )
    return jnp.stack(out, axis=0)


def solution(mesh):
    return jax.shard_map(
        local,
        mesh=mesh,
        in_specs=(P("tm", "tile", None), P("tile", "tm", None), P("tile"), P("tile"), P()),
        out_specs=P("tm", "tile", None, None),
        check_vma=False,
    )
```

```python
import jax
import jax.numpy as jnp
from jax import lax
from jax.experimental import pallas as pl
from jax.experimental.pallas import tpu as pltpu
from jax.sharding import PartitionSpec as P

LO = 128

SLOT = 2

AMP_FLOOR = 0.5
ENERGY_EPS = 1e-06


def hilbert_build(length):
    row = jnp.arange(LO, dtype=jnp.int32)[:, None]
    col = jnp.arange(length, dtype=jnp.int32)[None, :]
    lag_index = (col - row) % length
    odd_lag = lag_index % 2 == 1
    phase_angle = jnp.pi * lag_index.astype(jnp.float32) / length
    safe_sine = jnp.where(odd_lag, jnp.sin(phase_angle), 1.0)
    kernel = jnp.where(odd_lag, 2.0 / length * jnp.cos(phase_angle) / safe_sine, 0.0)
    first = kernel.astype(jnp.bfloat16)
    return jnp.concatenate(
        [jnp.roll(first, LO * i, axis=1) for i in range(length // LO)], axis=0
    )


def analytic(window_traces, hilbert):
    quadrature = jnp.dot(window_traces, hilbert, preferred_element_type=jnp.float32)
    real_part = window_traces.astype(jnp.float32)
    amplitude = jnp.maximum(jnp.sqrt(real_part * real_part + quadrature * quadrature), AMP_FLOOR)
    cosine = (real_part / amplitude).astype(jnp.bfloat16)
    sine_part = (quadrature / amplitude).astype(jnp.bfloat16)
    return jnp.stack([window_traces, cosine, sine_part], axis=0)


CHUNK = 8
INFO_ROWS = 8


def pair_kernel(order_ref, bstart_ref, dst_ref, empty_ref, w_ref, *refs):
    f_refs, o_ref, wscr = refs[:-2], refs[-2], refs[-1]
    b = pl.program_id(0)
    per_window = f_refs[0].shape[0]
    planes = per_window * len(f_refs)
    grid_count = w_ref.shape[1]
    pair_count = w_ref.shape[0]
    data_rows = planes * grid_count

    @pl.when(b == 0)
    def _():
        def zero_one(e, carry):
            o_ref[empty_ref[e]] = jnp.zeros(o_ref.shape[1:], o_ref.dtype)
            return carry

        lax.fori_loop(0, empty_ref.shape[0], zero_one, 0)

    lo_idx = bstart_ref[b]
    hi_idx = bstart_ref[b + 1]
    chunks = (hi_idx - lo_idx + CHUNK - 1) // CHUNK

    def one_chunk(ch, carry):
        base = lo_idx + ch * CHUNK
        for k in range(CHUNK):
            p = order_ref[jnp.minimum(base + k, pair_count - 1)]
            wscr[k * grid_count:(k + 1) * grid_count, :] = w_ref[p]
        rhs = jnp.concatenate(
            [f_refs[j // per_window][j % per_window] for j in range(planes)], axis=1
        )
        res = jnp.dot(wscr[...], rhs, preferred_element_type=jnp.float32)
        for k in range(CHUNK):
            @pl.when(base + k < hi_idx)
            def _():
                d = dst_ref[base + k]
                for j in range(planes):
                    o_ref[d, j * grid_count:(j + 1) * grid_count, :] = (
                        res[k * grid_count:(k + 1) * grid_count, j * LO:(j + 1) * LO]
                    )
        return carry

    lax.fori_loop(0, chunks, one_chunk, 0)


def pair_stacks(order, bstart, dst, empties, full_weights, info, window_feats, positions, with_info):
    pair_count, grid_count, channel_count = full_weights.shape
    per_window = window_feats[0].shape[0]
    planes = per_window * len(window_feats)
    blocks = window_feats[0].shape[2] // LO
    rows = planes * grid_count + (INFO_ROWS if with_info else 0)
    grid_spec = pltpu.PrefetchScalarGridSpec(
        num_scalar_prefetch=4,
        grid=(blocks,),
        in_specs=[
            pl.BlockSpec(full_weights.shape, lambda b, *_: (0, 0, 0)),
        ] + [
            pl.BlockSpec((per_window, channel_count, LO), lambda b, *_: (0, 0, b)) for _ in window_feats
        ],
        out_specs=pl.BlockSpec((positions, rows, LO), lambda b, *_: (0, 0, 0)),
        scratch_shapes=[pltpu.VMEM((CHUNK * grid_count, channel_count), full_weights.dtype)],
    )
    return pl.pallas_call(
        pair_kernel,
        grid_spec=grid_spec,
        out_shape=jax.ShapeDtypeStruct((positions, rows, LO), jnp.float32),
        compiler_params=pltpu.CompilerParams(
            vmem_limit_bytes=48 * 1024 * 1024,
            allow_input_fusion=[False] * 5 + [True] * len(window_feats),
        ),
    )(order, bstart, dst, empties, full_weights, *window_feats)


def gather_kernel(row_ref, x_ref, o_ref):
    c = pl.program_id(0)
    per = x_ref.shape[0]

    @pl.when(c == 0)
    def _():
        o_ref[...] = jnp.zeros(o_ref.shape, o_ref.dtype)

    for q in range(per):
        r = row_ref[c * per + q]

        @pl.when(r >= 0)
        def _():
            o_ref[r] += x_ref[q]


def slot_rows(received, owned, data_rows):
    onehot = received[:, data_rows, 32:32 + owned]
    return jnp.where(
        jnp.sum(onehot, axis=1) > 0.5,
        jnp.sum(onehot * jnp.arange(owned, dtype=jnp.float32)[None, :], axis=1),
        -1.0,
    ).astype(jnp.int32)


def gather_rows(received, row, owned):
    positions, rows, lanes = received.shape
    per = 64
    grid_spec = pltpu.PrefetchScalarGridSpec(
        num_scalar_prefetch=1,
        grid=(positions // per,),
        in_specs=[pl.BlockSpec((per, rows, lanes), lambda c, r: (c, 0, 0))],
        out_specs=pl.BlockSpec((owned, rows, lanes), lambda c, r: (0, 0, 0)),
    )
    return pl.pallas_call(
        gather_kernel,
        grid_spec=grid_spec,
        out_shape=jax.ShapeDtypeStruct((owned, rows, lanes), jnp.float32),
        compiler_params=pltpu.CompilerParams(allow_input_fusion=[False, True]),
    )(row, received)


def owner_of(pair_tile, tile_order, owned_count):
    tile_count = tile_order.shape[0]
    match = tile_order[None, :] == pair_tile[:, None]
    pos = jnp.sum(jnp.where(match, jnp.arange(tile_count, dtype=jnp.int32)[None, :], 0), axis=1)
    return pos // owned_count, pos % owned_count


def slot_of(owner):
    n = owner.shape[-1]
    idx = jnp.arange(n, dtype=jnp.int32)
    earlier = idx[None, :] < idx[:, None]
    same = owner[..., :, None] == owner[..., None, :]
    return jnp.sum((same & earlier).astype(jnp.int32), axis=-1)


def local(traces, weights, pair_tile, pair_offset, tile_order):
    window_count = traces.shape[0]
    sample_count = traces.shape[2]
    blocks = sample_count // LO
    devices = lax.axis_size("tile")
    tile_count = tile_order.shape[0]
    owned_count = tile_count // devices
    positions = devices * SLOT

    hilbert = hilbert_build(sample_count)

    full_weights = lax.all_gather(weights, "tm", axis=1, tiled=True)
    pair_count, grid_count, _ = full_weights.shape
    wf = full_weights.astype(jnp.float32)
    energy = jnp.sum(wf * wf, axis=2)

    pidx = jnp.arange(pair_count, dtype=jnp.int32)
    pair_block = pair_offset // LO
    key = pair_block * pair_count + pidx
    rank = jnp.sum((key[None, :] < key[:, None]).astype(jnp.int32), axis=1)
    order = jnp.sum(jnp.where(rank[None, :] == pidx[:, None], pidx[None, :], 0), axis=1)
    bidx = jnp.arange(blocks + 1, dtype=jnp.int32)
    bstart = jnp.sum((pair_block[None, :] < bidx[:, None]).astype(jnp.int32), axis=1)
    owner, row = owner_of(pair_tile, tile_order, owned_count)
    dst = owner * SLOT + slot_of(owner)
    pos_idx = jnp.arange(positions, dtype=jnp.int32)
    unused = jnp.sum((dst[None, :] == pos_idx[:, None]).astype(jnp.int32), axis=1) == 0
    empty_rank = jnp.cumsum(unused.astype(jnp.int32)) - 1
    empty_count = positions - pair_count
    eidx = jnp.arange(empty_count, dtype=jnp.int32)
    empties = jnp.sum(
        jnp.where(unused[None, :] & (empty_rank[None, :] == eidx[:, None]), pos_idx[None, :], 0), axis=1
    )
    dst_sorted = jnp.sum(jnp.where(order[:, None] == pidx[None, :], dst[None, :], 0), axis=1)

    feature_max = jnp.maximum(jnp.max(jnp.abs(traces.astype(jnp.float32))), 1.0)
    bound = jnp.max(jnp.sum(jnp.abs(wf), axis=2), axis=1) * feature_max
    exponent = jnp.where(bound > 0, jnp.ceil(jnp.log2(jnp.maximum(bound, 1e-30))) - 14.0, 0.0)

    lanes = jnp.arange(LO, dtype=jnp.int32)[None, :]
    energy_lanes = jnp.pad(energy, ((0, 0), (0, LO - grid_count)))
    info_row = jnp.where(
        lanes < grid_count,
        energy_lanes,
        jnp.where(lanes - 32 == row[:, None], 1.0, jnp.where(lanes == 40, exponent[:, None], 0.0)),
    )
    pos_pair = jnp.sum(jnp.where(dst[None, :] == pos_idx[:, None], pidx[None, :] + 1, 0), axis=1) - 1
    info_pos = jnp.where((pos_pair >= 0)[:, None], info_row[jnp.maximum(pos_pair, 0)], 0.0)
    info_pos = jnp.concatenate(
        [info_pos[:, None, :], jnp.zeros((positions, INFO_ROWS - 1, LO), jnp.float32)], axis=1
    )
    info_recv = lax.all_to_all(info_pos.reshape(devices, SLOT, INFO_ROWS, LO), "tile", 0, 0, tiled=True)
    info_recv = info_recv.reshape(positions, INFO_ROWS, LO)
    row_of_slot = slot_rows(info_recv, owned_count, 0)
    recv_scale = jnp.exp2(info_recv[:, 0, 40])
    send_exp = jnp.where(pos_pair >= 0, exponent[jnp.maximum(pos_pair, 0)], 0.0)
    send_inv = jnp.exp2(-send_exp)

    window_feats = [analytic(traces[w], hilbert) for w in range(window_count)]
    slots = pair_stacks(
        order, bstart, dst_sorted, empties, full_weights, None, window_feats, positions, False
    )
    rows = slots.shape[1]
    wire = (slots * send_inv[:, None, None]).astype(jnp.float16)
    received = lax.all_to_all(wire.reshape(devices, SLOT, rows, LO), "tile", 0, 0, tiled=True)
    received = received.reshape(positions, rows, LO).astype(jnp.float32) * recv_scale[:, None, None]
    stacked = gather_rows(received, row_of_slot, owned_count)

    data_rows = 3 * grid_count
    tile_energy = jnp.sum(
        jnp.where((row_of_slot[None, :] == jnp.arange(owned_count)[:, None])[:, :, None],
                  info_recv[None, :, 0, :grid_count], 0.0),
        axis=1,
    )
    energy_rows = tile_energy + ENERGY_EPS
    energy_b = energy_rows[:, :, None]
    out = []
    for w in range(window_count):
        row_stacks = stacked[:, w * data_rows:(w + 1) * data_rows].reshape(owned_count, 3, grid_count, LO)
        linear = row_stacks[:, 0]
        cosine_sum = row_stacks[:, 1]
        sine_sum = row_stacks[:, 2]
        out.append(
            linear * (cosine_sum * cosine_sum + sine_sum * sine_sum) / (energy_b * jnp.sqrt(energy_b))
        )
    return jnp.stack(out, axis=0)


def solution(mesh):
    return jax.shard_map(
        local,
        mesh=mesh,
        in_specs=(P("tm", "tile", None), P("tile", "tm", None), P("tile"), P("tile"), P()),
        out_specs=P("tm", "tile", None, None),
        check_vma=False,
    )
```
